32 devices in a mesh: group: 2 (over x), seq: 8 (over z, y), dp: 2 (over core).
Axes of the slice: x: 2, y: 2, z: 4, core: 2. Of those that a mesh axis runs over, the one named last changes fastest.
Arguments:
- queries: bfloat16 [4, 1024, 512], P(('group', 'dp'), 'seq'), parts along dimension 0, may hold values from -6 to 6
- key_rows: bfloat16 [4, 1024, 512], P(('group', 'dp'), 'seq'), parts along dimension 0, may hold values from -6 to 6
- value_rows: bfloat16 [4, 1024, 768], P(('group', 'dp'), 'seq'), parts along dimension 0, may hold values from -6 to 6
- trunk_state: bfloat16 [4, 1024, 768], P(('group', 'dp'), 'seq'), parts along dimension 0, may hold values from -6 to 6
- skip_input: bfloat16 [4, 2048, 768], P(('group', 'dp'), 'seq'), parts along dimension 0, may hold values from -6 to 6
- norm_gain: bfloat16 [768], replicated, may hold values from 0.099609375 to 1.8984375
- conv_weight: bfloat16 [3840, 384], replicated, may hold values from -0.09375 to 0.09375
- cotangent: bfloat16 [4, 2048, 384], P(('group', 'dp'), 'seq'), parts along dimension 0, may hold values from -6 to 6
Outputs:
- decoded: bfloat16 [4, 2048, 384], P(('group', 'dp'), 'seq'), parts along dimension 0
- grad_queries: bfloat16 [4, 1024, 512], P(('group', 'dp'), 'seq'), parts along dimension 0
- grad_keys: bfloat16 [4, 1024, 512], P(('group', 'dp'), 'seq'), parts along dimension 0
- grad_values: bfloat16 [4, 1024, 768], P(('group', 'dp'), 'seq'), parts along dimension 0
- grad_trunk: bfloat16 [4, 1024, 768], P(('group', 'dp'), 'seq'), parts along dimension 0
- grad_skip: bfloat16 [4, 2048, 768], P(('group', 'dp'), 'seq'), parts along dimension 0
- grad_weight: float32 [7680, 384], P(('group', 'seq', 'dp')), parts along dimension 0
The draws below stay inside these ranges and needn't reach their ends.
There are 2 independent parts, one for each index of `group`. The reference program is written for one: setup_inputs(seed, part) draws one part's arguments, and reference() takes and returns one part's arrays. A program takes and returns all parts, laid end to end along the dimension named above; an argument that names none is the same for every part. Nothing has to cross between parts.
All inputs are finite; a program needn't handle non-finite values.
Results may differ from the reference program's by a relative error of at most 0.029.
Values may be sent and summed in bfloat16 or wider, within the bound.
No kernel may reach another device: no remote copies, remote signals or barrier semaphores. Data moves between devices by JAX's collectives and lax.ppermute only.
A program may use at most 128 MiB of HBM per device.

```python
import math
import jax
import jax.numpy as jnp
from jax import lax

H = 4
DK = 128
DV = 192
C = 768
CO = 384
KW = 5
TOK_DEV = 128
TOKENS = 1024
POS = 2048
BATCH = 2


def paired_heads(key):
    array_shape = (BATCH, TOKENS, H * DK)
    query_base = jnp.clip(1.5 * jax.random.normal(jax.random.fold_in(key, 21), array_shape, jnp.float32), -6.0, 6.0)
    key_base = jnp.clip(1.5 * jax.random.normal(jax.random.fold_in(key, 22), array_shape, jnp.float32), -6.0, 6.0)
    return (query_base, key_base)


def draw_queries(key, part):
    return paired_heads(key)[0].astype(jnp.bfloat16)


def draw_key_rows(key, part):
    return paired_heads(key)[1].astype(jnp.bfloat16)


def block_scale(rng, extent, shards, low, high):
    level, own = 1.0, jax.random.fold_in(rng, 6)
    for position, blocks in shards:
        steps = jnp.exp(jax.random.uniform(jax.random.fold_in(own, position), (blocks,), jnp.float32, low / len(shards), high / len(shards)))
        level = level * jnp.repeat(steps, extent[position] // blocks).reshape([-1 if axis == position else 1 for axis in range(len(extent))])
    return level


def noise(own_key, shape, spread, bound, pieces=(), kind=jnp.bfloat16):
    gain = block_scale(own_key, shape, pieces, -0.22, 0.18) if pieces else 1.0
    result = jax.random.normal(own_key, shape, jnp.float32) * spread * gain
    return jnp.minimum(jnp.maximum(result, -bound), bound).astype(kind)


def setup_inputs(seed: int = 0, part: int = 0) -> dict:
    keys = jax.random.split(jax.random.key(seed), 9)
    part_splits = jax.random.split(jax.random.fold_in(keys[8], part), 9)
    queries = draw_queries(jax.random.fold_in(jax.random.fold_in(keys[8], part), 71), part)
    key_rows = draw_key_rows(jax.random.fold_in(jax.random.fold_in(keys[8], part), 71), part)
    value_rows = noise(part_splits[2], (BATCH, TOKENS, H * DV), 1.0, 6.0, ((0, 2), (1, 8)))
    trunk_state = noise(part_splits[3], (BATCH, TOKENS, C), 1.0, 6.0, ((0, 2), (1, 8)))
    skip_input = noise(part_splits[4], (BATCH, POS, C), 1.0, 6.0, ((0, 2), (1, 8)))
    norm_gain = jnp.clip(1.0 + 0.18 * jax.random.normal(keys[5], (C,), jnp.float32), 0.099609375, 1.8984375).astype(jnp.bfloat16)
    conv_weight = noise(keys[6], (KW * C, CO), (KW * C) ** -0.5, 0.09375)
    cotangent = noise(part_splits[7], (BATCH, POS, CO), 1.0, 6.0, ((0, 2), (1, 8)))
    return dict(queries=queries, key_rows=key_rows, value_rows=value_rows, trunk_state=trunk_state, skip_input=skip_input, norm_gain=norm_gain, conv_weight=conv_weight, cotangent=cotangent)


def gelu_parts(preact):
    cdf_value = 0.5 * (1.0 + jax.scipy.special.erf(preact * (1.0 / math.sqrt(2.0))))
    density = jnp.exp(-0.5 * preact * preact) * (1.0 / math.sqrt(2.0 * math.pi))
    return (preact * cdf_value, cdf_value + preact * density)

def attend_forward(query_rows, key_block, value_block):
    score_scale = DK ** (-0.5)
    all_keys = key_block.reshape(TOKENS, H, DK).astype(jnp.float32)
    all_values = value_block.reshape(TOKENS, H, DV).astype(jnp.float32)
    query_blocks = query_rows.reshape(TOKENS // TOK_DEV, TOK_DEV, H, DK)

    def forward_block(query_block):
        scores = jnp.einsum('ihd,jhd->hij', query_block.astype(jnp.float32), all_keys) * score_scale
        row_peak = lax.optimization_barrier(jnp.max(scores, axis=2, keepdims=True))
        row_total = lax.optimization_barrier(jnp.sum(jnp.exp(scores - row_peak), axis=2, keepdims=True))
        logsum = row_peak + jnp.log(row_total)
        rounded = jnp.exp(scores - logsum).astype(jnp.bfloat16)
        attended = jnp.einsum('hij,jhd->ihd', rounded.astype(jnp.float32), all_values).astype(jnp.bfloat16)
        return (attended, logsum[:, :, 0])
    attended, logsums = lax.map(forward_block, query_blocks)
    return (attended.reshape(TOKENS, H * DV), logsums)

def attend_backward(query_rows, key_block, value_block, attended, logsums, grad_trunk):
    score_scale = DK ** (-0.5)
    all_keys = key_block.reshape(TOKENS, H, DK).astype(jnp.float32)
    all_values = value_block.reshape(TOKENS, H, DV).astype(jnp.float32)
    block_count = TOKENS // TOK_DEV
    inputs = (query_rows.reshape(block_count, TOK_DEV, H, DK), attended.reshape(block_count, TOK_DEV, H, DV), grad_trunk.reshape(block_count, TOK_DEV, H, DV), logsums)

    def backward_block(running, inputs_block):
        query_block, output_block, grad_block, logsum = inputs_block
        query_float = query_block.astype(jnp.float32)
        grad_float = grad_block.astype(jnp.float32)
        scores = jnp.einsum('ihd,jhd->hij', query_float, all_keys) * score_scale
        softmax = jnp.exp(scores - logsum[:, :, None])
        rounded = softmax.astype(jnp.bfloat16)
        row_delta = lax.optimization_barrier(jnp.sum(grad_float * output_block.astype(jnp.float32), axis=2))
        value_grad = jnp.einsum('ihd,jhd->hij', grad_float, all_values)
        slopes = (softmax * (value_grad - row_delta.T[:, :, None])).astype(jnp.bfloat16)
        slopes_float = slopes.astype(jnp.float32)
        grad_query = (jnp.einsum('hij,jhd->ihd', slopes_float, all_keys) * score_scale).astype(jnp.bfloat16)
        key_terms = (jnp.einsum('hij,ihd->jhd', slopes_float, query_float) * score_scale).astype(jnp.bfloat16)
        value_terms = jnp.einsum('hij,ihd->jhd', rounded.astype(jnp.float32), grad_float).astype(jnp.bfloat16)
        key_terms, value_terms = lax.optimization_barrier((key_terms, value_terms))
        return ((running[0] + key_terms.astype(jnp.float32), running[1] + value_terms.astype(jnp.float32)), grad_query)
    zeros_pair = (jnp.zeros((TOKENS, H, DK), jnp.float32), jnp.zeros((TOKENS, H, DV), jnp.float32))
    sums_pair, grad_query = lax.scan(backward_block, zeros_pair, inputs)
    grad_queries = grad_query.reshape(TOKENS, H * DK)
    grad_keys = sums_pair[0].reshape(TOKENS, H * DK).astype(jnp.bfloat16)
    grad_values = sums_pair[1].reshape(TOKENS, H * DV).astype(jnp.bfloat16)
    return (grad_queries, grad_keys, grad_values)

def decode_one(hidden, skip_rows, channel_gain, conv_weight, cotangent_rows):
    half_kernel = KW // 2
    merged = jnp.repeat(hidden, 2, axis=0) + skip_rows.astype(jnp.float32)
    inverse = lax.rsqrt(lax.optimization_barrier(jnp.mean(merged * merged, axis=1, keepdims=True)) + 1e-06)
    normed = (merged * inverse * channel_gain).astype(jnp.bfloat16)
    padded = jnp.pad(normed, ((half_kernel, half_kernel), (0, 0)))
    columns = jnp.concatenate([padded[offset:offset + POS] for offset in range(KW)], axis=1)
    preact = jnp.dot(columns, conv_weight, preferred_element_type=jnp.float32)
    activated, derivative = gelu_parts(preact)
    grad_pre = (cotangent_rows.astype(jnp.float32) * derivative).astype(jnp.bfloat16)
    weight_part = jnp.dot(columns.T, grad_pre, preferred_element_type=jnp.float32)
    grad_padded = jnp.pad(grad_pre, ((half_kernel, half_kernel), (0, 0)))
    stacked = jnp.stack([grad_padded[2 * half_kernel - offset:2 * half_kernel - offset + POS] for offset in range(KW)], axis=1)
    grad_normed = jnp.einsum('pko,kco->pc', stacked.astype(jnp.float32), conv_weight.reshape(KW, C, CO).astype(jnp.float32))
    scaled_grad = grad_normed * channel_gain
    grad_merged = inverse * scaled_grad - merged * inverse ** 3 * lax.optimization_barrier(jnp.mean(scaled_grad * merged, axis=1, keepdims=True))
    grad_skip = grad_merged.astype(jnp.bfloat16)
    grad_trunk = grad_merged.reshape(TOKENS, 2, C).sum(axis=1).astype(jnp.bfloat16)
    return (activated.astype(jnp.bfloat16), grad_skip, grad_trunk, weight_part)

def reference(queries, key_rows, value_rows, trunk_state, skip_input, norm_gain, conv_weight, cotangent):
    channel_gain = norm_gain.astype(jnp.float32)
    results = []
    weight_total = jnp.zeros((KW * C, CO), jnp.float32)
    for member in range(BATCH):
        attended, logsums = attend_forward(queries[member], key_rows[member], value_rows[member])
        hidden = trunk_state[member].astype(jnp.float32) + attended.astype(jnp.float32)
        decoded, grad_skip, grad_trunk, weight_part = decode_one(hidden, skip_input[member], channel_gain, conv_weight, cotangent[member])
        weight_total = weight_total + weight_part
        grad_queries, grad_keys, grad_values = attend_backward(queries[member], key_rows[member], value_rows[member], attended, logsums, grad_trunk)
        results.append((decoded, grad_queries, grad_keys, grad_values, grad_trunk, grad_skip))
    stacked = [jnp.stack([result_set[number] for result_set in results]) for number in range(6)]
    grad_weight = weight_total * (BATCH * POS) ** (-0.5)
    return (stacked[0], stacked[1], stacked[2], stacked[3], stacked[4], stacked[5], grad_weight)
```

```python
import functools
import math

import jax
import jax.numpy as jnp
from jax import lax
from jax.sharding import PartitionSpec as P

H = 4
DK = 128
DV = 192
C = 768
CO = 384
KW = 5


def extended(array, sides, width):
    for axis, dim in sides:
        count, length = (lax.axis_size(axis), array.shape[dim])
        up = [(i, (i + 1) % count) for i in range(count - 1)]
        down = [(j, i) for i, j in up]
        last = lax.slice_in_dim(array, length - width, length, axis=dim)
        initial = lax.slice_in_dim(array, 0, width, axis=dim)
        before = lax.ppermute(last, axis, up)
        after = lax.ppermute(initial, axis, down)
        array = jnp.concatenate([before, array, after], axis=dim)
    return array


def gelu_parts(preact):
    cdf_value = 0.5 * (1.0 + jax.scipy.special.erf(preact * (1.0 / math.sqrt(2.0))))
    density = jnp.exp(-0.5 * preact * preact) * (1.0 / math.sqrt(2.0 * math.pi))
    return (preact * cdf_value, cdf_value + preact * density)


def window_rows(padded, kernel, row_count):
    return jnp.concatenate(
        [padded[offset : offset + row_count] for offset in range(kernel)], axis=1
    )


def ring_order(mesh):
    count = mesh.shape["seq"]
    try:
        row = mesh.devices.reshape(mesh.shape["group"], count, -1)[0, :, 0]
        coords = [tuple(device.coords) for device in row]
    except (AttributeError, TypeError):
        return list(range(count))
    varying = [d for d in range(3) if len({c[d] for c in coords}) > 1]
    if len(varying) == 2:
        for minor, major in (varying, varying[::-1]):
            if len({c[minor] for c in coords}) == 2:
                low = min(c[minor] for c in coords)
                first = sorted((c[major], s) for s, c in enumerate(coords) if c[minor] == low)
                second = sorted((c[major], s) for s, c in enumerate(coords) if c[minor] != low)
                return [s for _, s in first] + [s for _, s in second[::-1]]
    return list(range(count))


def ring_perms(ring):
    count = len(ring)
    forward = [(ring[q], ring[(q + 1) % count]) for q in range(count)]
    backward = [(ring[q], ring[(q - 1) % count]) for q in range(count)]
    return forward, backward


def ring_gather(block, ring):
    count = len(ring)
    forward, backward = ring_perms(ring)
    left_steps = count // 2
    right_steps = count - 1 - left_steps
    lefts, rights = [], []
    current = block
    for _ in range(left_steps):
        current = lax.ppermute(current, "seq", forward)
        lefts.append(current)
    current = block
    for _ in range(right_steps):
        current = lax.ppermute(current, "seq", backward)
        rights.append(current)
    return [block] + lefts + rights


def ring_scatter_back(blocks, ring):
    count = len(ring)
    forward, backward = ring_perms(ring)
    left_steps = count // 2
    right_steps = count - 1 - left_steps
    own = blocks[0].astype(jnp.float32)
    lefts = blocks[1 : 1 + left_steps]
    rights = blocks[1 + left_steps :]
    total = own
    if left_steps:
        acc = lefts[-1]
        for t in range(left_steps, 0, -1):
            received = lax.ppermute(acc, "seq", backward).astype(jnp.float32)
            if t == 1:
                total = total + received
            else:
                acc = (received + lefts[t - 2].astype(jnp.float32)).astype(jnp.bfloat16)
    if right_steps:
        acc = rights[-1]
        for t in range(right_steps, 0, -1):
            received = lax.ppermute(acc, "seq", forward).astype(jnp.float32)
            if t == 1:
                total = total + received
            else:
                acc = (received + rights[t - 2].astype(jnp.float32)).astype(jnp.bfloat16)
    return total


def ring_reduce_scatter(blocks, axis, ring, forward_dir=True):
    count = len(ring)
    if count == 1:
        return blocks[0]
    forward, backward = ring_perms(ring)
    perm = forward if forward_dir else backward
    sign = 1 if forward_dir else -1
    ring_table = jnp.array(ring, jnp.int32)
    position_table = jnp.array([ring.index(s) for s in range(count)], jnp.int32)
    position = position_table[lax.axis_index(axis)]

    def block_at(offset):
        index = ring_table[(position + count - sign * offset) % count]
        return lax.dynamic_index_in_dim(blocks, index, axis=0, keepdims=False)

    acc = block_at(1)
    for t in range(count - 1):
        received = lax.ppermute(acc, axis, perm)
        acc = received + block_at(t + 2)
    return acc


def body(ring, queries, key_rows, value_rows, trunk_state, skip_input, norm_gain, conv_weight, cotangent):
    score_scale = DK ** (-0.5)
    local_tokens = queries.shape[1]
    positions = 2 * local_tokens
    half_kernel = KW // 2
    query_heads = queries[0].reshape(local_tokens, H, DK)
    key_value_blocks = ring_gather(jnp.concatenate([key_rows[0], value_rows[0]], axis=1), ring)
    gathered = jnp.concatenate(key_value_blocks, axis=0)
    all_keys = gathered[:, : H * DK].reshape(-1, H, DK)
    all_values = gathered[:, H * DK :].reshape(-1, H, DV)
    scores = (
        jnp.einsum("ihd,jhd->hij", query_heads, all_keys, preferred_element_type=jnp.float32)
        * score_scale
    )
    row_peak = jnp.max(scores, axis=2, keepdims=True)
    row_total = jnp.sum(jnp.exp(scores - row_peak), axis=2, keepdims=True)
    logsum = row_peak + jnp.log(row_total)
    softmax = jnp.exp(scores - logsum)
    rounded = softmax.astype(jnp.bfloat16)
    attended = jnp.einsum(
        "hij,jhd->ihd", rounded, all_values, preferred_element_type=jnp.float32
    ).astype(jnp.bfloat16)
    hidden = trunk_state[0].astype(jnp.float32) + attended.reshape(local_tokens, H * DV).astype(
        jnp.float32
    )
    merged = jnp.repeat(hidden, 2, axis=0) + skip_input[0].astype(jnp.float32)
    inverse = lax.rsqrt(jnp.mean(merged * merged, axis=1, keepdims=True) + 1e-06)
    channel_gain = norm_gain.astype(jnp.float32)
    normed = (merged * inverse * channel_gain).astype(jnp.bfloat16)
    padded = extended(normed, (("seq", 0),), half_kernel)
    columns = window_rows(padded, KW, positions)
    preact = jnp.dot(columns, conv_weight, preferred_element_type=jnp.float32)
    activated, derivative = gelu_parts(preact)
    decoded = activated.astype(jnp.bfloat16)
    grad_pre = (cotangent[0].astype(jnp.float32) * derivative).astype(jnp.bfloat16)
    grad_padded = extended(grad_pre, (("seq", 0),), half_kernel)
    norm_scale = (lax.axis_size("dp") * positions * lax.axis_size("seq")) ** (-0.5)
    weight_part = (
        lax.dot_general(
            columns, grad_pre, (((0,), (0,)), ((), ())), preferred_element_type=jnp.float32
        )
        * norm_scale
    )
    seq_count, dp_count = lax.axis_size("seq"), lax.axis_size("dp")
    weight_blocks_all = weight_part.reshape(seq_count, dp_count, -1, CO)
    dp_summed = ring_reduce_scatter(
        jnp.swapaxes(weight_blocks_all, 0, 1), "dp", list(range(dp_count))
    )
    half_co = CO // 2
    grad_weight = jnp.concatenate(
        [
            ring_reduce_scatter(dp_summed[:, :, :half_co], "seq", ring, True),
            ring_reduce_scatter(dp_summed[:, :, half_co:], "seq", ring, False),
        ],
        axis=1,
    )
    stacked = jnp.stack(
        [
            grad_padded[2 * half_kernel - offset : 2 * half_kernel - offset + positions]
            for offset in range(KW)
        ],
        axis=1,
    )
    weight_blocks = conv_weight.reshape(KW, C, CO)
    grad_normed = jnp.einsum(
        "pko,kco->pc", stacked, weight_blocks, preferred_element_type=jnp.float32
    )
    scaled_grad = grad_normed * channel_gain
    grad_merged = inverse * scaled_grad - merged * inverse**3 * jnp.mean(
        scaled_grad * merged, axis=1, keepdims=True
    )
    grad_skip = grad_merged.astype(jnp.bfloat16)
    grad_trunk = grad_merged.reshape(local_tokens, 2, C).sum(axis=1).astype(jnp.bfloat16)
    grad_heads = grad_trunk.reshape(local_tokens, H, DV)
    row_delta = jnp.sum(grad_heads.astype(jnp.float32) * attended.astype(jnp.float32), axis=2)
    value_grad = jnp.einsum(
        "ihd,jhd->hij", grad_heads, all_values, preferred_element_type=jnp.float32
    )
    slopes = (softmax * (value_grad - row_delta.T[:, :, None])).astype(jnp.bfloat16)
    grad_queries = (
        jnp.einsum("hij,jhd->ihd", slopes, all_keys, preferred_element_type=jnp.float32)
        * score_scale
    ).astype(jnp.bfloat16)
    key_part = (
        jnp.einsum("hij,ihd->jhd", slopes, query_heads, preferred_element_type=jnp.float32)
        * score_scale
    )
    value_part = jnp.einsum("hij,ihd->jhd", rounded, grad_heads, preferred_element_type=jnp.float32)
    terms = jnp.concatenate(
        [
            key_part.reshape(-1, H * DK),
            value_part.reshape(-1, H * DV),
        ],
        axis=1,
    ).astype(jnp.bfloat16)
    term_blocks = [
        terms[m * local_tokens : (m + 1) * local_tokens] for m in range(lax.axis_size("seq"))
    ]
    summed = ring_scatter_back(term_blocks, ring)
    grad_keys = summed[:, : H * DK].astype(jnp.bfloat16)
    grad_values = summed[:, H * DK :].astype(jnp.bfloat16)
    return (
        decoded[None],
        grad_queries.reshape(local_tokens, H * DK)[None],
        grad_keys[None],
        grad_values[None],
        grad_trunk[None],
        grad_skip[None],
        grad_weight,
    )


def solution(mesh):
    return jax.shard_map(
        functools.partial(body, ring_order(mesh)),
        mesh=mesh,
        in_specs=(
            P(("group", "dp"), "seq", None),
            P(("group", "dp"), "seq", None),
            P(("group", "dp"), "seq", None),
            P(("group", "dp"), "seq", None),
            P(("group", "dp"), "seq", None),
            P(),
            P(),
            P(("group", "dp"), "seq", None),
        ),
        out_specs=(
            P(("group", "dp"), "seq", None),
            P(("group", "dp"), "seq", None),
            P(("group", "dp"), "seq", None),
            P(("group", "dp"), "seq", None),
            P(("group", "dp"), "seq", None),
            P(("group", "dp"), "seq", None),
            P(("group", "seq", "dp"), None),
        ),
        check_vma=False,
    )
```

```python
import functools
import math

import jax
import jax.numpy as jnp
from jax import lax
from jax.sharding import PartitionSpec as P

H = 4
DK = 128
DV = 192
C = 768
CO = 384
KW = 5


def extended(array, sides, width):
    for axis, dim in sides:
        count, length = (lax.axis_size(axis), array.shape[dim])
        up = [(i, (i + 1) % count) for i in range(count - 1)]
        down = [(j, i) for i, j in up]
        last = lax.slice_in_dim(array, length - width, length, axis=dim)
        initial = lax.slice_in_dim(array, 0, width, axis=dim)
        before = lax.ppermute(last, axis, up)
        after = lax.ppermute(initial, axis, down)
        array = jnp.concatenate([before, array, after], axis=dim)
    return array


def gelu_parts(preact):
    cdf_value = 0.5 * (1.0 + jax.scipy.special.erf(preact * (1.0 / math.sqrt(2.0))))
    density = jnp.exp(-0.5 * preact * preact) * (1.0 / math.sqrt(2.0 * math.pi))
    return (preact * cdf_value, cdf_value + preact * density)


def window_rows(padded, kernel, row_count):
    return jnp.concatenate(
        [padded[offset : offset + row_count] for offset in range(kernel)], axis=1
    )


def ring_order(mesh):
    count = mesh.shape["seq"]
    try:
        row = mesh.devices.reshape(mesh.shape["group"], count, -1)[0, :, 0]
        coords = [tuple(device.coords) for device in row]
    except (AttributeError, TypeError):
        return list(range(count))
    varying = [d for d in range(3) if len({c[d] for c in coords}) > 1]
    if len(varying) == 2:
        for minor, major in (varying, varying[::-1]):
            if len({c[minor] for c in coords}) == 2:
                low = min(c[minor] for c in coords)
                first = sorted((c[major], s) for s, c in enumerate(coords) if c[minor] == low)
                second = sorted((c[major], s) for s, c in enumerate(coords) if c[minor] != low)
                return [s for _, s in first] + [s for _, s in second[::-1]]
    return list(range(count))


def ring_perms(ring):
    count = len(ring)
    forward = [(ring[q], ring[(q + 1) % count]) for q in range(count)]
    backward = [(ring[q], ring[(q - 1) % count]) for q in range(count)]
    return forward, backward


def ring_gather(block, ring):
    count = len(ring)
    forward, backward = ring_perms(ring)
    left_steps = count // 2
    right_steps = count - 1 - left_steps
    lefts, rights = [], []
    current = block
    for _ in range(left_steps):
        current = lax.ppermute(current, "seq", forward)
        lefts.append(current)
    current = block
    for _ in range(right_steps):
        current = lax.ppermute(current, "seq", backward)
        rights.append(current)
    return [block] + lefts + rights


def ring_scatter_back(blocks, ring):
    count = len(ring)
    forward, backward = ring_perms(ring)
    left_steps = count // 2
    right_steps = count - 1 - left_steps
    own = blocks[0].astype(jnp.float32)
    lefts = blocks[1 : 1 + left_steps]
    rights = blocks[1 + left_steps :]
    total = own
    if left_steps:
        acc = lefts[-1]
        for t in range(left_steps, 0, -1):
            received = lax.ppermute(acc, "seq", backward).astype(jnp.float32)
            if t == 1:
                total = total + received
            else:
                acc = (received + lefts[t - 2].astype(jnp.float32)).astype(jnp.bfloat16)
    if right_steps:
        acc = rights[-1]
        for t in range(right_steps, 0, -1):
            received = lax.ppermute(acc, "seq", forward).astype(jnp.float32)
            if t == 1:
                total = total + received
            else:
                acc = (received + rights[t - 2].astype(jnp.float32)).astype(jnp.bfloat16)
    return total


def ring_reduce_scatter(blocks, axis, ring, forward_dir=True):
    count = len(ring)
    if count == 1:
        return blocks[0]
    forward, backward = ring_perms(ring)
    perm = forward if forward_dir else backward
    sign = 1 if forward_dir else -1
    ring_table = jnp.array(ring, jnp.int32)
    position_table = jnp.array([ring.index(s) for s in range(count)], jnp.int32)
    position = position_table[lax.axis_index(axis)]

    def block_at(offset):
        index = ring_table[(position + count - sign * offset) % count]
        return lax.dynamic_index_in_dim(blocks, index, axis=0, keepdims=False)

    acc = block_at(1)
    for t in range(count - 1):
        received = lax.ppermute(acc, axis, perm)
        acc = received + block_at(t + 2)
    return acc


def body(ring, queries, key_rows, value_rows, trunk_state, skip_input, norm_gain, conv_weight, cotangent):
    score_scale = DK ** (-0.5)
    local_tokens = queries.shape[1]
    positions = 2 * local_tokens
    half_kernel = KW // 2
    query_heads = queries[0].reshape(local_tokens, H, DK)
    key_value_blocks = ring_gather(jnp.concatenate([key_rows[0], value_rows[0]], axis=1), ring)
    gathered = jnp.concatenate(key_value_blocks, axis=0)
    all_keys = gathered[:, : H * DK].reshape(-1, H, DK)
    all_values = gathered[:, H * DK :].reshape(-1, H, DV)
    scores = (
        jnp.einsum("ihd,jhd->hij", query_heads, all_keys, preferred_element_type=jnp.float32)
        * score_scale
    )
    row_peak = jnp.max(scores, axis=2, keepdims=True)
    row_total = jnp.sum(jnp.exp(scores - row_peak), axis=2, keepdims=True)
    logsum = row_peak + jnp.log(row_total)
    softmax = jnp.exp(scores - logsum)
    rounded = softmax.astype(jnp.bfloat16)
    attended = jnp.einsum(
        "hij,jhd->ihd", rounded, all_values, preferred_element_type=jnp.float32
    ).astype(jnp.bfloat16)
    hidden = trunk_state[0].astype(jnp.float32) + attended.reshape(local_tokens, H * DV).astype(
        jnp.float32
    )
    merged = jnp.repeat(hidden, 2, axis=0) + skip_input[0].astype(jnp.float32)
    inverse = lax.rsqrt(jnp.mean(merged * merged, axis=1, keepdims=True) + 1e-06)
    channel_gain = norm_gain.astype(jnp.float32)
    normed = (merged * inverse * channel_gain).astype(jnp.bfloat16)
    padded = extended(normed, (("seq", 0),), half_kernel)
    columns = window_rows(padded, KW, positions)
    preact = jnp.dot(columns, conv_weight, preferred_element_type=jnp.float32)
    activated, derivative = gelu_parts(preact)
    decoded = activated.astype(jnp.bfloat16)
    grad_pre = (cotangent[0].astype(jnp.float32) * derivative).astype(jnp.bfloat16)
    grad_padded = extended(grad_pre, (("seq", 0),), half_kernel)
    norm_scale = (lax.axis_size("dp") * positions * lax.axis_size("seq")) ** (-0.5)
    seq_count, dp_count = lax.axis_size("seq"), lax.axis_size("dp")
    rows_per = KW * C // (seq_count * dp_count)
    if dp_count == 2:
        partner = [(0, 1), (1, 0)]
        partner_padded = lax.ppermute(padded, "dp", partner)
        partner_grad = lax.ppermute(grad_pre, "dp", partner)
        both_columns = jnp.concatenate(
            [columns, window_rows(partner_padded, KW, positions)], axis=0
        ).reshape(2 * positions, seq_count, dp_count, rows_per)
        mine = lax.dynamic_index_in_dim(both_columns, lax.axis_index("dp"), axis=2, keepdims=False)
        dp_summed = (
            jnp.einsum(
                "psr,po->sro",
                mine,
                jnp.concatenate([grad_pre, partner_grad], axis=0),
                preferred_element_type=jnp.float32,
            )
            * norm_scale
        )
    else:
        weight_part = (
            lax.dot_general(
                columns, grad_pre, (((0,), (0,)), ((), ())), preferred_element_type=jnp.float32
            )
            * norm_scale
        )
        weight_blocks_all = weight_part.reshape(seq_count, dp_count, -1, CO)
        dp_summed = ring_reduce_scatter(
            jnp.swapaxes(weight_blocks_all, 0, 1), "dp", list(range(dp_count))
        )
    half_co = CO // 2
    grad_weight = jnp.concatenate(
        [
            ring_reduce_scatter(dp_summed[:, :, :half_co], "seq", ring, True),
            ring_reduce_scatter(dp_summed[:, :, half_co:], "seq", ring, False),
        ],
        axis=1,
    )
    stacked = jnp.stack(
        [
            grad_padded[2 * half_kernel - offset : 2 * half_kernel - offset + positions]
            for offset in range(KW)
        ],
        axis=1,
    )
    weight_blocks = conv_weight.reshape(KW, C, CO)
    grad_normed = jnp.einsum(
        "pko,kco->pc", stacked, weight_blocks, preferred_element_type=jnp.float32
    )
    scaled_grad = grad_normed * channel_gain
    grad_merged = inverse * scaled_grad - merged * inverse**3 * jnp.mean(
        scaled_grad * merged, axis=1, keepdims=True
    )
    grad_skip = grad_merged.astype(jnp.bfloat16)
    grad_trunk = grad_merged.reshape(local_tokens, 2, C).sum(axis=1).astype(jnp.bfloat16)
    grad_heads = grad_trunk.reshape(local_tokens, H, DV)
    row_delta = jnp.sum(grad_heads.astype(jnp.float32) * attended.astype(jnp.float32), axis=2)
    value_grad = jnp.einsum(
        "ihd,jhd->hij", grad_heads, all_values, preferred_element_type=jnp.float32
    )
    slopes = (softmax * (value_grad - row_delta.T[:, :, None])).astype(jnp.bfloat16)
    grad_queries = (
        jnp.einsum("hij,jhd->ihd", slopes, all_keys, preferred_element_type=jnp.float32)
        * score_scale
    ).astype(jnp.bfloat16)
    key_part = (
        jnp.einsum("hij,ihd->jhd", slopes, query_heads, preferred_element_type=jnp.float32)
        * score_scale
    )
    value_part = jnp.einsum("hij,ihd->jhd", rounded, grad_heads, preferred_element_type=jnp.float32)
    terms = jnp.concatenate(
        [
            key_part.reshape(-1, H * DK),
            value_part.reshape(-1, H * DV),
        ],
        axis=1,
    ).astype(jnp.bfloat16)
    term_blocks = [
        terms[m * local_tokens : (m + 1) * local_tokens] for m in range(lax.axis_size("seq"))
    ]
    summed = ring_scatter_back(term_blocks, ring)
    grad_keys = summed[:, : H * DK].astype(jnp.bfloat16)
    grad_values = summed[:, H * DK :].astype(jnp.bfloat16)
    return (
        decoded[None],
        grad_queries.reshape(local_tokens, H * DK)[None],
        grad_keys[None],
        grad_values[None],
        grad_trunk[None],
        grad_skip[None],
        grad_weight,
    )


def solution(mesh):
    return jax.shard_map(
        functools.partial(body, ring_order(mesh)),
        mesh=mesh,
        in_specs=(
            P(("group", "dp"), "seq", None),
            P(("group", "dp"), "seq", None),
            P(("group", "dp"), "seq", None),
            P(("group", "dp"), "seq", None),
            P(("group", "dp"), "seq", None),
            P(),
            P(),
            P(("group", "dp"), "seq", None),
        ),
        out_specs=(
            P(("group", "dp"), "seq", None),
            P(("group", "dp"), "seq", None),
            P(("group", "dp"), "seq", None),
            P(("group", "dp"), "seq", None),
            P(("group", "dp"), "seq", None),
            P(("group", "dp"), "seq", None),
            P(("group", "seq", "dp"), None),
        ),
        check_vma=False,
    )
```

```python
import functools
import math

import jax
import jax.numpy as jnp
from jax import lax
from jax.sharding import PartitionSpec as P

H = 4
DK = 128
DV = 192
C = 768
CO = 384
KW = 5


def extended(array, sides, width):
    for axis, dim in sides:
        count, length = (lax.axis_size(axis), array.shape[dim])
        up = [(i, (i + 1) % count) for i in range(count - 1)]
        down = [(j, i) for i, j in up]
        last = lax.slice_in_dim(array, length - width, length, axis=dim)
        initial = lax.slice_in_dim(array, 0, width, axis=dim)
        before = lax.ppermute(last, axis, up)
        after = lax.ppermute(initial, axis, down)
        array = jnp.concatenate([before, array, after], axis=dim)
    return array


def gelu_parts(preact):
    cdf_value = 0.5 * (1.0 + jax.scipy.special.erf(preact * (1.0 / math.sqrt(2.0))))
    density = jnp.exp(-0.5 * preact * preact) * (1.0 / math.sqrt(2.0 * math.pi))
    return (preact * cdf_value, cdf_value + preact * density)


def window_rows(padded, kernel, row_count):
    return jnp.concatenate(
        [padded[offset : offset + row_count] for offset in range(kernel)], axis=1
    )


def ring_order(mesh):
    count = mesh.shape["seq"]
    try:
        row = mesh.devices.reshape(mesh.shape["group"], count, -1)[0, :, 0]
        coords = [tuple(device.coords) for device in row]
    except (AttributeError, TypeError):
        return list(range(count))
    varying = [d for d in range(3) if len({c[d] for c in coords}) > 1]
    if len(varying) == 2:
        for minor, major in (varying, varying[::-1]):
            if len({c[minor] for c in coords}) == 2:
                low = min(c[minor] for c in coords)
                first = sorted((c[major], s) for s, c in enumerate(coords) if c[minor] == low)
                second = sorted((c[major], s) for s, c in enumerate(coords) if c[minor] != low)
                return [s for _, s in first] + [s for _, s in second[::-1]]
    return list(range(count))


def ring_perms(ring):
    count = len(ring)
    forward = [(ring[q], ring[(q + 1) % count]) for q in range(count)]
    backward = [(ring[q], ring[(q - 1) % count]) for q in range(count)]
    return forward, backward


def ring_gather(block, ring):
    count = len(ring)
    forward, backward = ring_perms(ring)
    left_steps = count // 2
    right_steps = count - 1 - left_steps
    lefts, rights = [], []
    current = block
    for _ in range(left_steps):
        current = lax.ppermute(current, "seq", forward)
        lefts.append(current)
    current = block
    for _ in range(right_steps):
        current = lax.ppermute(current, "seq", backward)
        rights.append(current)
    return [block] + lefts + rights


def ring_scatter_back(blocks, ring):
    count = len(ring)
    forward, backward = ring_perms(ring)
    left_steps = count // 2
    right_steps = count - 1 - left_steps
    own = blocks[0].astype(jnp.float32)
    lefts = blocks[1 : 1 + left_steps]
    rights = blocks[1 + left_steps :]
    total = own
    if left_steps:
        acc = lefts[-1]
        for t in range(left_steps, 0, -1):
            received = lax.ppermute(acc, "seq", backward).astype(jnp.float32)
            if t == 1:
                total = total + received
            else:
                acc = (received + lefts[t - 2].astype(jnp.float32)).astype(jnp.bfloat16)
    if right_steps:
        acc = rights[-1]
        for t in range(right_steps, 0, -1):
            received = lax.ppermute(acc, "seq", forward).astype(jnp.float32)
            if t == 1:
                total = total + received
            else:
                acc = (received + rights[t - 2].astype(jnp.float32)).astype(jnp.bfloat16)
    return total


def ring_reduce_scatter(blocks, axis, ring, forward_dir=True):
    count = len(ring)
    if count == 1:
        return blocks[0]
    forward, backward = ring_perms(ring)
    perm = forward if forward_dir else backward
    sign = 1 if forward_dir else -1
    position = jnp.zeros((), jnp.int32)
    index = lax.axis_index(axis)
    for q, s in enumerate(ring):
        position = jnp.where(index == s, q, position)
    offsets = (position + count - sign * jnp.arange(count, dtype=jnp.int32)) % count
    order = jnp.zeros((count,), jnp.int32)
    for q, s in enumerate(ring):
        order = jnp.where(offsets == q, s, order)
    relative = jnp.take(blocks, order, axis=0)
    acc = relative[1]
    for t in range(count - 1):
        received = lax.ppermute(acc, axis, perm)
        acc = received + relative[(t + 2) % count]
    return acc


def body(ring, queries, key_rows, value_rows, trunk_state, skip_input, norm_gain, conv_weight, cotangent):
    score_scale = DK ** (-0.5)
    local_tokens = queries.shape[1]
    positions = 2 * local_tokens
    half_kernel = KW // 2
    query_heads = queries[0].reshape(local_tokens, H, DK)
    key_value_blocks = ring_gather(jnp.concatenate([key_rows[0], value_rows[0]], axis=1), ring)
    gathered = jnp.concatenate(key_value_blocks, axis=0)
    all_keys = gathered[:, : H * DK].reshape(-1, H, DK)
    all_values = gathered[:, H * DK :].reshape(-1, H, DV)
    scores = (
        jnp.einsum("ihd,jhd->hij", query_heads, all_keys, preferred_element_type=jnp.float32)
        * score_scale
    )
    row_peak = jnp.max(scores, axis=2, keepdims=True)
    row_total = jnp.sum(jnp.exp(scores - row_peak), axis=2, keepdims=True)
    logsum = row_peak + jnp.log(row_total)
    softmax = jnp.exp(scores - logsum)
    rounded = softmax.astype(jnp.bfloat16)
    attended = jnp.einsum(
        "hij,jhd->ihd", rounded, all_values, preferred_element_type=jnp.float32
    ).astype(jnp.bfloat16)
    hidden = trunk_state[0].astype(jnp.float32) + attended.reshape(local_tokens, H * DV).astype(
        jnp.float32
    )
    merged = jnp.repeat(hidden, 2, axis=0) + skip_input[0].astype(jnp.float32)
    inverse = lax.rsqrt(jnp.mean(merged * merged, axis=1, keepdims=True) + 1e-06)
    channel_gain = norm_gain.astype(jnp.float32)
    normed = (merged * inverse * channel_gain).astype(jnp.bfloat16)
    padded = extended(normed, (("seq", 0),), half_kernel)
    columns = window_rows(padded, KW, positions)
    preact = jnp.dot(columns, conv_weight, preferred_element_type=jnp.float32)
    activated, derivative = gelu_parts(preact)
    decoded = activated.astype(jnp.bfloat16)
    grad_pre = (cotangent[0].astype(jnp.float32) * derivative).astype(jnp.bfloat16)
    grad_padded = extended(grad_pre, (("seq", 0),), half_kernel)
    norm_scale = (lax.axis_size("dp") * positions * lax.axis_size("seq")) ** (-0.5)
    seq_count, dp_count = lax.axis_size("seq"), lax.axis_size("dp")
    rows_per = KW * C // (seq_count * dp_count)
    if dp_count == 2:
        partner = [(0, 1), (1, 0)]
        partner_padded = lax.ppermute(padded, "dp", partner)
        partner_grad = lax.ppermute(grad_pre, "dp", partner)
        both_columns = jnp.concatenate(
            [columns, window_rows(partner_padded, KW, positions)], axis=0
        ).reshape(2 * positions, seq_count, dp_count, rows_per)
        mine = lax.dynamic_index_in_dim(both_columns, lax.axis_index("dp"), axis=2, keepdims=False)
        dp_summed = (
            jnp.einsum(
                "psr,po->sro",
                mine,
                jnp.concatenate([grad_pre, partner_grad], axis=0),
                preferred_element_type=jnp.float32,
            )
            * norm_scale
        )
    else:
        weight_part = (
            lax.dot_general(
                columns, grad_pre, (((0,), (0,)), ((), ())), preferred_element_type=jnp.float32
            )
            * norm_scale
        )
        weight_blocks_all = weight_part.reshape(seq_count, dp_count, -1, CO)
        dp_summed = ring_reduce_scatter(
            jnp.swapaxes(weight_blocks_all, 0, 1), "dp", list(range(dp_count))
        )
    half_co = CO // 2
    grad_weight = jnp.concatenate(
        [
            ring_reduce_scatter(dp_summed[:, :, :half_co], "seq", ring, True),
            ring_reduce_scatter(dp_summed[:, :, half_co:], "seq", ring, False),
        ],
        axis=1,
    )
    stacked = jnp.stack(
        [
            grad_padded[2 * half_kernel - offset : 2 * half_kernel - offset + positions]
            for offset in range(KW)
        ],
        axis=1,
    )
    weight_blocks = conv_weight.reshape(KW, C, CO)
    grad_normed = jnp.einsum(
        "pko,kco->pc", stacked, weight_blocks, preferred_element_type=jnp.float32
    )
    scaled_grad = grad_normed * channel_gain
    grad_merged = inverse * scaled_grad - merged * inverse**3 * jnp.mean(
        scaled_grad * merged, axis=1, keepdims=True
    )
    grad_skip = grad_merged.astype(jnp.bfloat16)
    grad_trunk = grad_merged.reshape(local_tokens, 2, C).sum(axis=1).astype(jnp.bfloat16)
    grad_heads = grad_trunk.reshape(local_tokens, H, DV)
    row_delta = jnp.sum(grad_heads.astype(jnp.float32) * attended.astype(jnp.float32), axis=2)
    value_grad = jnp.einsum(
        "ihd,jhd->hij", grad_heads, all_values, preferred_element_type=jnp.float32
    )
    slopes = (softmax * (value_grad - row_delta.T[:, :, None])).astype(jnp.bfloat16)
    grad_queries = (
        jnp.einsum("hij,jhd->ihd", slopes, all_keys, preferred_element_type=jnp.float32)
        * score_scale
    ).astype(jnp.bfloat16)
    key_part = (
        jnp.einsum("hij,ihd->jhd", slopes, query_heads, preferred_element_type=jnp.float32)
        * score_scale
    )
    value_part = jnp.einsum("hij,ihd->jhd", rounded, grad_heads, preferred_element_type=jnp.float32)
    terms = jnp.concatenate(
        [
            key_part.reshape(-1, H * DK),
            value_part.reshape(-1, H * DV),
        ],
        axis=1,
    ).astype(jnp.bfloat16)
    term_blocks = [
        terms[m * local_tokens : (m + 1) * local_tokens] for m in range(lax.axis_size("seq"))
    ]
    summed = ring_scatter_back(term_blocks, ring)
    grad_keys = summed[:, : H * DK].astype(jnp.bfloat16)
    grad_values = summed[:, H * DK :].astype(jnp.bfloat16)
    return (
        decoded[None],
        grad_queries.reshape(local_tokens, H * DK)[None],
        grad_keys[None],
        grad_values[None],
        grad_trunk[None],
        grad_skip[None],
        grad_weight,
    )


def solution(mesh):
    return jax.shard_map(
        functools.partial(body, ring_order(mesh)),
        mesh=mesh,
        in_specs=(
            P(("group", "dp"), "seq", None),
            P(("group", "dp"), "seq", None),
            P(("group", "dp"), "seq", None),
            P(("group", "dp"), "seq", None),
            P(("group", "dp"), "seq", None),
            P(),
            P(),
            P(("group", "dp"), "seq", None),
        ),
        out_specs=(
            P(("group", "dp"), "seq", None),
            P(("group", "dp"), "seq", None),
            P(("group", "dp"), "seq", None),
            P(("group", "dp"), "seq", None),
            P(("group", "dp"), "seq", None),
            P(("group", "dp"), "seq", None),
            P(("group", "seq", "dp"), None),
        ),
        check_vma=False,
    )
```

```python
import functools
import math

import jax
import jax.numpy as jnp
from jax import lax
from jax.sharding import PartitionSpec as P

H = 4
DK = 128
DV = 192
C = 768
CO = 384
KW = 5


def extended(array, sides, width):
    for axis, dim in sides:
        count, length = (lax.axis_size(axis), array.shape[dim])
        up = [(i, (i + 1) % count) for i in range(count - 1)]
        down = [(j, i) for i, j in up]
        last = lax.slice_in_dim(array, length - width, length, axis=dim)
        initial = lax.slice_in_dim(array, 0, width, axis=dim)
        before = lax.ppermute(last, axis, up)
        after = lax.ppermute(initial, axis, down)
        array = jnp.concatenate([before, array, after], axis=dim)
    return array


def gelu_parts(preact):
    cdf_value = 0.5 * (1.0 + jax.scipy.special.erf(preact * (1.0 / math.sqrt(2.0))))
    density = jnp.exp(-0.5 * preact * preact) * (1.0 / math.sqrt(2.0 * math.pi))
    return (preact * cdf_value, cdf_value + preact * density)


def window_rows(padded, kernel, row_count):
    return jnp.concatenate(
        [padded[offset : offset + row_count] for offset in range(kernel)], axis=1
    )


def ring_order(mesh):
    count = mesh.shape["seq"]
    try:
        row = mesh.devices.reshape(mesh.shape["group"], count, -1)[0, :, 0]
        coords = [tuple(device.coords) for device in row]
    except (AttributeError, TypeError):
        return list(range(count))
    varying = [d for d in range(3) if len({c[d] for c in coords}) > 1]
    if len(varying) == 2:
        for minor, major in (varying, varying[::-1]):
            if len({c[minor] for c in coords}) == 2:
                low = min(c[minor] for c in coords)
                first = sorted((c[major], s) for s, c in enumerate(coords) if c[minor] == low)
                second = sorted((c[major], s) for s, c in enumerate(coords) if c[minor] != low)
                return [s for _, s in first] + [s for _, s in second[::-1]]
    return list(range(count))


def ring_perms(ring):
    count = len(ring)
    forward = [(ring[q], ring[(q + 1) % count]) for q in range(count)]
    backward = [(ring[q], ring[(q - 1) % count]) for q in range(count)]
    return forward, backward


def ring_gather(block, ring):
    count = len(ring)
    forward, backward = ring_perms(ring)
    left_steps = count // 2
    right_steps = count - 1 - left_steps
    lefts, rights = [], []
    current = block
    for _ in range(left_steps):
        current = lax.ppermute(current, "seq", forward)
        lefts.append(current)
    current = block
    for _ in range(right_steps):
        current = lax.ppermute(current, "seq", backward)
        rights.append(current)
    return [block] + lefts + rights


def ring_scatter_back(blocks, ring):
    count = len(ring)
    forward, backward = ring_perms(ring)
    left_steps = count // 2
    right_steps = count - 1 - left_steps
    own = blocks[0].astype(jnp.float32)
    lefts = blocks[1 : 1 + left_steps]
    rights = blocks[1 + left_steps :]
    total = own
    if left_steps:
        acc = lefts[-1]
        for t in range(left_steps, 0, -1):
            received = lax.ppermute(acc, "seq", backward).astype(jnp.float32)
            if t == 1:
                total = total + received
            else:
                acc = (received + lefts[t - 2].astype(jnp.float32)).astype(jnp.bfloat16)
    if right_steps:
        acc = rights[-1]
        for t in range(right_steps, 0, -1):
            received = lax.ppermute(acc, "seq", forward).astype(jnp.float32)
            if t == 1:
                total = total + received
            else:
                acc = (received + rights[t - 2].astype(jnp.float32)).astype(jnp.bfloat16)
    return total


def ring_reduce_scatter(blocks, axis, ring, forward_dir=True):
    count = len(ring)
    if count == 1:
        return blocks[0]
    forward, backward = ring_perms(ring)
    perm = forward if forward_dir else backward
    sign = 1 if forward_dir else -1
    position = jnp.zeros((), jnp.int32)
    index = lax.axis_index(axis)
    for q, s in enumerate(ring):
        position = jnp.where(index == s, q, position)
    offsets = (position + count - sign * jnp.arange(count, dtype=jnp.int32)) % count
    order = jnp.zeros((count,), jnp.int32)
    for q, s in enumerate(ring):
        order = jnp.where(offsets == q, s, order)
    relative = jnp.take(blocks, order, axis=0)
    acc = relative[1]
    for t in range(count - 1):
        received = lax.ppermute(acc, axis, perm)
        acc = received + relative[(t + 2) % count]
    return acc


def ring_position(axis, ring):
    position = jnp.zeros((), jnp.int32)
    index = lax.axis_index(axis)
    for q, s in enumerate(ring):
        position = jnp.where(index == s, q, position)
    return position


def ring_reduce_scatter_sliced(select_block, axis, ring, forward_dir=True):
    count = len(ring)
    forward, backward = ring_perms(ring)
    perm = forward if forward_dir else backward
    sign = 1 if forward_dir else -1
    position = ring_position(axis, ring)

    def block_at(offset):
        target = (position + count - sign * (offset % count)) % count
        index = jnp.zeros((), jnp.int32)
        for q, s in enumerate(ring):
            index = jnp.where(target == q, s, index)
        return select_block(index)

    acc = block_at(1)
    for t in range(count - 1):
        received = lax.ppermute(acc, axis, perm)
        acc = received + block_at(t + 2)
    return acc


def body(ring, queries, key_rows, value_rows, trunk_state, skip_input, norm_gain, conv_weight, cotangent):
    score_scale = DK ** (-0.5)
    local_tokens = queries.shape[1]
    positions = 2 * local_tokens
    half_kernel = KW // 2
    query_heads = queries[0].reshape(local_tokens, H, DK)
    key_value_blocks = ring_gather(jnp.concatenate([key_rows[0], value_rows[0]], axis=1), ring)
    gathered = jnp.concatenate(key_value_blocks, axis=0)
    all_keys = gathered[:, : H * DK].reshape(-1, H, DK)
    all_values = gathered[:, H * DK :].reshape(-1, H, DV)
    scores = (
        jnp.einsum("ihd,jhd->hij", query_heads, all_keys, preferred_element_type=jnp.float32)
        * score_scale
    )
    row_peak = jnp.max(scores, axis=2, keepdims=True)
    row_total = jnp.sum(jnp.exp(scores - row_peak), axis=2, keepdims=True)
    logsum = row_peak + jnp.log(row_total)
    softmax = jnp.exp(scores - logsum)
    rounded = softmax.astype(jnp.bfloat16)
    attended = jnp.einsum(
        "hij,jhd->ihd", rounded, all_values, preferred_element_type=jnp.float32
    ).astype(jnp.bfloat16)
    hidden = trunk_state[0].astype(jnp.float32) + attended.reshape(local_tokens, H * DV).astype(
        jnp.float32
    )
    merged = jnp.repeat(hidden, 2, axis=0) + skip_input[0].astype(jnp.float32)
    inverse = lax.rsqrt(jnp.mean(merged * merged, axis=1, keepdims=True) + 1e-06)
    channel_gain = norm_gain.astype(jnp.float32)
    normed = (merged * inverse * channel_gain).astype(jnp.bfloat16)
    padded = extended(normed, (("seq", 0),), half_kernel)
    columns = window_rows(padded, KW, positions)
    preact = jnp.dot(columns, conv_weight, preferred_element_type=jnp.float32)
    activated, derivative = gelu_parts(preact)
    decoded = activated.astype(jnp.bfloat16)
    grad_pre = (cotangent[0].astype(jnp.float32) * derivative).astype(jnp.bfloat16)
    grad_padded = extended(grad_pre, (("seq", 0),), half_kernel)
    norm_scale = (lax.axis_size("dp") * positions * lax.axis_size("seq")) ** (-0.5)
    seq_count, dp_count = lax.axis_size("seq"), lax.axis_size("dp")
    rows_per = KW * C // (seq_count * dp_count)
    half_co = CO // 2
    if dp_count == 2:
        partner = [(0, 1), (1, 0)]
        both_padded = jnp.stack([padded, lax.ppermute(padded, "dp", partner)])
        both_grad = jnp.stack([grad_pre, lax.ppermute(grad_pre, "dp", partner)])
        full_weight = (
            jnp.concatenate(
                [
                    jnp.einsum(
                        "spc,spo->co",
                        both_padded[:, offset : offset + positions],
                        both_grad,
                        preferred_element_type=jnp.float32,
                    )
                    for offset in range(KW)
                ],
                axis=0,
            )
            * norm_scale
        ).reshape(seq_count, dp_count, rows_per, CO)
        dp_index = lax.axis_index("dp")

        def weight_block(column, width):
            return lambda index: lax.dynamic_slice(
                full_weight, (index, dp_index, 0, column), (1, 1, rows_per, width)
            ).reshape(rows_per, width)

        grad_weight = jnp.concatenate(
            [
                ring_reduce_scatter_sliced(weight_block(0, half_co), "seq", ring, True),
                ring_reduce_scatter_sliced(
                    weight_block(half_co, CO - half_co), "seq", ring, False
                ),
            ],
            axis=1,
        )
    else:
        weight_part = (
            lax.dot_general(
                columns, grad_pre, (((0,), (0,)), ((), ())), preferred_element_type=jnp.float32
            )
            * norm_scale
        )
        weight_blocks_all = weight_part.reshape(seq_count, dp_count, -1, CO)
        dp_summed = ring_reduce_scatter(
            jnp.swapaxes(weight_blocks_all, 0, 1), "dp", list(range(dp_count))
        )
        grad_weight = jnp.concatenate(
            [
                ring_reduce_scatter(dp_summed[:, :, :half_co], "seq", ring, True),
                ring_reduce_scatter(dp_summed[:, :, half_co:], "seq", ring, False),
            ],
            axis=1,
        )
    stacked = jnp.stack(
        [
            grad_padded[2 * half_kernel - offset : 2 * half_kernel - offset + positions]
            for offset in range(KW)
        ],
        axis=1,
    )
    weight_blocks = conv_weight.reshape(KW, C, CO)
    grad_normed = jnp.einsum(
        "pko,kco->pc", stacked, weight_blocks, preferred_element_type=jnp.float32
    )
    scaled_grad = grad_normed * channel_gain
    grad_merged = inverse * scaled_grad - merged * inverse**3 * jnp.mean(
        scaled_grad * merged, axis=1, keepdims=True
    )
    grad_skip = grad_merged.astype(jnp.bfloat16)
    grad_trunk = grad_merged.reshape(local_tokens, 2, C).sum(axis=1).astype(jnp.bfloat16)
    grad_heads = grad_trunk.reshape(local_tokens, H, DV)
    row_delta = jnp.sum(grad_heads.astype(jnp.float32) * attended.astype(jnp.float32), axis=2)
    value_grad = jnp.einsum(
        "ihd,jhd->hij", grad_heads, all_values, preferred_element_type=jnp.float32
    )
    slopes = (softmax * (value_grad - row_delta.T[:, :, None])).astype(jnp.bfloat16)
    grad_queries = (
        jnp.einsum("hij,jhd->ihd", slopes, all_keys, preferred_element_type=jnp.float32)
        * score_scale
    ).astype(jnp.bfloat16)
    key_part = (
        jnp.einsum("hij,ihd->jhd", slopes, query_heads, preferred_element_type=jnp.float32)
        * score_scale
    )
    value_part = jnp.einsum("hij,ihd->jhd", rounded, grad_heads, preferred_element_type=jnp.float32)
    terms = jnp.concatenate(
        [
            key_part.reshape(-1, H * DK),
            value_part.reshape(-1, H * DV),
        ],
        axis=1,
    ).astype(jnp.bfloat16)
    term_blocks = [
        terms[m * local_tokens : (m + 1) * local_tokens] for m in range(lax.axis_size("seq"))
    ]
    summed = ring_scatter_back(term_blocks, ring)
    grad_keys = summed[:, : H * DK].astype(jnp.bfloat16)
    grad_values = summed[:, H * DK :].astype(jnp.bfloat16)
    return (
        decoded[None],
        grad_queries.reshape(local_tokens, H * DK)[None],
        grad_keys[None],
        grad_values[None],
        grad_trunk[None],
        grad_skip[None],
        grad_weight,
    )


def solution(mesh):
    return jax.shard_map(
        functools.partial(body, ring_order(mesh)),
        mesh=mesh,
        in_specs=(
            P(("group", "dp"), "seq", None),
            P(("group", "dp"), "seq", None),
            P(("group", "dp"), "seq", None),
            P(("group", "dp"), "seq", None),
            P(("group", "dp"), "seq", None),
            P(),
            P(),
            P(("group", "dp"), "seq", None),
        ),
        out_specs=(
            P(("group", "dp"), "seq", None),
            P(("group", "dp"), "seq", None),
            P(("group", "dp"), "seq", None),
            P(("group", "dp"), "seq", None),
            P(("group", "dp"), "seq", None),
            P(("group", "dp"), "seq", None),
            P(("group", "seq", "dp"), None),
        ),
        check_vma=False,
    )
```

```python
import functools
import math

import jax
import jax.numpy as jnp
from jax import lax
from jax.sharding import PartitionSpec as P

H = 4
DK = 128
DV = 192
C = 768
CO = 384
KW = 5


def extended(array, sides, width):
    for axis, dim in sides:
        count, length = (lax.axis_size(axis), array.shape[dim])
        up = [(i, (i + 1) % count) for i in range(count - 1)]
        down = [(j, i) for i, j in up]
        last = lax.slice_in_dim(array, length - width, length, axis=dim)
        initial = lax.slice_in_dim(array, 0, width, axis=dim)
        before = lax.ppermute(last, axis, up)
        after = lax.ppermute(initial, axis, down)
        array = jnp.concatenate([before, array, after], axis=dim)
    return array


def gelu_parts(preact):
    cdf_value = 0.5 * (1.0 + jax.scipy.special.erf(preact * (1.0 / math.sqrt(2.0))))
    density = jnp.exp(-0.5 * preact * preact) * (1.0 / math.sqrt(2.0 * math.pi))
    return (preact * cdf_value, cdf_value + preact * density)


def window_rows(padded, kernel, row_count):
    return jnp.concatenate(
        [padded[offset : offset + row_count] for offset in range(kernel)], axis=1
    )


def ring_order(mesh):
    count = mesh.shape["seq"]
    try:
        row = mesh.devices.reshape(mesh.shape["group"], count, -1)[0, :, 0]
        coords = [tuple(device.coords) for device in row]
    except (AttributeError, TypeError):
        return list(range(count))
    varying = [d for d in range(3) if len({c[d] for c in coords}) > 1]
    if len(varying) == 2:
        for minor, major in (varying, varying[::-1]):
            if len({c[minor] for c in coords}) == 2:
                low = min(c[minor] for c in coords)
                first = sorted((c[major], s) for s, c in enumerate(coords) if c[minor] == low)
                second = sorted((c[major], s) for s, c in enumerate(coords) if c[minor] != low)
                return [s for _, s in first] + [s for _, s in second[::-1]]
    return list(range(count))


def ring_perms(ring):
    count = len(ring)
    forward = [(ring[q], ring[(q + 1) % count]) for q in range(count)]
    backward = [(ring[q], ring[(q - 1) % count]) for q in range(count)]
    return forward, backward


def ring_gather(block, ring):
    count = len(ring)
    forward, backward = ring_perms(ring)
    left_steps = count // 2
    right_steps = count - 1 - left_steps
    lefts, rights = [], []
    current = block
    for _ in range(left_steps):
        current = lax.ppermute(current, "seq", forward)
        lefts.append(current)
    current = block
    for _ in range(right_steps):
        current = lax.ppermute(current, "seq", backward)
        rights.append(current)
    return [block] + lefts + rights


def ring_scatter_back(blocks, ring):
    count = len(ring)
    forward, backward = ring_perms(ring)
    left_steps = count // 2
    right_steps = count - 1 - left_steps
    own = blocks[0].astype(jnp.float32)
    lefts = blocks[1 : 1 + left_steps]
    rights = blocks[1 + left_steps :]
    total = own
    if left_steps:
        acc = lefts[-1]
        for t in range(left_steps, 0, -1):
            received = lax.ppermute(acc, "seq", backward).astype(jnp.float32)
            if t == 1:
                total = total + received
            else:
                acc = (received + lefts[t - 2].astype(jnp.float32)).astype(jnp.bfloat16)
    if right_steps:
        acc = rights[-1]
        for t in range(right_steps, 0, -1):
            received = lax.ppermute(acc, "seq", forward).astype(jnp.float32)
            if t == 1:
                total = total + received
            else:
                acc = (received + rights[t - 2].astype(jnp.float32)).astype(jnp.bfloat16)
    return total


def ring_reduce_scatter(blocks, axis, ring, forward_dir=True):
    count = len(ring)
    if count == 1:
        return blocks[0]
    forward, backward = ring_perms(ring)
    perm = forward if forward_dir else backward
    sign = 1 if forward_dir else -1
    position = jnp.zeros((), jnp.int32)
    index = lax.axis_index(axis)
    for q, s in enumerate(ring):
        position = jnp.where(index == s, q, position)
    offsets = (position + count - sign * jnp.arange(count, dtype=jnp.int32)) % count
    order = jnp.zeros((count,), jnp.int32)
    for q, s in enumerate(ring):
        order = jnp.where(offsets == q, s, order)
    relative = jnp.take(blocks, order, axis=0)
    acc = relative[1]
    for t in range(count - 1):
        received = lax.ppermute(acc, axis, perm)
        acc = received + relative[(t + 2) % count]
    return acc


def ring_position(axis, ring):
    position = jnp.zeros((), jnp.int32)
    index = lax.axis_index(axis)
    for q, s in enumerate(ring):
        position = jnp.where(index == s, q, position)
    return position


def ring_reduce_scatter_sliced(select_block, axis, ring, forward_dir=True, wire_dtype=jnp.bfloat16):
    count = len(ring)
    forward, backward = ring_perms(ring)
    perm = forward if forward_dir else backward
    sign = 1 if forward_dir else -1
    position = ring_position(axis, ring)

    def block_at(offset):
        target = (position + count - sign * (offset % count)) % count
        index = jnp.zeros((), jnp.int32)
        for q, s in enumerate(ring):
            index = jnp.where(target == q, s, index)
        return select_block(index)

    acc = block_at(1).astype(wire_dtype)
    for t in range(count - 1):
        received = lax.ppermute(acc, axis, perm).astype(jnp.float32)
        acc = received + block_at(t + 2)
        if t < count - 2:
            acc = acc.astype(wire_dtype)
    return acc


def body(ring, queries, key_rows, value_rows, trunk_state, skip_input, norm_gain, conv_weight, cotangent):
    score_scale = DK ** (-0.5)
    local_tokens = queries.shape[1]
    positions = 2 * local_tokens
    half_kernel = KW // 2
    query_heads = queries[0].reshape(local_tokens, H, DK)
    key_value_blocks = ring_gather(jnp.concatenate([key_rows[0], value_rows[0]], axis=1), ring)
    gathered = jnp.concatenate(key_value_blocks, axis=0)
    all_keys = gathered[:, : H * DK].reshape(-1, H, DK)
    all_values = gathered[:, H * DK :].reshape(-1, H, DV)
    scores = (
        jnp.einsum("ihd,jhd->hij", query_heads, all_keys, preferred_element_type=jnp.float32)
        * score_scale
    )
    row_peak = jnp.max(scores, axis=2, keepdims=True)
    row_total = jnp.sum(jnp.exp(scores - row_peak), axis=2, keepdims=True)
    logsum = row_peak + jnp.log(row_total)
    softmax = jnp.exp(scores - logsum)
    rounded = softmax.astype(jnp.bfloat16)
    attended = jnp.einsum(
        "hij,jhd->ihd", rounded, all_values, preferred_element_type=jnp.float32
    ).astype(jnp.bfloat16)
    hidden = trunk_state[0].astype(jnp.float32) + attended.reshape(local_tokens, H * DV).astype(
        jnp.float32
    )
    merged = jnp.repeat(hidden, 2, axis=0) + skip_input[0].astype(jnp.float32)
    inverse = lax.rsqrt(jnp.mean(merged * merged, axis=1, keepdims=True) + 1e-06)
    channel_gain = norm_gain.astype(jnp.float32)
    normed = (merged * inverse * channel_gain).astype(jnp.bfloat16)
    padded = extended(normed, (("seq", 0),), half_kernel)
    columns = window_rows(padded, KW, positions)
    preact = jnp.dot(columns, conv_weight, preferred_element_type=jnp.float32)
    activated, derivative = gelu_parts(preact)
    decoded = activated.astype(jnp.bfloat16)
    grad_pre = (cotangent[0].astype(jnp.float32) * derivative).astype(jnp.bfloat16)
    grad_padded = extended(grad_pre, (("seq", 0),), half_kernel)
    norm_scale = (lax.axis_size("dp") * positions * lax.axis_size("seq")) ** (-0.5)
    seq_count, dp_count = lax.axis_size("seq"), lax.axis_size("dp")
    rows_per = KW * C // (seq_count * dp_count)
    half_co = CO // 2
    if dp_count == 2:
        partner = [(0, 1), (1, 0)]
        both_padded = jnp.stack([padded, lax.ppermute(padded, "dp", partner)])
        both_grad = jnp.stack([grad_pre, lax.ppermute(grad_pre, "dp", partner)])
        full_weight = (
            jnp.concatenate(
                [
                    jnp.einsum(
                        "spc,spo->co",
                        both_padded[:, offset : offset + positions],
                        both_grad,
                        preferred_element_type=jnp.float32,
                    )
                    for offset in range(KW)
                ],
                axis=0,
            )
            * norm_scale
        ).reshape(seq_count, dp_count, rows_per, CO)
        dp_index = lax.axis_index("dp")

        def weight_block(column, width):
            return lambda index: lax.dynamic_slice(
                full_weight, (index, dp_index, 0, column), (1, 1, rows_per, width)
            ).reshape(rows_per, width)

        grad_weight = jnp.concatenate(
            [
                ring_reduce_scatter_sliced(weight_block(0, half_co), "seq", ring, True),
                ring_reduce_scatter_sliced(
                    weight_block(half_co, CO - half_co), "seq", ring, False
                ),
            ],
            axis=1,
        )
    else:
        weight_part = (
            lax.dot_general(
                columns, grad_pre, (((0,), (0,)), ((), ())), preferred_element_type=jnp.float32
            )
            * norm_scale
        )
        weight_blocks_all = weight_part.reshape(seq_count, dp_count, -1, CO)
        dp_summed = ring_reduce_scatter(
            jnp.swapaxes(weight_blocks_all, 0, 1), "dp", list(range(dp_count))
        )
        grad_weight = jnp.concatenate(
            [
                ring_reduce_scatter(dp_summed[:, :, :half_co], "seq", ring, True),
                ring_reduce_scatter(dp_summed[:, :, half_co:], "seq", ring, False),
            ],
            axis=1,
        )
    stacked = jnp.stack(
        [
            grad_padded[2 * half_kernel - offset : 2 * half_kernel - offset + positions]
            for offset in range(KW)
        ],
        axis=1,
    )
    weight_blocks = conv_weight.reshape(KW, C, CO)
    grad_normed = jnp.einsum(
        "pko,kco->pc", stacked, weight_blocks, preferred_element_type=jnp.float32
    )
    scaled_grad = grad_normed * channel_gain
    grad_merged = inverse * scaled_grad - merged * inverse**3 * jnp.mean(
        scaled_grad * merged, axis=1, keepdims=True
    )
    grad_skip = grad_merged.astype(jnp.bfloat16)
    grad_trunk = grad_merged.reshape(local_tokens, 2, C).sum(axis=1).astype(jnp.bfloat16)
    grad_heads = grad_trunk.reshape(local_tokens, H, DV)
    row_delta = jnp.sum(grad_heads.astype(jnp.float32) * attended.astype(jnp.float32), axis=2)
    value_grad = jnp.einsum(
        "ihd,jhd->hij", grad_heads, all_values, preferred_element_type=jnp.float32
    )
    slopes = (softmax * (value_grad - row_delta.T[:, :, None])).astype(jnp.bfloat16)
    grad_queries = (
        jnp.einsum("hij,jhd->ihd", slopes, all_keys, preferred_element_type=jnp.float32)
        * score_scale
    ).astype(jnp.bfloat16)
    key_part = (
        jnp.einsum("hij,ihd->jhd", slopes, query_heads, preferred_element_type=jnp.float32)
        * score_scale
    )
    value_part = jnp.einsum("hij,ihd->jhd", rounded, grad_heads, preferred_element_type=jnp.float32)
    terms = jnp.concatenate(
        [
            key_part.reshape(-1, H * DK),
            value_part.reshape(-1, H * DV),
        ],
        axis=1,
    ).astype(jnp.bfloat16)
    term_blocks = [
        terms[m * local_tokens : (m + 1) * local_tokens] for m in range(lax.axis_size("seq"))
    ]
    summed = ring_scatter_back(term_blocks, ring)
    grad_keys = summed[:, : H * DK].astype(jnp.bfloat16)
    grad_values = summed[:, H * DK :].astype(jnp.bfloat16)
    return (
        decoded[None],
        grad_queries.reshape(local_tokens, H * DK)[None],
        grad_keys[None],
        grad_values[None],
        grad_trunk[None],
        grad_skip[None],
        grad_weight,
    )


def solution(mesh):
    return jax.shard_map(
        functools.partial(body, ring_order(mesh)),
        mesh=mesh,
        in_specs=(
            P(("group", "dp"), "seq", None),
            P(("group", "dp"), "seq", None),
            P(("group", "dp"), "seq", None),
            P(("group", "dp"), "seq", None),
            P(("group", "dp"), "seq", None),
            P(),
            P(),
            P(("group", "dp"), "seq", None),
        ),
        out_specs=(
            P(("group", "dp"), "seq", None),
            P(("group", "dp"), "seq", None),
            P(("group", "dp"), "seq", None),
            P(("group", "dp"), "seq", None),
            P(("group", "dp"), "seq", None),
            P(("group", "dp"), "seq", None),
            P(("group", "seq", "dp"), None),
        ),
        check_vma=False,
    )
```

```python
import functools
import math

import jax
import jax.numpy as jnp
from jax import lax
from jax.sharding import PartitionSpec as P

H = 4
DK = 128
DV = 192
C = 768
CO = 384
KW = 5


def extended(array, sides, width):
    for axis, dim in sides:
        count, length = (lax.axis_size(axis), array.shape[dim])
        up = [(i, (i + 1) % count) for i in range(count - 1)]
        down = [(j, i) for i, j in up]
        last = lax.slice_in_dim(array, length - width, length, axis=dim)
        initial = lax.slice_in_dim(array, 0, width, axis=dim)
        before = lax.ppermute(last, axis, up)
        after = lax.ppermute(initial, axis, down)
        array = jnp.concatenate([before, array, after], axis=dim)
    return array


def gelu_parts(preact):
    cdf_value = 0.5 * (1.0 + jax.scipy.special.erf(preact * (1.0 / math.sqrt(2.0))))
    density = jnp.exp(-0.5 * preact * preact) * (1.0 / math.sqrt(2.0 * math.pi))
    return (preact * cdf_value, cdf_value + preact * density)


def window_rows(padded, kernel, row_count):
    return jnp.concatenate(
        [padded[offset : offset + row_count] for offset in range(kernel)], axis=1
    )


def ring_order(mesh):
    count = mesh.shape["seq"]
    try:
        row = mesh.devices.reshape(mesh.shape["group"], count, -1)[0, :, 0]
        coords = [tuple(device.coords) for device in row]
    except (AttributeError, TypeError):
        return list(range(count))
    varying = [d for d in range(3) if len({c[d] for c in coords}) > 1]
    if len(varying) == 2:
        for minor, major in (varying, varying[::-1]):
            if len({c[minor] for c in coords}) == 2:
                low = min(c[minor] for c in coords)
                first = sorted((c[major], s) for s, c in enumerate(coords) if c[minor] == low)
                second = sorted((c[major], s) for s, c in enumerate(coords) if c[minor] != low)
                return [s for _, s in first] + [s for _, s in second[::-1]]
    return list(range(count))


def ring_perms(ring):
    count = len(ring)
    forward = [(ring[q], ring[(q + 1) % count]) for q in range(count)]
    backward = [(ring[q], ring[(q - 1) % count]) for q in range(count)]
    return forward, backward


def ring_gather(block, ring):
    count = len(ring)
    forward, backward = ring_perms(ring)
    left_steps = count // 2
    right_steps = count - 1 - left_steps
    lefts, rights = [], []
    current = block
    for _ in range(left_steps):
        current = lax.ppermute(current, "seq", forward)
        lefts.append(current)
    current = block
    for _ in range(right_steps):
        current = lax.ppermute(current, "seq", backward)
        rights.append(current)
    return [block] + lefts + rights


def ring_scatter_back(blocks, ring):
    count = len(ring)
    forward, backward = ring_perms(ring)
    left_steps = count // 2
    right_steps = count - 1 - left_steps
    own = blocks[0].astype(jnp.float32)
    lefts = blocks[1 : 1 + left_steps]
    rights = blocks[1 + left_steps :]
    total = own
    if left_steps:
        acc = lefts[-1]
        for t in range(left_steps, 0, -1):
            received = lax.ppermute(acc, "seq", backward).astype(jnp.float32)
            if t == 1:
                total = total + received
            else:
                acc = (received + lefts[t - 2].astype(jnp.float32)).astype(jnp.bfloat16)
    if right_steps:
        acc = rights[-1]
        for t in range(right_steps, 0, -1):
            received = lax.ppermute(acc, "seq", forward).astype(jnp.float32)
            if t == 1:
                total = total + received
            else:
                acc = (received + rights[t - 2].astype(jnp.float32)).astype(jnp.bfloat16)
    return total


def ring_reduce_scatter(blocks, axis, ring, forward_dir=True):
    count = len(ring)
    if count == 1:
        return blocks[0]
    forward, backward = ring_perms(ring)
    perm = forward if forward_dir else backward
    sign = 1 if forward_dir else -1
    position = jnp.zeros((), jnp.int32)
    index = lax.axis_index(axis)
    for q, s in enumerate(ring):
        position = jnp.where(index == s, q, position)
    offsets = (position + count - sign * jnp.arange(count, dtype=jnp.int32)) % count
    order = jnp.zeros((count,), jnp.int32)
    for q, s in enumerate(ring):
        order = jnp.where(offsets == q, s, order)
    relative = jnp.take(blocks, order, axis=0)
    acc = relative[1]
    for t in range(count - 1):
        received = lax.ppermute(acc, axis, perm)
        acc = received + relative[(t + 2) % count]
    return acc


def ring_position(axis, ring):
    position = jnp.zeros((), jnp.int32)
    index = lax.axis_index(axis)
    for q, s in enumerate(ring):
        position = jnp.where(index == s, q, position)
    return position


def ring_reduce_scatter_sliced(select_block, axis, ring, forward_dir=True, wire_dtype=jnp.bfloat16):
    count = len(ring)
    forward, backward = ring_perms(ring)
    perm = forward if forward_dir else backward
    sign = 1 if forward_dir else -1
    position = ring_position(axis, ring)

    def block_at(offset):
        target = (position + count - sign * (offset % count)) % count
        index = jnp.zeros((), jnp.int32)
        for q, s in enumerate(ring):
            index = jnp.where(target == q, s, index)
        return select_block(index)

    acc = block_at(1).astype(wire_dtype)
    for t in range(count - 1):
        received = lax.ppermute(acc, axis, perm).astype(jnp.float32)
        acc = received + block_at(t + 2)
        if t < count - 2:
            acc = acc.astype(wire_dtype)
    return acc


def body(ring, queries, key_rows, value_rows, trunk_state, skip_input, norm_gain, conv_weight, cotangent):
    score_scale = DK ** (-0.5)
    local_tokens = queries.shape[1]
    positions = 2 * local_tokens
    half_kernel = KW // 2
    query_heads = queries[0].reshape(local_tokens, H, DK)
    key_value_blocks = ring_gather(jnp.concatenate([key_rows[0], value_rows[0]], axis=1), ring)
    all_keys = jnp.concatenate([block[:, : H * DK] for block in key_value_blocks], axis=0).reshape(
        -1, H, DK
    )
    all_values = jnp.concatenate(
        [block[:, H * DK :] for block in key_value_blocks], axis=0
    ).reshape(-1, H, DV)
    scores = (
        jnp.einsum("ihd,jhd->hij", query_heads, all_keys, preferred_element_type=jnp.float32)
        * score_scale
    )
    row_peak = jnp.max(scores, axis=2, keepdims=True)
    row_total = jnp.sum(jnp.exp(scores - row_peak), axis=2, keepdims=True)
    logsum = row_peak + jnp.log(row_total)
    softmax = jnp.exp(scores - logsum)
    rounded = softmax.astype(jnp.bfloat16)
    attended = jnp.einsum(
        "hij,jhd->ihd", rounded, all_values, preferred_element_type=jnp.float32
    ).astype(jnp.bfloat16)
    upsample = (
        jnp.arange(positions, dtype=jnp.int32)[:, None] // 2
        == jnp.arange(local_tokens, dtype=jnp.int32)[None, :]
    ).astype(jnp.bfloat16)
    hidden_up = jnp.dot(
        upsample, trunk_state[0], preferred_element_type=jnp.float32
    ) + jnp.dot(
        upsample, attended.reshape(local_tokens, H * DV), preferred_element_type=jnp.float32
    )
    merged = hidden_up + skip_input[0].astype(jnp.float32)
    inverse = lax.rsqrt(jnp.mean(merged * merged, axis=1, keepdims=True) + 1e-06)
    channel_gain = norm_gain.astype(jnp.float32)
    normed = (merged * inverse * channel_gain).astype(jnp.bfloat16)
    padded = extended(normed, (("seq", 0),), half_kernel)
    columns = window_rows(padded, KW, positions)
    preact = jnp.dot(columns, conv_weight, preferred_element_type=jnp.float32)
    activated, derivative = gelu_parts(preact)
    decoded = activated.astype(jnp.bfloat16)
    grad_pre = (cotangent[0].astype(jnp.float32) * derivative).astype(jnp.bfloat16)
    grad_padded = extended(grad_pre, (("seq", 0),), half_kernel)
    norm_scale = (lax.axis_size("dp") * positions * lax.axis_size("seq")) ** (-0.5)
    seq_count, dp_count = lax.axis_size("seq"), lax.axis_size("dp")
    rows_per = KW * C // (seq_count * dp_count)
    half_co = CO // 2
    if dp_count == 2:
        partner = [(0, 1), (1, 0)]
        both_padded = jnp.stack([padded, lax.ppermute(padded, "dp", partner)])
        both_grad = jnp.stack([grad_pre, lax.ppermute(grad_pre, "dp", partner)])
        full_weight = (
            jnp.concatenate(
                [
                    jnp.einsum(
                        "spc,spo->co",
                        both_padded[:, offset : offset + positions],
                        both_grad,
                        preferred_element_type=jnp.float32,
                    )
                    for offset in range(KW)
                ],
                axis=0,
            )
            * norm_scale
        ).reshape(seq_count, dp_count, rows_per, CO)
        dp_index = lax.axis_index("dp")

        def weight_block(column, width):
            return lambda index: lax.dynamic_slice(
                full_weight, (index, dp_index, 0, column), (1, 1, rows_per, width)
            ).reshape(rows_per, width)

        grad_weight = jnp.concatenate(
            [
                ring_reduce_scatter_sliced(weight_block(0, half_co), "seq", ring, True),
                ring_reduce_scatter_sliced(
                    weight_block(half_co, CO - half_co), "seq", ring, False
                ),
            ],
            axis=1,
        )
    else:
        weight_part = (
            lax.dot_general(
                columns, grad_pre, (((0,), (0,)), ((), ())), preferred_element_type=jnp.float32
            )
            * norm_scale
        )
        weight_blocks_all = weight_part.reshape(seq_count, dp_count, -1, CO)
        dp_summed = ring_reduce_scatter(
            jnp.swapaxes(weight_blocks_all, 0, 1), "dp", list(range(dp_count))
        )
        grad_weight = jnp.concatenate(
            [
                ring_reduce_scatter(dp_summed[:, :, :half_co], "seq", ring, True),
                ring_reduce_scatter(dp_summed[:, :, half_co:], "seq", ring, False),
            ],
            axis=1,
        )
    stacked = jnp.stack(
        [
            grad_padded[2 * half_kernel - offset : 2 * half_kernel - offset + positions]
            for offset in range(KW)
        ],
        axis=1,
    )
    weight_blocks = conv_weight.reshape(KW, C, CO)
    grad_normed = jnp.einsum(
        "pko,kco->pc", stacked, weight_blocks, preferred_element_type=jnp.float32
    )
    scaled_grad = grad_normed * channel_gain
    grad_merged = inverse * scaled_grad - merged * inverse**3 * jnp.mean(
        scaled_grad * merged, axis=1, keepdims=True
    )
    grad_skip = grad_merged.astype(jnp.bfloat16)
    grad_trunk = jnp.dot(
        upsample.T.astype(jnp.float32),
        grad_merged,
        precision=lax.Precision.HIGHEST,
        preferred_element_type=jnp.float32,
    ).astype(jnp.bfloat16)
    grad_heads = grad_trunk.reshape(local_tokens, H, DV)
    row_delta = jnp.sum(grad_heads.astype(jnp.float32) * attended.astype(jnp.float32), axis=2)
    value_grad = jnp.einsum(
        "ihd,jhd->hij", grad_heads, all_values, preferred_element_type=jnp.float32
    )
    slopes = (softmax * (value_grad - row_delta.T[:, :, None])).astype(jnp.bfloat16)
    grad_queries = (
        jnp.einsum("hij,jhd->ihd", slopes, all_keys, preferred_element_type=jnp.float32)
        * score_scale
    ).astype(jnp.bfloat16)
    key_part = (
        jnp.einsum("hij,ihd->jhd", slopes, query_heads, preferred_element_type=jnp.float32)
        * score_scale
    )
    value_part = jnp.einsum("hij,ihd->jhd", rounded, grad_heads, preferred_element_type=jnp.float32)
    terms = jnp.concatenate(
        [
            key_part.reshape(-1, H * DK),
            value_part.reshape(-1, H * DV),
        ],
        axis=1,
    ).astype(jnp.bfloat16)
    term_blocks = [
        terms[m * local_tokens : (m + 1) * local_tokens] for m in range(lax.axis_size("seq"))
    ]
    summed = ring_scatter_back(term_blocks, ring)
    grad_keys = summed[:, : H * DK].astype(jnp.bfloat16)
    grad_values = summed[:, H * DK :].astype(jnp.bfloat16)
    return (
        decoded[None],
        grad_queries.reshape(local_tokens, H * DK)[None],
        grad_keys[None],
        grad_values[None],
        grad_trunk[None],
        grad_skip[None],
        grad_weight,
    )


def solution(mesh):
    return jax.shard_map(
        functools.partial(body, ring_order(mesh)),
        mesh=mesh,
        in_specs=(
            P(("group", "dp"), "seq", None),
            P(("group", "dp"), "seq", None),
            P(("group", "dp"), "seq", None),
            P(("group", "dp"), "seq", None),
            P(("group", "dp"), "seq", None),
            P(),
            P(),
            P(("group", "dp"), "seq", None),
        ),
        out_specs=(
            P(("group", "dp"), "seq", None),
            P(("group", "dp"), "seq", None),
            P(("group", "dp"), "seq", None),
            P(("group", "dp"), "seq", None),
            P(("group", "dp"), "seq", None),
            P(("group", "dp"), "seq", None),
            P(("group", "seq", "dp"), None),
        ),
        check_vma=False,
    )
```

```python
import functools
import math

import jax
import jax.numpy as jnp
from jax import lax
from jax.sharding import PartitionSpec as P

H = 4
DK = 128
DV = 192
C = 768
CO = 384
KW = 5


def extended(array, sides, width):
    for axis, dim in sides:
        count, length = (lax.axis_size(axis), array.shape[dim])
        up = [(i, (i + 1) % count) for i in range(count - 1)]
        down = [(j, i) for i, j in up]
        last = lax.slice_in_dim(array, length - width, length, axis=dim)
        initial = lax.slice_in_dim(array, 0, width, axis=dim)
        before = lax.ppermute(last, axis, up)
        after = lax.ppermute(initial, axis, down)
        array = jnp.concatenate([before, array, after], axis=dim)
    return array


def gelu_parts(preact):
    cdf_value = 0.5 * (1.0 + jax.scipy.special.erf(preact * (1.0 / math.sqrt(2.0))))
    density = jnp.exp(-0.5 * preact * preact) * (1.0 / math.sqrt(2.0 * math.pi))
    return (preact * cdf_value, cdf_value + preact * density)


def window_rows(padded, kernel, row_count):
    return jnp.concatenate(
        [padded[offset : offset + row_count] for offset in range(kernel)], axis=1
    )


def ring_order(mesh):
    count = mesh.shape["seq"]
    try:
        row = mesh.devices.reshape(mesh.shape["group"], count, -1)[0, :, 0]
        coords = [tuple(device.coords) for device in row]
    except (AttributeError, TypeError):
        return list(range(count))
    varying = [d for d in range(3) if len({c[d] for c in coords}) > 1]
    if len(varying) == 2:
        for minor, major in (varying, varying[::-1]):
            if len({c[minor] for c in coords}) == 2:
                low = min(c[minor] for c in coords)
                first = sorted((c[major], s) for s, c in enumerate(coords) if c[minor] == low)
                second = sorted((c[major], s) for s, c in enumerate(coords) if c[minor] != low)
                return [s for _, s in first] + [s for _, s in second[::-1]]
    return list(range(count))


def ring_perms(ring):
    count = len(ring)
    forward = [(ring[q], ring[(q + 1) % count]) for q in range(count)]
    backward = [(ring[q], ring[(q - 1) % count]) for q in range(count)]
    return forward, backward


def ring_gather(block, ring):
    count = len(ring)
    forward, backward = ring_perms(ring)
    left_steps = count // 2
    right_steps = count - 1 - left_steps
    lefts, rights = [], []
    current = block
    for _ in range(left_steps):
        current = lax.ppermute(current, "seq", forward)
        lefts.append(current)
    current = block
    for _ in range(right_steps):
        current = lax.ppermute(current, "seq", backward)
        rights.append(current)
    return [block] + lefts + rights


def ring_scatter_back(blocks, ring):
    count = len(ring)
    forward, backward = ring_perms(ring)
    left_steps = count // 2
    right_steps = count - 1 - left_steps
    own = blocks[0].astype(jnp.float32)
    lefts = blocks[1 : 1 + left_steps]
    rights = blocks[1 + left_steps :]
    total = own
    if left_steps:
        acc = lefts[-1]
        for t in range(left_steps, 0, -1):
            received = lax.ppermute(acc, "seq", backward).astype(jnp.float32)
            if t == 1:
                total = total + received
            else:
                acc = (received + lefts[t - 2].astype(jnp.float32)).astype(jnp.bfloat16)
    if right_steps:
        acc = rights[-1]
        for t in range(right_steps, 0, -1):
            received = lax.ppermute(acc, "seq", forward).astype(jnp.float32)
            if t == 1:
                total = total + received
            else:
                acc = (received + rights[t - 2].astype(jnp.float32)).astype(jnp.bfloat16)
    return total


def ring_reduce_scatter(blocks, axis, ring, forward_dir=True):
    count = len(ring)
    if count == 1:
        return blocks[0]
    forward, backward = ring_perms(ring)
    perm = forward if forward_dir else backward
    sign = 1 if forward_dir else -1
    position = jnp.zeros((), jnp.int32)
    index = lax.axis_index(axis)
    for q, s in enumerate(ring):
        position = jnp.where(index == s, q, position)
    offsets = (position + count - sign * jnp.arange(count, dtype=jnp.int32)) % count
    order = jnp.zeros((count,), jnp.int32)
    for q, s in enumerate(ring):
        order = jnp.where(offsets == q, s, order)
    relative = jnp.take(blocks, order, axis=0)
    acc = relative[1]
    for t in range(count - 1):
        received = lax.ppermute(acc, axis, perm)
        acc = received + relative[(t + 2) % count]
    return acc


def ring_position(axis, ring):
    position = jnp.zeros((), jnp.int32)
    index = lax.axis_index(axis)
    for q, s in enumerate(ring):
        position = jnp.where(index == s, q, position)
    return position


def ring_reduce_scatter_sliced(select_block, axis, ring, forward_dir=True, wire_dtype=jnp.bfloat16):
    count = len(ring)
    forward, backward = ring_perms(ring)
    perm = forward if forward_dir else backward
    sign = 1 if forward_dir else -1
    position = ring_position(axis, ring)

    def block_at(offset):
        target = (position + count - sign * (offset % count)) % count
        index = jnp.zeros((), jnp.int32)
        for q, s in enumerate(ring):
            index = jnp.where(target == q, s, index)
        return select_block(index)

    acc = block_at(1).astype(wire_dtype)
    for t in range(count - 1):
        received = lax.ppermute(acc, axis, perm).astype(jnp.float32)
        acc = received + block_at(t + 2)
        if t < count - 2:
            acc = acc.astype(wire_dtype)
    return acc


def body(ring, queries, key_rows, value_rows, trunk_state, skip_input, norm_gain, conv_weight, cotangent):
    score_scale = DK ** (-0.5)
    local_tokens = queries.shape[1]
    positions = 2 * local_tokens
    half_kernel = KW // 2
    query_heads = queries[0].reshape(local_tokens, H, DK)
    key_value_blocks = ring_gather(jnp.concatenate([key_rows[0], value_rows[0]], axis=1), ring)
    gathered = jnp.concatenate(key_value_blocks, axis=0)
    all_keys = gathered[:, : H * DK].reshape(-1, H, DK)
    all_values = gathered[:, H * DK :].reshape(-1, H, DV)
    scores = (
        jnp.einsum("ihd,jhd->hij", query_heads, all_keys, preferred_element_type=jnp.float32)
        * score_scale
    )
    row_peak = jnp.max(scores, axis=2, keepdims=True)
    row_total = jnp.sum(jnp.exp(scores - row_peak), axis=2, keepdims=True)
    logsum = row_peak + jnp.log(row_total)
    softmax = jnp.exp(scores - logsum)
    rounded = softmax.astype(jnp.bfloat16)
    attended = jnp.einsum(
        "hij,jhd->ihd", rounded, all_values, preferred_element_type=jnp.float32
    ).astype(jnp.bfloat16)
    upsample = (
        jnp.arange(positions, dtype=jnp.int32)[:, None] // 2
        == jnp.arange(local_tokens, dtype=jnp.int32)[None, :]
    ).astype(jnp.bfloat16)
    hidden_up = jnp.dot(
        upsample, trunk_state[0], preferred_element_type=jnp.float32
    ) + jnp.dot(
        upsample, attended.reshape(local_tokens, H * DV), preferred_element_type=jnp.float32
    )
    merged = hidden_up + skip_input[0].astype(jnp.float32)
    inverse = lax.rsqrt(jnp.mean(merged * merged, axis=1, keepdims=True) + 1e-06)
    channel_gain = norm_gain.astype(jnp.float32)
    normed = (merged * inverse * channel_gain).astype(jnp.bfloat16)
    padded = extended(normed, (("seq", 0),), half_kernel)
    columns = window_rows(padded, KW, positions)
    preact = jnp.dot(columns, conv_weight, preferred_element_type=jnp.float32)
    activated, derivative = gelu_parts(preact)
    decoded = activated.astype(jnp.bfloat16)
    grad_pre = (cotangent[0].astype(jnp.float32) * derivative).astype(jnp.bfloat16)
    grad_padded = extended(grad_pre, (("seq", 0),), half_kernel)
    norm_scale = (lax.axis_size("dp") * positions * lax.axis_size("seq")) ** (-0.5)
    seq_count, dp_count = lax.axis_size("seq"), lax.axis_size("dp")
    rows_per = KW * C // (seq_count * dp_count)
    half_co = CO // 2
    if dp_count == 2:
        partner = [(0, 1), (1, 0)]
        both_padded = jnp.stack([padded, lax.ppermute(padded, "dp", partner)])
        both_grad = jnp.stack([grad_pre, lax.ppermute(grad_pre, "dp", partner)])
        full_weight = (
            jnp.concatenate(
                [
                    jnp.einsum(
                        "spc,spo->co",
                        both_padded[:, offset : offset + positions],
                        both_grad,
                        preferred_element_type=jnp.float32,
                    )
                    for offset in range(KW)
                ],
                axis=0,
            )
            * norm_scale
        ).reshape(seq_count, dp_count, rows_per, CO)
        dp_index = lax.axis_index("dp")

        def weight_block(column, width):
            return lambda index: lax.dynamic_slice(
                full_weight, (index, dp_index, 0, column), (1, 1, rows_per, width)
            ).reshape(rows_per, width)

        grad_weight = jnp.concatenate(
            [
                ring_reduce_scatter_sliced(weight_block(0, half_co), "seq", ring, True),
                ring_reduce_scatter_sliced(
                    weight_block(half_co, CO - half_co), "seq", ring, False
                ),
            ],
            axis=1,
        )
    else:
        weight_part = (
            lax.dot_general(
                columns, grad_pre, (((0,), (0,)), ((), ())), preferred_element_type=jnp.float32
            )
            * norm_scale
        )
        weight_blocks_all = weight_part.reshape(seq_count, dp_count, -1, CO)
        dp_summed = ring_reduce_scatter(
            jnp.swapaxes(weight_blocks_all, 0, 1), "dp", list(range(dp_count))
        )
        grad_weight = jnp.concatenate(
            [
                ring_reduce_scatter(dp_summed[:, :, :half_co], "seq", ring, True),
                ring_reduce_scatter(dp_summed[:, :, half_co:], "seq", ring, False),
            ],
            axis=1,
        )
    stacked = jnp.stack(
        [
            grad_padded[2 * half_kernel - offset : 2 * half_kernel - offset + positions]
            for offset in range(KW)
        ],
        axis=1,
    )
    weight_blocks = conv_weight.reshape(KW, C, CO)
    grad_normed = jnp.einsum(
        "pko,kco->pc", stacked, weight_blocks, preferred_element_type=jnp.float32
    )
    scaled_grad = grad_normed * channel_gain
    grad_merged = inverse * scaled_grad - merged * inverse**3 * jnp.mean(
        scaled_grad * merged, axis=1, keepdims=True
    )
    grad_skip = grad_merged.astype(jnp.bfloat16)
    grad_trunk = jnp.dot(
        upsample.T.astype(jnp.float32),
        grad_merged,
        precision=lax.Precision.HIGHEST,
        preferred_element_type=jnp.float32,
    ).astype(jnp.bfloat16)
    grad_heads = grad_trunk.reshape(local_tokens, H, DV)
    row_delta = jnp.sum(grad_heads.astype(jnp.float32) * attended.astype(jnp.float32), axis=2)
    value_grad = jnp.einsum(
        "ihd,jhd->hij", grad_heads, all_values, preferred_element_type=jnp.float32
    )
    slopes = (softmax * (value_grad - row_delta.T[:, :, None])).astype(jnp.bfloat16)
    grad_queries = (
        jnp.einsum("hij,jhd->ihd", slopes, all_keys, preferred_element_type=jnp.float32)
        * score_scale
    ).astype(jnp.bfloat16)
    key_part = (
        jnp.einsum("hij,ihd->jhd", slopes, query_heads, preferred_element_type=jnp.float32)
        * score_scale
    )
    value_part = jnp.einsum("hij,ihd->jhd", rounded, grad_heads, preferred_element_type=jnp.float32)
    terms = jnp.concatenate(
        [
            key_part.reshape(-1, H * DK),
            value_part.reshape(-1, H * DV),
        ],
        axis=1,
    ).astype(jnp.bfloat16)
    term_blocks = [
        terms[m * local_tokens : (m + 1) * local_tokens] for m in range(lax.axis_size("seq"))
    ]
    summed = ring_scatter_back(term_blocks, ring)
    grad_keys = summed[:, : H * DK].astype(jnp.bfloat16)
    grad_values = summed[:, H * DK :].astype(jnp.bfloat16)
    return (
        decoded[None],
        grad_queries.reshape(local_tokens, H * DK)[None],
        grad_keys[None],
        grad_values[None],
        grad_trunk[None],
        grad_skip[None],
        grad_weight,
    )


def solution(mesh):
    return jax.shard_map(
        functools.partial(body, ring_order(mesh)),
        mesh=mesh,
        in_specs=(
            P(("group", "dp"), "seq", None),
            P(("group", "dp"), "seq", None),
            P(("group", "dp"), "seq", None),
            P(("group", "dp"), "seq", None),
            P(("group", "dp"), "seq", None),
            P(),
            P(),
            P(("group", "dp"), "seq", None),
        ),
        out_specs=(
            P(("group", "dp"), "seq", None),
            P(("group", "dp"), "seq", None),
            P(("group", "dp"), "seq", None),
            P(("group", "dp"), "seq", None),
            P(("group", "dp"), "seq", None),
            P(("group", "dp"), "seq", None),
            P(("group", "seq", "dp"), None),
        ),
        check_vma=False,
    )
```

```python
import functools
import math

import jax
import jax.numpy as jnp
from jax import lax
from jax.sharding import PartitionSpec as P

H = 4
DK = 128
DV = 192
C = 768
CO = 384
KW = 5


def extended(array, sides, width):
    for axis, dim in sides:
        count, length = (lax.axis_size(axis), array.shape[dim])
        up = [(i, (i + 1) % count) for i in range(count - 1)]
        down = [(j, i) for i, j in up]
        last = lax.slice_in_dim(array, length - width, length, axis=dim)
        initial = lax.slice_in_dim(array, 0, width, axis=dim)
        before = lax.ppermute(last, axis, up)
        after = lax.ppermute(initial, axis, down)
        array = jnp.concatenate([before, array, after], axis=dim)
    return array


def gelu_parts(preact):
    cdf_value = 0.5 * (1.0 + jax.scipy.special.erf(preact * (1.0 / math.sqrt(2.0))))
    density = jnp.exp(-0.5 * preact * preact) * (1.0 / math.sqrt(2.0 * math.pi))
    return (preact * cdf_value, cdf_value + preact * density)


def window_rows(padded, kernel, row_count):
    return jnp.concatenate(
        [padded[offset : offset + row_count] for offset in range(kernel)], axis=1
    )


def ring_order(mesh):
    count = mesh.shape["seq"]
    try:
        row = mesh.devices.reshape(mesh.shape["group"], count, -1)[0, :, 0]
        coords = [tuple(device.coords) for device in row]
    except (AttributeError, TypeError):
        return list(range(count))
    varying = [d for d in range(3) if len({c[d] for c in coords}) > 1]
    if len(varying) == 2:
        for minor, major in (varying, varying[::-1]):
            if len({c[minor] for c in coords}) == 2:
                low = min(c[minor] for c in coords)
                first = sorted((c[major], s) for s, c in enumerate(coords) if c[minor] == low)
                second = sorted((c[major], s) for s, c in enumerate(coords) if c[minor] != low)
                return [s for _, s in first] + [s for _, s in second[::-1]]
    return list(range(count))


def ring_perms(ring):
    count = len(ring)
    forward = [(ring[q], ring[(q + 1) % count]) for q in range(count)]
    backward = [(ring[q], ring[(q - 1) % count]) for q in range(count)]
    return forward, backward


def ring_gather(block, ring):
    count = len(ring)
    forward, backward = ring_perms(ring)
    full_steps = (count - 1) // 2
    split = count % 2 == 0
    half = block.shape[1] // 2
    lefts, rights = [], []
    current = block
    for _ in range(full_steps):
        current = lax.ppermute(current, "seq", forward)
        lefts.append(current)
    if split:
        left_half = lax.ppermute(current[:, :half], "seq", forward)
    current = block
    for _ in range(full_steps):
        current = lax.ppermute(current, "seq", backward)
        rights.append(current)
    if split:
        right_half = lax.ppermute(current[:, half:], "seq", backward)
    opposite = [jnp.concatenate([left_half, right_half], axis=1)] if split else []
    return [block] + lefts + rights + opposite


def add_part(term, received, side):
    if received.shape == term.shape:
        return term + received
    half = term.shape[1] - received.shape[1] if side else received.shape[1]
    if side:
        return jnp.concatenate([term[:, :half], term[:, half:] + received], axis=1)
    return jnp.concatenate([term[:, :half] + received, term[:, half:]], axis=1)


def ring_scatter_back(blocks, ring):
    count = len(ring)
    forward, backward = ring_perms(ring)
    full_steps = (count - 1) // 2
    split = count % 2 == 0
    own = blocks[0].astype(jnp.float32)
    lefts = blocks[1 : 1 + full_steps]
    rights = blocks[1 + full_steps : 1 + 2 * full_steps]
    total = own
    for side, chain, perm in ((0, lefts, backward), (1, rights, forward)):
        if split:
            half = blocks[-1].shape[1] // 2
            acc = blocks[-1][:, half:] if side else blocks[-1][:, :half]
            top = full_steps + 1
        elif full_steps:
            acc = chain[-1]
            top = full_steps
        else:
            continue
        for t in range(top, 0, -1):
            received = lax.ppermute(acc, "seq", perm).astype(jnp.float32)
            if t == 1:
                total = add_part(total, received, side)
            else:
                acc = add_part(chain[t - 2].astype(jnp.float32), received, side).astype(
                    jnp.bfloat16
                )
    return total


def ring_reduce_scatter(blocks, axis, ring, forward_dir=True):
    count = len(ring)
    if count == 1:
        return blocks[0]
    forward, backward = ring_perms(ring)
    perm = forward if forward_dir else backward
    sign = 1 if forward_dir else -1
    position = jnp.zeros((), jnp.int32)
    index = lax.axis_index(axis)
    for q, s in enumerate(ring):
        position = jnp.where(index == s, q, position)
    offsets = (position + count - sign * jnp.arange(count, dtype=jnp.int32)) % count
    order = jnp.zeros((count,), jnp.int32)
    for q, s in enumerate(ring):
        order = jnp.where(offsets == q, s, order)
    relative = jnp.take(blocks, order, axis=0)
    acc = relative[1]
    for t in range(count - 1):
        received = lax.ppermute(acc, axis, perm)
        acc = received + relative[(t + 2) % count]
    return acc


def ring_position(axis, ring):
    position = jnp.zeros((), jnp.int32)
    index = lax.axis_index(axis)
    for q, s in enumerate(ring):
        position = jnp.where(index == s, q, position)
    return position


def ring_reduce_scatter_sliced(select_block, axis, ring, forward_dir=True, wire_dtype=jnp.bfloat16):
    count = len(ring)
    forward, backward = ring_perms(ring)
    perm = forward if forward_dir else backward
    sign = 1 if forward_dir else -1
    position = ring_position(axis, ring)

    def block_at(offset):
        target = (position + count - sign * (offset % count)) % count
        index = jnp.zeros((), jnp.int32)
        for q, s in enumerate(ring):
            index = jnp.where(target == q, s, index)
        return select_block(index)

    acc = block_at(1).astype(wire_dtype)
    for t in range(count - 1):
        received = lax.ppermute(acc, axis, perm).astype(jnp.float32)
        acc = received + block_at(t + 2)
        if t < count - 2:
            acc = acc.astype(wire_dtype)
    return acc


def body(ring, queries, key_rows, value_rows, trunk_state, skip_input, norm_gain, conv_weight, cotangent):
    score_scale = DK ** (-0.5)
    local_tokens = queries.shape[1]
    positions = 2 * local_tokens
    half_kernel = KW // 2
    query_heads = queries[0].reshape(local_tokens, H, DK)
    key_value_blocks = ring_gather(jnp.concatenate([key_rows[0], value_rows[0]], axis=1), ring)
    gathered = jnp.concatenate(key_value_blocks, axis=0)
    all_keys = gathered[:, : H * DK].reshape(-1, H, DK)
    all_values = gathered[:, H * DK :].reshape(-1, H, DV)
    scores = (
        jnp.einsum("ihd,jhd->hij", query_heads, all_keys, preferred_element_type=jnp.float32)
        * score_scale
    )
    row_peak = jnp.max(scores, axis=2, keepdims=True)
    row_total = jnp.sum(jnp.exp(scores - row_peak), axis=2, keepdims=True)
    logsum = row_peak + jnp.log(row_total)
    softmax = jnp.exp(scores - logsum)
    rounded = softmax.astype(jnp.bfloat16)
    attended = jnp.einsum(
        "hij,jhd->ihd", rounded, all_values, preferred_element_type=jnp.float32
    ).astype(jnp.bfloat16)
    upsample = (
        jnp.arange(positions, dtype=jnp.int32)[:, None] // 2
        == jnp.arange(local_tokens, dtype=jnp.int32)[None, :]
    ).astype(jnp.bfloat16)
    hidden_up = jnp.dot(
        upsample, trunk_state[0], preferred_element_type=jnp.float32
    ) + jnp.dot(
        upsample, attended.reshape(local_tokens, H * DV), preferred_element_type=jnp.float32
    )
    merged = hidden_up + skip_input[0].astype(jnp.float32)
    inverse = lax.rsqrt(jnp.mean(merged * merged, axis=1, keepdims=True) + 1e-06)
    channel_gain = norm_gain.astype(jnp.float32)
    normed = (merged * inverse * channel_gain).astype(jnp.bfloat16)
    padded = extended(normed, (("seq", 0),), half_kernel)
    columns = window_rows(padded, KW, positions)
    preact = jnp.dot(columns, conv_weight, preferred_element_type=jnp.float32)
    activated, derivative = gelu_parts(preact)
    decoded = activated.astype(jnp.bfloat16)
    grad_pre = (cotangent[0].astype(jnp.float32) * derivative).astype(jnp.bfloat16)
    grad_padded = extended(grad_pre, (("seq", 0),), half_kernel)
    norm_scale = (lax.axis_size("dp") * positions * lax.axis_size("seq")) ** (-0.5)
    seq_count, dp_count = lax.axis_size("seq"), lax.axis_size("dp")
    rows_per = KW * C // (seq_count * dp_count)
    half_co = CO // 2
    if dp_count == 2:
        partner = [(0, 1), (1, 0)]
        both_padded = jnp.stack([padded, lax.ppermute(padded, "dp", partner)])
        both_grad = jnp.stack([grad_pre, lax.ppermute(grad_pre, "dp", partner)])
        full_weight = (
            jnp.concatenate(
                [
                    jnp.einsum(
                        "spc,spo->co",
                        both_padded[:, offset : offset + positions],
                        both_grad,
                        preferred_element_type=jnp.float32,
                    )
                    for offset in range(KW)
                ],
                axis=0,
            )
            * norm_scale
        ).reshape(seq_count, dp_count, rows_per, CO)
        dp_index = lax.axis_index("dp")

        def weight_block(column, width):
            return lambda index: lax.dynamic_slice(
                full_weight, (index, dp_index, 0, column), (1, 1, rows_per, width)
            ).reshape(rows_per, width)

        grad_weight = jnp.concatenate(
            [
                ring_reduce_scatter_sliced(weight_block(0, half_co), "seq", ring, True),
                ring_reduce_scatter_sliced(
                    weight_block(half_co, CO - half_co), "seq", ring, False
                ),
            ],
            axis=1,
        )
    else:
        weight_part = (
            lax.dot_general(
                columns, grad_pre, (((0,), (0,)), ((), ())), preferred_element_type=jnp.float32
            )
            * norm_scale
        )
        weight_blocks_all = weight_part.reshape(seq_count, dp_count, -1, CO)
        dp_summed = ring_reduce_scatter(
            jnp.swapaxes(weight_blocks_all, 0, 1), "dp", list(range(dp_count))
        )
        grad_weight = jnp.concatenate(
            [
                ring_reduce_scatter(dp_summed[:, :, :half_co], "seq", ring, True),
                ring_reduce_scatter(dp_summed[:, :, half_co:], "seq", ring, False),
            ],
            axis=1,
        )
    stacked = jnp.stack(
        [
            grad_padded[2 * half_kernel - offset : 2 * half_kernel - offset + positions]
            for offset in range(KW)
        ],
        axis=1,
    )
    weight_blocks = conv_weight.reshape(KW, C, CO)
    grad_normed = jnp.einsum(
        "pko,kco->pc", stacked, weight_blocks, preferred_element_type=jnp.float32
    )
    scaled_grad = grad_normed * channel_gain
    grad_merged = inverse * scaled_grad - merged * inverse**3 * jnp.mean(
        scaled_grad * merged, axis=1, keepdims=True
    )
    grad_skip = grad_merged.astype(jnp.bfloat16)
    grad_trunk = jnp.dot(
        upsample.T.astype(jnp.float32),
        grad_merged,
        precision=lax.Precision.HIGHEST,
        preferred_element_type=jnp.float32,
    ).astype(jnp.bfloat16)
    grad_heads = grad_trunk.reshape(local_tokens, H, DV)
    row_delta = jnp.sum(grad_heads.astype(jnp.float32) * attended.astype(jnp.float32), axis=2)
    value_grad = jnp.einsum(
        "ihd,jhd->hij", grad_heads, all_values, preferred_element_type=jnp.float32
    )
    slopes = (softmax * (value_grad - row_delta.T[:, :, None])).astype(jnp.bfloat16)
    grad_queries = (
        jnp.einsum("hij,jhd->ihd", slopes, all_keys, preferred_element_type=jnp.float32)
        * score_scale
    ).astype(jnp.bfloat16)
    key_part = (
        jnp.einsum("hij,ihd->jhd", slopes, query_heads, preferred_element_type=jnp.float32)
        * score_scale
    )
    value_part = jnp.einsum("hij,ihd->jhd", rounded, grad_heads, preferred_element_type=jnp.float32)
    terms = jnp.concatenate(
        [
            key_part.reshape(-1, H * DK),
            value_part.reshape(-1, H * DV),
        ],
        axis=1,
    ).astype(jnp.bfloat16)
    term_blocks = [
        terms[m * local_tokens : (m + 1) * local_tokens] for m in range(lax.axis_size("seq"))
    ]
    summed = ring_scatter_back(term_blocks, ring)
    grad_keys = summed[:, : H * DK].astype(jnp.bfloat16)
    grad_values = summed[:, H * DK :].astype(jnp.bfloat16)
    return (
        decoded[None],
        grad_queries.reshape(local_tokens, H * DK)[None],
        grad_keys[None],
        grad_values[None],
        grad_trunk[None],
        grad_skip[None],
        grad_weight,
    )


def solution(mesh):
    return jax.shard_map(
        functools.partial(body, ring_order(mesh)),
        mesh=mesh,
        in_specs=(
            P(("group", "dp"), "seq", None),
            P(("group", "dp"), "seq", None),
            P(("group", "dp"), "seq", None),
            P(("group", "dp"), "seq", None),
            P(("group", "dp"), "seq", None),
            P(),
            P(),
            P(("group", "dp"), "seq", None),
        ),
        out_specs=(
            P(("group", "dp"), "seq", None),
            P(("group", "dp"), "seq", None),
            P(("group", "dp"), "seq", None),
            P(("group", "dp"), "seq", None),
            P(("group", "dp"), "seq", None),
            P(("group", "dp"), "seq", None),
            P(("group", "seq", "dp"), None),
        ),
        check_vma=False,
    )
```

```python
import functools
import math

import jax
import jax.numpy as jnp
from jax import lax
from jax.sharding import PartitionSpec as P

H = 4
DK = 128
DV = 192
C = 768
CO = 384
KW = 5


def extended(array, sides, width):
    for axis, dim in sides:
        count, length = (lax.axis_size(axis), array.shape[dim])
        up = [(i, (i + 1) % count) for i in range(count - 1)]
        down = [(j, i) for i, j in up]
        last = lax.slice_in_dim(array, length - width, length, axis=dim)
        initial = lax.slice_in_dim(array, 0, width, axis=dim)
        before = lax.ppermute(last, axis, up)
        after = lax.ppermute(initial, axis, down)
        array = jnp.concatenate([before, array, after], axis=dim)
    return array


def gelu_parts(preact):
    cdf_value = 0.5 * (1.0 + jax.scipy.special.erf(preact * (1.0 / math.sqrt(2.0))))
    density = jnp.exp(-0.5 * preact * preact) * (1.0 / math.sqrt(2.0 * math.pi))
    return (preact * cdf_value, cdf_value + preact * density)


def window_rows(padded, kernel, row_count):
    return jnp.concatenate(
        [padded[offset : offset + row_count] for offset in range(kernel)], axis=1
    )


def ring_order(mesh):
    count = mesh.shape["seq"]
    try:
        row = mesh.devices.reshape(mesh.shape["group"], count, -1)[0, :, 0]
        coords = [tuple(device.coords) for device in row]
    except (AttributeError, TypeError):
        return list(range(count))
    varying = [d for d in range(3) if len({c[d] for c in coords}) > 1]
    if len(varying) == 2:
        for minor, major in (varying, varying[::-1]):
            if len({c[minor] for c in coords}) == 2:
                low = min(c[minor] for c in coords)
                first = sorted((c[major], s) for s, c in enumerate(coords) if c[minor] == low)
                second = sorted((c[major], s) for s, c in enumerate(coords) if c[minor] != low)
                return [s for _, s in first] + [s for _, s in second[::-1]]
    return list(range(count))


def ring_perms(ring):
    count = len(ring)
    forward = [(ring[q], ring[(q + 1) % count]) for q in range(count)]
    backward = [(ring[q], ring[(q - 1) % count]) for q in range(count)]
    return forward, backward


def ring_gather(block, ring):
    count = len(ring)
    forward, backward = ring_perms(ring)
    full_steps = (count - 1) // 2
    split = count % 2 == 0
    half = block.shape[1] // 2
    lefts, rights = [], []
    current = block
    for _ in range(full_steps):
        current = lax.ppermute(current, "seq", forward)
        lefts.append(current)
    if split:
        left_half = lax.ppermute(current[:, :half], "seq", forward)
    current = block
    for _ in range(full_steps):
        current = lax.ppermute(current, "seq", backward)
        rights.append(current)
    if split:
        right_half = lax.ppermute(current[:, half:], "seq", backward)
    opposite = [jnp.concatenate([left_half, right_half], axis=1)] if split else []
    return [block] + lefts + rights + opposite


def add_part(term, received, side):
    if received.shape == term.shape:
        return term + received
    half = term.shape[1] - received.shape[1] if side else received.shape[1]
    if side:
        return jnp.concatenate([term[:, :half], term[:, half:] + received], axis=1)
    return jnp.concatenate([term[:, :half] + received, term[:, half:]], axis=1)


def ring_scatter_back(blocks, ring):
    count = len(ring)
    forward, backward = ring_perms(ring)
    full_steps = (count - 1) // 2
    split = count % 2 == 0
    own = blocks[0].astype(jnp.float32)
    lefts = blocks[1 : 1 + full_steps]
    rights = blocks[1 + full_steps : 1 + 2 * full_steps]
    total = own
    for side, chain, perm in ((0, lefts, backward), (1, rights, forward)):
        if split:
            half = blocks[-1].shape[1] // 2
            acc = blocks[-1][:, half:] if side else blocks[-1][:, :half]
            top = full_steps + 1
        elif full_steps:
            acc = chain[-1]
            top = full_steps
        else:
            continue
        for t in range(top, 0, -1):
            received = lax.ppermute(acc, "seq", perm).astype(jnp.float32)
            if t == 1:
                total = add_part(total, received, side)
            else:
                acc = add_part(chain[t - 2].astype(jnp.float32), received, side).astype(
                    jnp.bfloat16
                )
    return total


def ring_reduce_scatter(blocks, axis, ring, forward_dir=True):
    count = len(ring)
    if count == 1:
        return blocks[0]
    forward, backward = ring_perms(ring)
    perm = forward if forward_dir else backward
    sign = 1 if forward_dir else -1
    position = jnp.zeros((), jnp.int32)
    index = lax.axis_index(axis)
    for q, s in enumerate(ring):
        position = jnp.where(index == s, q, position)
    offsets = (position + count - sign * jnp.arange(count, dtype=jnp.int32)) % count
    order = jnp.zeros((count,), jnp.int32)
    for q, s in enumerate(ring):
        order = jnp.where(offsets == q, s, order)
    relative = jnp.take(blocks, order, axis=0)
    acc = relative[1]
    for t in range(count - 1):
        received = lax.ppermute(acc, axis, perm)
        acc = received + relative[(t + 2) % count]
    return acc


def ring_position(axis, ring):
    position = jnp.zeros((), jnp.int32)
    index = lax.axis_index(axis)
    for q, s in enumerate(ring):
        position = jnp.where(index == s, q, position)
    return position


def ring_reduce_scatter_sliced(select_block, axis, ring, forward_dir=True, wire_dtype=jnp.bfloat16):
    count = len(ring)
    forward, backward = ring_perms(ring)
    perm = forward if forward_dir else backward
    sign = 1 if forward_dir else -1
    position = ring_position(axis, ring)

    def block_at(offset):
        target = (position + count - sign * (offset % count)) % count
        index = jnp.zeros((), jnp.int32)
        for q, s in enumerate(ring):
            index = jnp.where(target == q, s, index)
        return select_block(index)

    acc = block_at(1).astype(wire_dtype)
    for t in range(count - 1):
        received = lax.ppermute(acc, axis, perm).astype(jnp.float32)
        acc = received + block_at(t + 2)
        if t < count - 2:
            acc = acc.astype(wire_dtype)
    return acc


def direct_reduce_scatter(select_block, axis, count):
    index = lax.axis_index(axis)
    total = select_block(index).astype(jnp.float32)
    for shift in range(1, count):
        perm = [(s, (s + shift) % count) for s in range(count)]
        sent = select_block((index + shift) % count).astype(jnp.bfloat16)
        total = total + lax.ppermute(sent, axis, perm).astype(jnp.float32)
    return total


def body(ring, queries, key_rows, value_rows, trunk_state, skip_input, norm_gain, conv_weight, cotangent):
    score_scale = DK ** (-0.5)
    local_tokens = queries.shape[1]
    positions = 2 * local_tokens
    half_kernel = KW // 2
    query_heads = queries[0].reshape(local_tokens, H, DK)
    key_value_blocks = ring_gather(jnp.concatenate([key_rows[0], value_rows[0]], axis=1), ring)
    gathered = jnp.concatenate(key_value_blocks, axis=0)
    all_keys = gathered[:, : H * DK].reshape(-1, H, DK)
    all_values = gathered[:, H * DK :].reshape(-1, H, DV)
    scores = (
        jnp.einsum("ihd,jhd->hij", query_heads, all_keys, preferred_element_type=jnp.float32)
        * score_scale
    )
    row_peak = jnp.max(scores, axis=2, keepdims=True)
    row_total = jnp.sum(jnp.exp(scores - row_peak), axis=2, keepdims=True)
    logsum = row_peak + jnp.log(row_total)
    softmax = jnp.exp(scores - logsum)
    rounded = softmax.astype(jnp.bfloat16)
    attended = jnp.einsum(
        "hij,jhd->ihd", rounded, all_values, preferred_element_type=jnp.float32
    ).astype(jnp.bfloat16)
    upsample = (
        jnp.arange(positions, dtype=jnp.int32)[:, None] // 2
        == jnp.arange(local_tokens, dtype=jnp.int32)[None, :]
    ).astype(jnp.bfloat16)
    hidden_up = jnp.dot(
        upsample, trunk_state[0], preferred_element_type=jnp.float32
    ) + jnp.dot(
        upsample, attended.reshape(local_tokens, H * DV), preferred_element_type=jnp.float32
    )
    merged = hidden_up + skip_input[0].astype(jnp.float32)
    inverse = lax.rsqrt(jnp.mean(merged * merged, axis=1, keepdims=True) + 1e-06)
    channel_gain = norm_gain.astype(jnp.float32)
    normed = (merged * inverse * channel_gain).astype(jnp.bfloat16)
    padded = extended(normed, (("seq", 0),), half_kernel)
    columns = window_rows(padded, KW, positions)
    preact = jnp.dot(columns, conv_weight, preferred_element_type=jnp.float32)
    activated, derivative = gelu_parts(preact)
    decoded = activated.astype(jnp.bfloat16)
    grad_pre = (cotangent[0].astype(jnp.float32) * derivative).astype(jnp.bfloat16)
    grad_padded = extended(grad_pre, (("seq", 0),), half_kernel)
    norm_scale = (lax.axis_size("dp") * positions * lax.axis_size("seq")) ** (-0.5)
    seq_count, dp_count = lax.axis_size("seq"), lax.axis_size("dp")
    rows_per = KW * C // (seq_count * dp_count)
    half_co = CO // 2
    if dp_count == 2:
        partner = [(0, 1), (1, 0)]
        both_padded = jnp.stack([padded, lax.ppermute(padded, "dp", partner)])
        both_grad = jnp.stack([grad_pre, lax.ppermute(grad_pre, "dp", partner)])
        full_weight = (
            jnp.concatenate(
                [
                    jnp.einsum(
                        "spc,spo->co",
                        both_padded[:, offset : offset + positions],
                        both_grad,
                        preferred_element_type=jnp.float32,
                    )
                    for offset in range(KW)
                ],
                axis=0,
            )
            * norm_scale
        ).reshape(seq_count, dp_count, rows_per, CO)
        dp_index = lax.axis_index("dp")

        def weight_block(column, width):
            return lambda index: lax.dynamic_slice(
                full_weight, (index, dp_index, 0, column), (1, 1, rows_per, width)
            ).reshape(rows_per, width)

        grad_weight = direct_reduce_scatter(weight_block(0, CO), "seq", seq_count)
    else:
        weight_part = (
            lax.dot_general(
                columns, grad_pre, (((0,), (0,)), ((), ())), preferred_element_type=jnp.float32
            )
            * norm_scale
        )
        weight_blocks_all = weight_part.reshape(seq_count, dp_count, -1, CO)
        dp_summed = ring_reduce_scatter(
            jnp.swapaxes(weight_blocks_all, 0, 1), "dp", list(range(dp_count))
        )
        grad_weight = jnp.concatenate(
            [
                ring_reduce_scatter(dp_summed[:, :, :half_co], "seq", ring, True),
                ring_reduce_scatter(dp_summed[:, :, half_co:], "seq", ring, False),
            ],
            axis=1,
        )
    stacked = jnp.stack(
        [
            grad_padded[2 * half_kernel - offset : 2 * half_kernel - offset + positions]
            for offset in range(KW)
        ],
        axis=1,
    )
    weight_blocks = conv_weight.reshape(KW, C, CO)
    grad_normed = jnp.einsum(
        "pko,kco->pc", stacked, weight_blocks, preferred_element_type=jnp.float32
    )
    scaled_grad = grad_normed * channel_gain
    grad_merged = inverse * scaled_grad - merged * inverse**3 * jnp.mean(
        scaled_grad * merged, axis=1, keepdims=True
    )
    grad_skip = grad_merged.astype(jnp.bfloat16)
    grad_trunk = jnp.dot(
        upsample.T.astype(jnp.float32),
        grad_merged,
        precision=lax.Precision.HIGHEST,
        preferred_element_type=jnp.float32,
    ).astype(jnp.bfloat16)
    grad_heads = grad_trunk.reshape(local_tokens, H, DV)
    row_delta = jnp.sum(grad_heads.astype(jnp.float32) * attended.astype(jnp.float32), axis=2)
    value_grad = jnp.einsum(
        "ihd,jhd->hij", grad_heads, all_values, preferred_element_type=jnp.float32
    )
    slopes = (softmax * (value_grad - row_delta.T[:, :, None])).astype(jnp.bfloat16)
    grad_queries = (
        jnp.einsum("hij,jhd->ihd", slopes, all_keys, preferred_element_type=jnp.float32)
        * score_scale
    ).astype(jnp.bfloat16)
    key_part = (
        jnp.einsum("hij,ihd->jhd", slopes, query_heads, preferred_element_type=jnp.float32)
        * score_scale
    )
    value_part = jnp.einsum("hij,ihd->jhd", rounded, grad_heads, preferred_element_type=jnp.float32)
    terms = jnp.concatenate(
        [
            key_part.reshape(-1, H * DK),
            value_part.reshape(-1, H * DV),
        ],
        axis=1,
    ).astype(jnp.bfloat16)
    term_blocks = [
        terms[m * local_tokens : (m + 1) * local_tokens] for m in range(lax.axis_size("seq"))
    ]
    summed = ring_scatter_back(term_blocks, ring)
    grad_keys = summed[:, : H * DK].astype(jnp.bfloat16)
    grad_values = summed[:, H * DK :].astype(jnp.bfloat16)
    return (
        decoded[None],
        grad_queries.reshape(local_tokens, H * DK)[None],
        grad_keys[None],
        grad_values[None],
        grad_trunk[None],
        grad_skip[None],
        grad_weight,
    )


def solution(mesh):
    return jax.shard_map(
        functools.partial(body, ring_order(mesh)),
        mesh=mesh,
        in_specs=(
            P(("group", "dp"), "seq", None),
            P(("group", "dp"), "seq", None),
            P(("group", "dp"), "seq", None),
            P(("group", "dp"), "seq", None),
            P(("group", "dp"), "seq", None),
            P(),
            P(),
            P(("group", "dp"), "seq", None),
        ),
        out_specs=(
            P(("group", "dp"), "seq", None),
            P(("group", "dp"), "seq", None),
            P(("group", "dp"), "seq", None),
            P(("group", "dp"), "seq", None),
            P(("group", "dp"), "seq", None),
            P(("group", "dp"), "seq", None),
            P(("group", "seq", "dp"), None),
        ),
        check_vma=False,
    )
```

```python
import functools
import math

import jax
import jax.numpy as jnp
from jax import lax
from jax.sharding import PartitionSpec as P

H = 4
DK = 128
DV = 192
C = 768
CO = 384
KW = 5


def extended(array, sides, width):
    for axis, dim in sides:
        count, length = (lax.axis_size(axis), array.shape[dim])
        up = [(i, (i + 1) % count) for i in range(count - 1)]
        down = [(j, i) for i, j in up]
        last = lax.slice_in_dim(array, length - width, length, axis=dim)
        initial = lax.slice_in_dim(array, 0, width, axis=dim)
        before = lax.ppermute(last, axis, up)
        after = lax.ppermute(initial, axis, down)
        array = jnp.concatenate([before, array, after], axis=dim)
    return array


def gelu_parts(preact):
    cdf_value = 0.5 * (1.0 + jax.scipy.special.erf(preact * (1.0 / math.sqrt(2.0))))
    density = jnp.exp(-0.5 * preact * preact) * (1.0 / math.sqrt(2.0 * math.pi))
    return (preact * cdf_value, cdf_value + preact * density)


def window_rows(padded, kernel, row_count):
    return jnp.concatenate(
        [padded[offset : offset + row_count] for offset in range(kernel)], axis=1
    )


def ring_order(mesh):
    count = mesh.shape["seq"]
    try:
        row = mesh.devices.reshape(mesh.shape["group"], count, -1)[0, :, 0]
        coords = [tuple(device.coords) for device in row]
    except (AttributeError, TypeError):
        return list(range(count))
    varying = [d for d in range(3) if len({c[d] for c in coords}) > 1]
    if len(varying) == 2:
        for minor, major in (varying, varying[::-1]):
            if len({c[minor] for c in coords}) == 2:
                low = min(c[minor] for c in coords)
                first = sorted((c[major], s) for s, c in enumerate(coords) if c[minor] == low)
                second = sorted((c[major], s) for s, c in enumerate(coords) if c[minor] != low)
                return [s for _, s in first] + [s for _, s in second[::-1]]
    return list(range(count))


def ring_perms(ring):
    count = len(ring)
    forward = [(ring[q], ring[(q + 1) % count]) for q in range(count)]
    backward = [(ring[q], ring[(q - 1) % count]) for q in range(count)]
    return forward, backward


def ring_gather(block, ring):
    count = len(ring)
    forward, backward = ring_perms(ring)
    full_steps = (count - 1) // 2
    split = count % 2 == 0
    half = block.shape[1] // 2
    lefts, rights = [], []
    current = block
    for _ in range(full_steps):
        current = lax.ppermute(current, "seq", forward)
        lefts.append(current)
    if split:
        left_half = lax.ppermute(current[:, :half], "seq", forward)
    current = block
    for _ in range(full_steps):
        current = lax.ppermute(current, "seq", backward)
        rights.append(current)
    if split:
        right_half = lax.ppermute(current[:, half:], "seq", backward)
    opposite = [jnp.concatenate([left_half, right_half], axis=1)] if split else []
    return [block] + lefts + rights + opposite


def add_part(term, received, side):
    if received.shape == term.shape:
        return term + received
    half = term.shape[1] - received.shape[1] if side else received.shape[1]
    if side:
        return jnp.concatenate([term[:, :half], term[:, half:] + received], axis=1)
    return jnp.concatenate([term[:, :half] + received, term[:, half:]], axis=1)


def ring_scatter_back(blocks, ring):
    count = len(ring)
    forward, backward = ring_perms(ring)
    full_steps = (count - 1) // 2
    split = count % 2 == 0
    own = blocks[0].astype(jnp.float32)
    lefts = blocks[1 : 1 + full_steps]
    rights = blocks[1 + full_steps : 1 + 2 * full_steps]
    total = own
    for side, chain, perm in ((0, lefts, backward), (1, rights, forward)):
        if split:
            half = blocks[-1].shape[1] // 2
            acc = blocks[-1][:, half:] if side else blocks[-1][:, :half]
            top = full_steps + 1
        elif full_steps:
            acc = chain[-1]
            top = full_steps
        else:
            continue
        for t in range(top, 0, -1):
            received = lax.ppermute(acc, "seq", perm).astype(jnp.float32)
            if t == 1:
                total = add_part(total, received, side)
            else:
                acc = add_part(chain[t - 2].astype(jnp.float32), received, side).astype(
                    jnp.bfloat16
                )
    return total


def ring_reduce_scatter(blocks, axis, ring, forward_dir=True):
    count = len(ring)
    if count == 1:
        return blocks[0]
    forward, backward = ring_perms(ring)
    perm = forward if forward_dir else backward
    sign = 1 if forward_dir else -1
    position = jnp.zeros((), jnp.int32)
    index = lax.axis_index(axis)
    for q, s in enumerate(ring):
        position = jnp.where(index == s, q, position)
    offsets = (position + count - sign * jnp.arange(count, dtype=jnp.int32)) % count
    order = jnp.zeros((count,), jnp.int32)
    for q, s in enumerate(ring):
        order = jnp.where(offsets == q, s, order)
    relative = jnp.take(blocks, order, axis=0)
    acc = relative[1]
    for t in range(count - 1):
        received = lax.ppermute(acc, axis, perm)
        acc = received + relative[(t + 2) % count]
    return acc


def ring_position(axis, ring):
    position = jnp.zeros((), jnp.int32)
    index = lax.axis_index(axis)
    for q, s in enumerate(ring):
        position = jnp.where(index == s, q, position)
    return position


def ring_reduce_scatter_sliced(select_block, axis, ring, forward_dir=True, wire_dtype=jnp.bfloat16):
    count = len(ring)
    forward, backward = ring_perms(ring)
    perm = forward if forward_dir else backward
    sign = 1 if forward_dir else -1
    position = ring_position(axis, ring)

    def block_at(offset):
        target = (position + count - sign * (offset % count)) % count
        index = jnp.zeros((), jnp.int32)
        for q, s in enumerate(ring):
            index = jnp.where(target == q, s, index)
        return select_block(index)

    acc = block_at(1).astype(wire_dtype)
    for t in range(count - 1):
        received = lax.ppermute(acc, axis, perm).astype(jnp.float32)
        acc = received + block_at(t + 2)
        if t < count - 2:
            acc = acc.astype(wire_dtype)
    return acc


def body(ring, queries, key_rows, value_rows, trunk_state, skip_input, norm_gain, conv_weight, cotangent):
    score_scale = DK ** (-0.5)
    local_tokens = queries.shape[1]
    positions = 2 * local_tokens
    half_kernel = KW // 2
    query_heads = queries[0].reshape(local_tokens, H, DK)
    key_value_blocks = ring_gather(jnp.concatenate([key_rows[0], value_rows[0]], axis=1), ring)
    gathered = jnp.concatenate(key_value_blocks, axis=0)
    all_keys = gathered[:, : H * DK].reshape(-1, H, DK)
    all_values = gathered[:, H * DK :].reshape(-1, H, DV)
    scores = (
        jnp.einsum("ihd,jhd->hij", query_heads, all_keys, preferred_element_type=jnp.float32)
        * score_scale
    )
    row_peak = jnp.max(scores, axis=2, keepdims=True)
    row_total = jnp.sum(jnp.exp(scores - row_peak), axis=2, keepdims=True)
    logsum = row_peak + jnp.log(row_total)
    softmax = jnp.exp(scores - logsum)
    rounded = softmax.astype(jnp.bfloat16)
    attended = jnp.einsum(
        "hij,jhd->ihd", rounded, all_values, preferred_element_type=jnp.float32
    ).astype(jnp.bfloat16)
    upsample = (
        jnp.arange(positions, dtype=jnp.int32)[:, None] // 2
        == jnp.arange(local_tokens, dtype=jnp.int32)[None, :]
    ).astype(jnp.bfloat16)
    hidden_up = jnp.dot(
        upsample, trunk_state[0], preferred_element_type=jnp.float32
    ) + jnp.dot(
        upsample, attended.reshape(local_tokens, H * DV), preferred_element_type=jnp.float32
    )
    merged = hidden_up + skip_input[0].astype(jnp.float32)
    inverse = lax.rsqrt(jnp.mean(merged * merged, axis=1, keepdims=True) + 1e-06)
    channel_gain = norm_gain.astype(jnp.float32)
    normed = (merged * inverse * channel_gain).astype(jnp.bfloat16)
    padded = extended(normed, (("seq", 0),), half_kernel)
    columns = window_rows(padded, KW, positions)
    preact = jnp.dot(columns, conv_weight, preferred_element_type=jnp.float32)
    activated, derivative = gelu_parts(preact)
    decoded = activated.astype(jnp.bfloat16)
    grad_pre = (cotangent[0].astype(jnp.float32) * derivative).astype(jnp.bfloat16)
    grad_padded = extended(grad_pre, (("seq", 0),), half_kernel)
    norm_scale = (lax.axis_size("dp") * positions * lax.axis_size("seq")) ** (-0.5)
    seq_count, dp_count = lax.axis_size("seq"), lax.axis_size("dp")
    rows_per = KW * C // (seq_count * dp_count)
    half_co = CO // 2
    if dp_count == 2:
        partner = [(0, 1), (1, 0)]
        both_padded = jnp.stack([padded, lax.ppermute(padded, "dp", partner)])
        both_grad = jnp.stack([grad_pre, lax.ppermute(grad_pre, "dp", partner)])
        full_weight = (
            jnp.concatenate(
                [
                    jnp.einsum(
                        "spc,spo->co",
                        both_padded[:, offset : offset + positions],
                        both_grad,
                        preferred_element_type=jnp.float32,
                    )
                    for offset in range(KW)
                ],
                axis=0,
            )
            * norm_scale
        ).reshape(seq_count, dp_count, rows_per, CO)
        full_weight, grad_padded = lax.optimization_barrier((full_weight, grad_padded))
        dp_index = lax.axis_index("dp")

        def weight_block(column, width):
            return lambda index: lax.dynamic_slice(
                full_weight, (index, dp_index, 0, column), (1, 1, rows_per, width)
            ).reshape(rows_per, width)

        grad_weight = jnp.concatenate(
            [
                ring_reduce_scatter_sliced(weight_block(0, half_co), "seq", ring, True),
                ring_reduce_scatter_sliced(
                    weight_block(half_co, CO - half_co), "seq", ring, False
                ),
            ],
            axis=1,
        )
    else:
        weight_part = (
            lax.dot_general(
                columns, grad_pre, (((0,), (0,)), ((), ())), preferred_element_type=jnp.float32
            )
            * norm_scale
        )
        weight_blocks_all = weight_part.reshape(seq_count, dp_count, -1, CO)
        dp_summed = ring_reduce_scatter(
            jnp.swapaxes(weight_blocks_all, 0, 1), "dp", list(range(dp_count))
        )
        grad_weight = jnp.concatenate(
            [
                ring_reduce_scatter(dp_summed[:, :, :half_co], "seq", ring, True),
                ring_reduce_scatter(dp_summed[:, :, half_co:], "seq", ring, False),
            ],
            axis=1,
        )
    stacked = jnp.stack(
        [
            grad_padded[2 * half_kernel - offset : 2 * half_kernel - offset + positions]
            for offset in range(KW)
        ],
        axis=1,
    )
    weight_blocks = conv_weight.reshape(KW, C, CO)
    grad_normed = jnp.einsum(
        "pko,kco->pc", stacked, weight_blocks, preferred_element_type=jnp.float32
    )
    scaled_grad = grad_normed * channel_gain
    grad_merged = inverse * scaled_grad - merged * inverse**3 * jnp.mean(
        scaled_grad * merged, axis=1, keepdims=True
    )
    grad_skip = grad_merged.astype(jnp.bfloat16)
    grad_trunk = jnp.dot(
        upsample.T.astype(jnp.float32),
        grad_merged,
        precision=lax.Precision.HIGHEST,
        preferred_element_type=jnp.float32,
    ).astype(jnp.bfloat16)
    grad_heads = grad_trunk.reshape(local_tokens, H, DV)
    row_delta = jnp.sum(grad_heads.astype(jnp.float32) * attended.astype(jnp.float32), axis=2)
    value_grad = jnp.einsum(
        "ihd,jhd->hij", grad_heads, all_values, preferred_element_type=jnp.float32
    )
    slopes = (softmax * (value_grad - row_delta.T[:, :, None])).astype(jnp.bfloat16)
    grad_queries = (
        jnp.einsum("hij,jhd->ihd", slopes, all_keys, preferred_element_type=jnp.float32)
        * score_scale
    ).astype(jnp.bfloat16)
    key_part = (
        jnp.einsum("hij,ihd->jhd", slopes, query_heads, preferred_element_type=jnp.float32)
        * score_scale
    )
    value_part = jnp.einsum("hij,ihd->jhd", rounded, grad_heads, preferred_element_type=jnp.float32)
    terms = jnp.concatenate(
        [
            key_part.reshape(-1, H * DK),
            value_part.reshape(-1, H * DV),
        ],
        axis=1,
    ).astype(jnp.bfloat16)
    term_blocks = [
        terms[m * local_tokens : (m + 1) * local_tokens] for m in range(lax.axis_size("seq"))
    ]
    summed = ring_scatter_back(term_blocks, ring)
    grad_keys = summed[:, : H * DK].astype(jnp.bfloat16)
    grad_values = summed[:, H * DK :].astype(jnp.bfloat16)
    return (
        decoded[None],
        grad_queries.reshape(local_tokens, H * DK)[None],
        grad_keys[None],
        grad_values[None],
        grad_trunk[None],
        grad_skip[None],
        grad_weight,
    )


def solution(mesh):
    return jax.shard_map(
        functools.partial(body, ring_order(mesh)),
        mesh=mesh,
        in_specs=(
            P(("group", "dp"), "seq", None),
            P(("group", "dp"), "seq", None),
            P(("group", "dp"), "seq", None),
            P(("group", "dp"), "seq", None),
            P(("group", "dp"), "seq", None),
            P(),
            P(),
            P(("group", "dp"), "seq", None),
        ),
        out_specs=(
            P(("group", "dp"), "seq", None),
            P(("group", "dp"), "seq", None),
            P(("group", "dp"), "seq", None),
            P(("group", "dp"), "seq", None),
            P(("group", "dp"), "seq", None),
            P(("group", "dp"), "seq", None),
            P(("group", "seq", "dp"), None),
        ),
        check_vma=False,
    )
```

```python
import functools
import math

import jax
import jax.numpy as jnp
from jax import lax
from jax.sharding import PartitionSpec as P

H = 4
DK = 128
DV = 192
C = 768
CO = 384
KW = 5


def extended(array, sides, width):
    for axis, dim in sides:
        count, length = (lax.axis_size(axis), array.shape[dim])
        up = [(i, (i + 1) % count) for i in range(count - 1)]
        down = [(j, i) for i, j in up]
        last = lax.slice_in_dim(array, length - width, length, axis=dim)
        initial = lax.slice_in_dim(array, 0, width, axis=dim)
        before = lax.ppermute(last, axis, up)
        after = lax.ppermute(initial, axis, down)
        array = jnp.concatenate([before, array, after], axis=dim)
    return array


def gelu_parts(preact):
    cdf_value = 0.5 * (1.0 + jax.scipy.special.erf(preact * (1.0 / math.sqrt(2.0))))
    density = jnp.exp(-0.5 * preact * preact) * (1.0 / math.sqrt(2.0 * math.pi))
    return (preact * cdf_value, cdf_value + preact * density)


def window_rows(padded, kernel, row_count):
    return jnp.concatenate(
        [padded[offset : offset + row_count] for offset in range(kernel)], axis=1
    )


def ring_order(mesh):
    count = mesh.shape["seq"]
    try:
        row = mesh.devices.reshape(mesh.shape["group"], count, -1)[0, :, 0]
        coords = [tuple(device.coords) for device in row]
    except (AttributeError, TypeError):
        return list(range(count))
    varying = [d for d in range(3) if len({c[d] for c in coords}) > 1]
    if len(varying) == 2:
        for minor, major in (varying, varying[::-1]):
            if len({c[minor] for c in coords}) == 2:
                low = min(c[minor] for c in coords)
                first = sorted((c[major], s) for s, c in enumerate(coords) if c[minor] == low)
                second = sorted((c[major], s) for s, c in enumerate(coords) if c[minor] != low)
                return [s for _, s in first] + [s for _, s in second[::-1]]
    return list(range(count))


def ring_perms(ring):
    count = len(ring)
    forward = [(ring[q], ring[(q + 1) % count]) for q in range(count)]
    backward = [(ring[q], ring[(q - 1) % count]) for q in range(count)]
    return forward, backward


def ring_gather(block, ring):
    count = len(ring)
    forward, backward = ring_perms(ring)
    full_steps = (count - 1) // 2
    split = count % 2 == 0
    half = block.shape[1] // 2
    lefts, rights = [], []
    current = block
    for _ in range(full_steps):
        current = lax.ppermute(current, "seq", forward)
        lefts.append(current)
    if split:
        left_half = lax.ppermute(current[:, :half], "seq", forward)
    current = block
    for _ in range(full_steps):
        current = lax.ppermute(current, "seq", backward)
        rights.append(current)
    if split:
        right_half = lax.ppermute(current[:, half:], "seq", backward)
    opposite = [jnp.concatenate([left_half, right_half], axis=1)] if split else []
    return [block] + lefts + rights + opposite


def add_part(term, received, side):
    if received.shape == term.shape:
        return term + received
    half = term.shape[1] - received.shape[1] if side else received.shape[1]
    if side:
        return jnp.concatenate([term[:, :half], term[:, half:] + received], axis=1)
    return jnp.concatenate([term[:, :half] + received, term[:, half:]], axis=1)


def ring_scatter_back(blocks, ring):
    count = len(ring)
    forward, backward = ring_perms(ring)
    full_steps = (count - 1) // 2
    split = count % 2 == 0
    own = blocks[0].astype(jnp.float32)
    lefts = blocks[1 : 1 + full_steps]
    rights = blocks[1 + full_steps : 1 + 2 * full_steps]
    total = own
    for side, chain, perm in ((0, lefts, backward), (1, rights, forward)):
        if split:
            half = blocks[-1].shape[1] // 2
            acc = blocks[-1][:, half:] if side else blocks[-1][:, :half]
            top = full_steps + 1
        elif full_steps:
            acc = chain[-1]
            top = full_steps
        else:
            continue
        for t in range(top, 0, -1):
            received = lax.ppermute(acc, "seq", perm).astype(jnp.float32)
            if t == 1:
                total = add_part(total, received, side)
            else:
                acc = add_part(chain[t - 2].astype(jnp.float32), received, side).astype(
                    jnp.bfloat16
                )
    return total


def ring_reduce_scatter(blocks, axis, ring, forward_dir=True):
    count = len(ring)
    if count == 1:
        return blocks[0]
    forward, backward = ring_perms(ring)
    perm = forward if forward_dir else backward
    sign = 1 if forward_dir else -1
    position = jnp.zeros((), jnp.int32)
    index = lax.axis_index(axis)
    for q, s in enumerate(ring):
        position = jnp.where(index == s, q, position)
    offsets = (position + count - sign * jnp.arange(count, dtype=jnp.int32)) % count
    order = jnp.zeros((count,), jnp.int32)
    for q, s in enumerate(ring):
        order = jnp.where(offsets == q, s, order)
    relative = jnp.take(blocks, order, axis=0)
    acc = relative[1]
    for t in range(count - 1):
        received = lax.ppermute(acc, axis, perm)
        acc = received + relative[(t + 2) % count]
    return acc


def ring_position(axis, ring):
    position = jnp.zeros((), jnp.int32)
    index = lax.axis_index(axis)
    for q, s in enumerate(ring):
        position = jnp.where(index == s, q, position)
    return position


def ring_reduce_scatter_sliced(select_block, axis, ring, forward_dir=True, wire_dtype=jnp.bfloat16):
    count = len(ring)
    forward, backward = ring_perms(ring)
    perm = forward if forward_dir else backward
    sign = 1 if forward_dir else -1
    position = ring_position(axis, ring)

    def block_at(offset):
        target = (position + count - sign * (offset % count)) % count
        index = jnp.zeros((), jnp.int32)
        for q, s in enumerate(ring):
            index = jnp.where(target == q, s, index)
        return select_block(index)

    acc = block_at(1).astype(wire_dtype)
    for t in range(count - 1):
        received = lax.ppermute(acc, axis, perm).astype(jnp.float32)
        acc = received + block_at(t + 2)
        if t < count - 2:
            acc = acc.astype(wire_dtype)
    return acc


def neighbor_rows(array, width):
    count = lax.axis_size("seq")
    up = [(i, i + 1) for i in range(count - 1)]
    down = [(j, i) for i, j in up]
    before = lax.ppermute(array[-width:], "seq", up)
    after = lax.ppermute(array[:width], "seq", down)
    return before, after


def attend_rows(query_rows, all_keys, all_values, score_scale):
    scores = (
        jnp.einsum(
            "ihd,jhd->hij",
            query_rows.reshape(query_rows.shape[0], H, DK),
            all_keys,
            preferred_element_type=jnp.float32,
        )
        * score_scale
    )
    row_peak = jnp.max(scores, axis=2, keepdims=True)
    row_total = jnp.sum(jnp.exp(scores - row_peak), axis=2, keepdims=True)
    rounded = jnp.exp(scores - (row_peak + jnp.log(row_total))).astype(jnp.bfloat16)
    return jnp.einsum(
        "hij,jhd->ihd", rounded, all_values, preferred_element_type=jnp.float32
    ).astype(jnp.bfloat16)


def body(ring, queries, key_rows, value_rows, trunk_state, skip_input, norm_gain, conv_weight, cotangent):
    score_scale = DK ** (-0.5)
    local_tokens = queries.shape[1]
    positions = 2 * local_tokens
    half_kernel = KW // 2
    query_heads = queries[0].reshape(local_tokens, H, DK)
    seq_index, seq_total = lax.axis_index("seq"), lax.axis_size("seq")
    halo_tokens = half_kernel
    query_before, query_after = neighbor_rows(queries[0], halo_tokens)
    trunk_before, trunk_after = neighbor_rows(trunk_state[0], halo_tokens)
    skip_before, skip_after = neighbor_rows(skip_input[0], 2 * halo_tokens)
    cotangent_before, cotangent_after = neighbor_rows(cotangent[0], half_kernel)
    key_value_blocks = ring_gather(jnp.concatenate([key_rows[0], value_rows[0]], axis=1), ring)
    gathered = jnp.concatenate(key_value_blocks, axis=0)
    all_keys = gathered[:, : H * DK].reshape(-1, H, DK)
    all_values = gathered[:, H * DK :].reshape(-1, H, DV)
    scores = (
        jnp.einsum("ihd,jhd->hij", query_heads, all_keys, preferred_element_type=jnp.float32)
        * score_scale
    )
    row_peak = jnp.max(scores, axis=2, keepdims=True)
    row_total = jnp.sum(jnp.exp(scores - row_peak), axis=2, keepdims=True)
    logsum = row_peak + jnp.log(row_total)
    softmax = jnp.exp(scores - logsum)
    rounded = softmax.astype(jnp.bfloat16)
    attended = jnp.einsum(
        "hij,jhd->ihd", rounded, all_values, preferred_element_type=jnp.float32
    ).astype(jnp.bfloat16)
    upsample = (
        jnp.arange(positions, dtype=jnp.int32)[:, None] // 2
        == jnp.arange(local_tokens, dtype=jnp.int32)[None, :]
    ).astype(jnp.bfloat16)
    hidden_up = jnp.dot(
        upsample, trunk_state[0], preferred_element_type=jnp.float32
    ) + jnp.dot(
        upsample, attended.reshape(local_tokens, H * DV), preferred_element_type=jnp.float32
    )
    merged = hidden_up + skip_input[0].astype(jnp.float32)
    inverse = lax.rsqrt(jnp.mean(merged * merged, axis=1, keepdims=True) + 1e-06)
    channel_gain = norm_gain.astype(jnp.float32)
    normed = (merged * inverse * channel_gain).astype(jnp.bfloat16)
    halo_attended = attend_rows(
        jnp.concatenate([query_before, query_after], axis=0), all_keys, all_values, score_scale
    ).reshape(2 * halo_tokens, H * DV)
    halo_hidden = jnp.concatenate([trunk_before, trunk_after], axis=0).astype(
        jnp.float32
    ) + halo_attended.astype(jnp.float32)
    halo_merged = jnp.repeat(halo_hidden, 2, axis=0) + jnp.concatenate(
        [skip_before, skip_after], axis=0
    ).astype(jnp.float32)
    halo_inverse = lax.rsqrt(jnp.mean(halo_merged * halo_merged, axis=1, keepdims=True) + 1e-06)
    halo_rows = 2 * halo_tokens
    halo_valid = jnp.concatenate(
        [
            jnp.broadcast_to(seq_index > 0, (halo_rows,)),
            jnp.broadcast_to(seq_index < seq_total - 1, (halo_rows,)),
        ]
    )
    halo_normed = jnp.where(
        halo_valid[:, None], halo_merged * halo_inverse * channel_gain, 0.0
    ).astype(jnp.bfloat16)
    normed_before, normed_after = halo_normed[:halo_rows], halo_normed[halo_rows:]
    padded = jnp.concatenate(
        [normed_before[halo_rows - half_kernel :], normed, normed_after[:half_kernel]], axis=0
    )
    columns = window_rows(padded, KW, positions)
    preact = jnp.dot(columns, conv_weight, preferred_element_type=jnp.float32)
    activated, derivative = gelu_parts(preact)
    decoded = activated.astype(jnp.bfloat16)
    grad_pre = (cotangent[0].astype(jnp.float32) * derivative).astype(jnp.bfloat16)
    halo_columns = jnp.concatenate(
        [
            window_rows(
                jnp.concatenate([normed_before, normed[:half_kernel]], axis=0)[
                    halo_rows - 2 * half_kernel :
                ],
                KW,
                half_kernel,
            ),
            window_rows(
                jnp.concatenate([normed[positions - half_kernel :], normed_after], axis=0)[
                    : 4 * half_kernel
                ],
                KW,
                half_kernel,
            ),
        ],
        axis=0,
    )
    halo_preact = jnp.dot(halo_columns, conv_weight, preferred_element_type=jnp.float32)
    halo_grad = (
        jnp.concatenate([cotangent_before, cotangent_after], axis=0).astype(jnp.float32)
        * gelu_parts(halo_preact)[1]
    ).astype(jnp.bfloat16)
    grad_padded = jnp.concatenate(
        [halo_grad[:half_kernel], grad_pre, halo_grad[half_kernel:]], axis=0
    )
    norm_scale = (lax.axis_size("dp") * positions * lax.axis_size("seq")) ** (-0.5)
    seq_count, dp_count = lax.axis_size("seq"), lax.axis_size("dp")
    rows_per = KW * C // (seq_count * dp_count)
    half_co = CO // 2
    if dp_count == 2:
        partner = [(0, 1), (1, 0)]
        both_padded = jnp.stack([padded, lax.ppermute(padded, "dp", partner)])
        both_grad = jnp.stack([grad_pre, lax.ppermute(grad_pre, "dp", partner)])
        full_weight = (
            jnp.concatenate(
                [
                    jnp.einsum(
                        "spc,spo->co",
                        both_padded[:, offset : offset + positions],
                        both_grad,
                        preferred_element_type=jnp.float32,
                    )
                    for offset in range(KW)
                ],
                axis=0,
            )
            * norm_scale
        ).reshape(seq_count, dp_count, rows_per, CO)
        dp_index = lax.axis_index("dp")

        def weight_block(column, width):
            return lambda index: lax.dynamic_slice(
                full_weight, (index, dp_index, 0, column), (1, 1, rows_per, width)
            ).reshape(rows_per, width)

        grad_weight = jnp.concatenate(
            [
                ring_reduce_scatter_sliced(weight_block(0, half_co), "seq", ring, True),
                ring_reduce_scatter_sliced(
                    weight_block(half_co, CO - half_co), "seq", ring, False
                ),
            ],
            axis=1,
        )
    else:
        weight_part = (
            lax.dot_general(
                columns, grad_pre, (((0,), (0,)), ((), ())), preferred_element_type=jnp.float32
            )
            * norm_scale
        )
        weight_blocks_all = weight_part.reshape(seq_count, dp_count, -1, CO)
        dp_summed = ring_reduce_scatter(
            jnp.swapaxes(weight_blocks_all, 0, 1), "dp", list(range(dp_count))
        )
        grad_weight = jnp.concatenate(
            [
                ring_reduce_scatter(dp_summed[:, :, :half_co], "seq", ring, True),
                ring_reduce_scatter(dp_summed[:, :, half_co:], "seq", ring, False),
            ],
            axis=1,
        )
    stacked = jnp.stack(
        [
            grad_padded[2 * half_kernel - offset : 2 * half_kernel - offset + positions]
            for offset in range(KW)
        ],
        axis=1,
    )
    weight_blocks = conv_weight.reshape(KW, C, CO)
    grad_normed = jnp.einsum(
        "pko,kco->pc", stacked, weight_blocks, preferred_element_type=jnp.float32
    )
    scaled_grad = grad_normed * channel_gain
    grad_merged = inverse * scaled_grad - merged * inverse**3 * jnp.mean(
        scaled_grad * merged, axis=1, keepdims=True
    )
    grad_skip = grad_merged.astype(jnp.bfloat16)
    grad_trunk = jnp.dot(
        upsample.T.astype(jnp.float32),
        grad_merged,
        precision=lax.Precision.HIGHEST,
        preferred_element_type=jnp.float32,
    ).astype(jnp.bfloat16)
    grad_heads = grad_trunk.reshape(local_tokens, H, DV)
    row_delta = jnp.sum(grad_heads.astype(jnp.float32) * attended.astype(jnp.float32), axis=2)
    value_grad = jnp.einsum(
        "ihd,jhd->hij", grad_heads, all_values, preferred_element_type=jnp.float32
    )
    slopes = (softmax * (value_grad - row_delta.T[:, :, None])).astype(jnp.bfloat16)
    grad_queries = (
        jnp.einsum("hij,jhd->ihd", slopes, all_keys, preferred_element_type=jnp.float32)
        * score_scale
    ).astype(jnp.bfloat16)
    key_part = (
        jnp.einsum("hij,ihd->jhd", slopes, query_heads, preferred_element_type=jnp.float32)
        * score_scale
    )
    value_part = jnp.einsum("hij,ihd->jhd", rounded, grad_heads, preferred_element_type=jnp.float32)
    terms = jnp.concatenate(
        [
            key_part.reshape(-1, H * DK),
            value_part.reshape(-1, H * DV),
        ],
        axis=1,
    ).astype(jnp.bfloat16)
    term_blocks = [
        terms[m * local_tokens : (m + 1) * local_tokens] for m in range(lax.axis_size("seq"))
    ]
    summed = ring_scatter_back(term_blocks, ring)
    grad_keys = summed[:, : H * DK].astype(jnp.bfloat16)
    grad_values = summed[:, H * DK :].astype(jnp.bfloat16)
    return (
        decoded[None],
        grad_queries.reshape(local_tokens, H * DK)[None],
        grad_keys[None],
        grad_values[None],
        grad_trunk[None],
        grad_skip[None],
        grad_weight,
    )


def solution(mesh):
    return jax.shard_map(
        functools.partial(body, ring_order(mesh)),
        mesh=mesh,
        in_specs=(
            P(("group", "dp"), "seq", None),
            P(("group", "dp"), "seq", None),
            P(("group", "dp"), "seq", None),
            P(("group", "dp"), "seq", None),
            P(("group", "dp"), "seq", None),
            P(),
            P(),
            P(("group", "dp"), "seq", None),
        ),
        out_specs=(
            P(("group", "dp"), "seq", None),
            P(("group", "dp"), "seq", None),
            P(("group", "dp"), "seq", None),
            P(("group", "dp"), "seq", None),
            P(("group", "dp"), "seq", None),
            P(("group", "dp"), "seq", None),
            P(("group", "seq", "dp"), None),
        ),
        check_vma=False,
    )
```

```python
import functools
import math

import jax
import jax.numpy as jnp
from jax import lax
from jax.sharding import PartitionSpec as P

H = 4
DK = 128
DV = 192
C = 768
CO = 384
KW = 5


def extended(array, sides, width):
    for axis, dim in sides:
        count, length = (lax.axis_size(axis), array.shape[dim])
        up = [(i, (i + 1) % count) for i in range(count - 1)]
        down = [(j, i) for i, j in up]
        last = lax.slice_in_dim(array, length - width, length, axis=dim)
        initial = lax.slice_in_dim(array, 0, width, axis=dim)
        before = lax.ppermute(last, axis, up)
        after = lax.ppermute(initial, axis, down)
        array = jnp.concatenate([before, array, after], axis=dim)
    return array


def gelu_parts(preact):
    cdf_value = 0.5 * (1.0 + jax.scipy.special.erf(preact * (1.0 / math.sqrt(2.0))))
    density = jnp.exp(-0.5 * preact * preact) * (1.0 / math.sqrt(2.0 * math.pi))
    return (preact * cdf_value, cdf_value + preact * density)


def window_rows(padded, kernel, row_count):
    return jnp.concatenate(
        [padded[offset : offset + row_count] for offset in range(kernel)], axis=1
    )


def ring_order(mesh):
    count = mesh.shape["seq"]
    try:
        row = mesh.devices.reshape(mesh.shape["group"], count, -1)[0, :, 0]
        coords = [tuple(device.coords) for device in row]
    except (AttributeError, TypeError):
        return list(range(count))
    varying = [d for d in range(3) if len({c[d] for c in coords}) > 1]
    if len(varying) == 2:
        for minor, major in (varying, varying[::-1]):
            if len({c[minor] for c in coords}) == 2:
                low = min(c[minor] for c in coords)
                first = sorted((c[major], s) for s, c in enumerate(coords) if c[minor] == low)
                second = sorted((c[major], s) for s, c in enumerate(coords) if c[minor] != low)
                return [s for _, s in first] + [s for _, s in second[::-1]]
    return list(range(count))


def ring_perms(ring):
    count = len(ring)
    forward = [(ring[q], ring[(q + 1) % count]) for q in range(count)]
    backward = [(ring[q], ring[(q - 1) % count]) for q in range(count)]
    return forward, backward


def ring_gather(block, ring):
    count = len(ring)
    forward, backward = ring_perms(ring)
    full_steps = (count - 1) // 2
    split = count % 2 == 0
    half = block.shape[1] // 2
    lefts, rights = [], []
    current = block
    for _ in range(full_steps):
        current = lax.ppermute(current, "seq", forward)
        lefts.append(current)
    if split:
        left_half = lax.ppermute(current[:, :half], "seq", forward)
    current = block
    for _ in range(full_steps):
        current = lax.ppermute(current, "seq", backward)
        rights.append(current)
    if split:
        right_half = lax.ppermute(current[:, half:], "seq", backward)
    opposite = [jnp.concatenate([left_half, right_half], axis=1)] if split else []
    return [block] + lefts + rights + opposite


def add_part(term, received, side):
    if received.shape == term.shape:
        return term + received
    half = term.shape[1] - received.shape[1] if side else received.shape[1]
    if side:
        return jnp.concatenate([term[:, :half], term[:, half:] + received], axis=1)
    return jnp.concatenate([term[:, :half] + received, term[:, half:]], axis=1)


def ring_scatter_back(blocks, ring):
    count = len(ring)
    forward, backward = ring_perms(ring)
    full_steps = (count - 1) // 2
    split = count % 2 == 0
    own = blocks[0].astype(jnp.float32)
    lefts = blocks[1 : 1 + full_steps]
    rights = blocks[1 + full_steps : 1 + 2 * full_steps]
    total = own
    for side, chain, perm in ((0, lefts, backward), (1, rights, forward)):
        if split:
            half = blocks[-1].shape[1] // 2
            acc = blocks[-1][:, half:] if side else blocks[-1][:, :half]
            top = full_steps + 1
        elif full_steps:
            acc = chain[-1]
            top = full_steps
        else:
            continue
        for t in range(top, 0, -1):
            received = lax.ppermute(acc, "seq", perm).astype(jnp.float32)
            if t == 1:
                total = add_part(total, received, side)
            else:
                acc = add_part(chain[t - 2].astype(jnp.float32), received, side).astype(
                    jnp.bfloat16
                )
    return total


def ring_reduce_scatter(blocks, axis, ring, forward_dir=True):
    count = len(ring)
    if count == 1:
        return blocks[0]
    forward, backward = ring_perms(ring)
    perm = forward if forward_dir else backward
    sign = 1 if forward_dir else -1
    position = jnp.zeros((), jnp.int32)
    index = lax.axis_index(axis)
    for q, s in enumerate(ring):
        position = jnp.where(index == s, q, position)
    offsets = (position + count - sign * jnp.arange(count, dtype=jnp.int32)) % count
    order = jnp.zeros((count,), jnp.int32)
    for q, s in enumerate(ring):
        order = jnp.where(offsets == q, s, order)
    relative = jnp.take(blocks, order, axis=0)
    acc = relative[1]
    for t in range(count - 1):
        received = lax.ppermute(acc, axis, perm)
        acc = received + relative[(t + 2) % count]
    return acc


def ring_position(axis, ring):
    position = jnp.zeros((), jnp.int32)
    index = lax.axis_index(axis)
    for q, s in enumerate(ring):
        position = jnp.where(index == s, q, position)
    return position


def ring_reduce_scatter_sliced(select_block, axis, ring, forward_dir=True, wire_dtype=jnp.bfloat16):
    count = len(ring)
    forward, backward = ring_perms(ring)
    perm = forward if forward_dir else backward
    sign = 1 if forward_dir else -1
    position = ring_position(axis, ring)

    def block_at(offset):
        target = (position + count - sign * (offset % count)) % count
        index = jnp.zeros((), jnp.int32)
        for q, s in enumerate(ring):
            index = jnp.where(target == q, s, index)
        return select_block(index)

    acc = block_at(1).astype(wire_dtype)
    for t in range(count - 1):
        received = lax.ppermute(acc, axis, perm).astype(jnp.float32)
        acc = received + block_at(t + 2)
        if t < count - 2:
            acc = acc.astype(wire_dtype)
    return acc


def body(ring, queries, key_rows, value_rows, trunk_state, skip_input, norm_gain, conv_weight, cotangent):
    score_scale = DK ** (-0.5)
    local_tokens = queries.shape[1]
    positions = 2 * local_tokens
    half_kernel = KW // 2
    query_heads = queries[0].reshape(local_tokens, H, DK)
    key_value_blocks = ring_gather(jnp.concatenate([key_rows[0], value_rows[0]], axis=1), ring)
    gathered = jnp.concatenate(key_value_blocks, axis=0)
    queries_after, gathered = lax.optimization_barrier((queries[0], gathered))
    query_blocks = ring_gather(queries_after, ring)
    all_keys = gathered[:, : H * DK].reshape(-1, H, DK)
    all_values = gathered[:, H * DK :].reshape(-1, H, DV)
    scores = (
        jnp.einsum("ihd,jhd->hij", query_heads, all_keys, preferred_element_type=jnp.float32)
        * score_scale
    )
    row_peak = jnp.max(scores, axis=2, keepdims=True)
    row_total = jnp.sum(jnp.exp(scores - row_peak), axis=2, keepdims=True)
    logsum = row_peak + jnp.log(row_total)
    softmax = jnp.exp(scores - logsum)
    rounded = softmax.astype(jnp.bfloat16)
    attended = jnp.einsum(
        "hij,jhd->ihd", rounded, all_values, preferred_element_type=jnp.float32
    ).astype(jnp.bfloat16)
    upsample = (
        jnp.arange(positions, dtype=jnp.int32)[:, None] // 2
        == jnp.arange(local_tokens, dtype=jnp.int32)[None, :]
    ).astype(jnp.bfloat16)
    hidden_up = jnp.dot(
        upsample, trunk_state[0], preferred_element_type=jnp.float32
    ) + jnp.dot(
        upsample, attended.reshape(local_tokens, H * DV), preferred_element_type=jnp.float32
    )
    merged = hidden_up + skip_input[0].astype(jnp.float32)
    inverse = lax.rsqrt(jnp.mean(merged * merged, axis=1, keepdims=True) + 1e-06)
    channel_gain = norm_gain.astype(jnp.float32)
    normed = (merged * inverse * channel_gain).astype(jnp.bfloat16)
    padded = extended(normed, (("seq", 0),), half_kernel)
    columns = window_rows(padded, KW, positions)
    preact = jnp.dot(columns, conv_weight, preferred_element_type=jnp.float32)
    activated, derivative = gelu_parts(preact)
    decoded = activated.astype(jnp.bfloat16)
    grad_pre = (cotangent[0].astype(jnp.float32) * derivative).astype(jnp.bfloat16)
    grad_padded = extended(grad_pre, (("seq", 0),), half_kernel)
    norm_scale = (lax.axis_size("dp") * positions * lax.axis_size("seq")) ** (-0.5)
    seq_count, dp_count = lax.axis_size("seq"), lax.axis_size("dp")
    rows_per = KW * C // (seq_count * dp_count)
    half_co = CO // 2
    if dp_count == 2:
        partner = [(0, 1), (1, 0)]
        both_padded = jnp.stack([padded, lax.ppermute(padded, "dp", partner)])
        both_grad = jnp.stack([grad_pre, lax.ppermute(grad_pre, "dp", partner)])
        full_weight = (
            jnp.concatenate(
                [
                    jnp.einsum(
                        "spc,spo->co",
                        both_padded[:, offset : offset + positions],
                        both_grad,
                        preferred_element_type=jnp.float32,
                    )
                    for offset in range(KW)
                ],
                axis=0,
            )
            * norm_scale
        ).reshape(seq_count, dp_count, rows_per, CO)
        dp_index = lax.axis_index("dp")

        def weight_block(column, width):
            return lambda index: lax.dynamic_slice(
                full_weight, (index, dp_index, 0, column), (1, 1, rows_per, width)
            ).reshape(rows_per, width)

        grad_weight = jnp.concatenate(
            [
                ring_reduce_scatter_sliced(weight_block(0, half_co), "seq", ring, True),
                ring_reduce_scatter_sliced(
                    weight_block(half_co, CO - half_co), "seq", ring, False
                ),
            ],
            axis=1,
        )
    else:
        weight_part = (
            lax.dot_general(
                columns, grad_pre, (((0,), (0,)), ((), ())), preferred_element_type=jnp.float32
            )
            * norm_scale
        )
        weight_blocks_all = weight_part.reshape(seq_count, dp_count, -1, CO)
        dp_summed = ring_reduce_scatter(
            jnp.swapaxes(weight_blocks_all, 0, 1), "dp", list(range(dp_count))
        )
        grad_weight = jnp.concatenate(
            [
                ring_reduce_scatter(dp_summed[:, :, :half_co], "seq", ring, True),
                ring_reduce_scatter(dp_summed[:, :, half_co:], "seq", ring, False),
            ],
            axis=1,
        )
    stacked = jnp.stack(
        [
            grad_padded[2 * half_kernel - offset : 2 * half_kernel - offset + positions]
            for offset in range(KW)
        ],
        axis=1,
    )
    weight_blocks = conv_weight.reshape(KW, C, CO)
    grad_normed = jnp.einsum(
        "pko,kco->pc", stacked, weight_blocks, preferred_element_type=jnp.float32
    )
    scaled_grad = grad_normed * channel_gain
    grad_merged = inverse * scaled_grad - merged * inverse**3 * jnp.mean(
        scaled_grad * merged, axis=1, keepdims=True
    )
    grad_skip = grad_merged.astype(jnp.bfloat16)
    grad_trunk = jnp.dot(
        upsample.T.astype(jnp.float32),
        grad_merged,
        precision=lax.Precision.HIGHEST,
        preferred_element_type=jnp.float32,
    ).astype(jnp.bfloat16)
    grad_heads = grad_trunk.reshape(local_tokens, H, DV)
    row_delta = jnp.sum(grad_heads.astype(jnp.float32) * attended.astype(jnp.float32), axis=2)
    value_grad = jnp.einsum(
        "ihd,jhd->hij", grad_heads, all_values, preferred_element_type=jnp.float32
    )
    slopes = (softmax * (value_grad - row_delta.T[:, :, None])).astype(jnp.bfloat16)
    grad_queries = (
        jnp.einsum("hij,jhd->ihd", slopes, all_keys, preferred_element_type=jnp.float32)
        * score_scale
    ).astype(jnp.bfloat16)
    stats = jnp.concatenate([logsum[:, :, 0].T, row_delta], axis=1)
    query_all = jnp.stack(query_blocks).reshape(-1, local_tokens, H, DK)
    grad_all = jnp.stack(ring_gather(grad_trunk, ring)).reshape(-1, local_tokens, H, DV)
    stats_all = jnp.stack(ring_gather(stats, ring))
    logsum_all = jnp.swapaxes(stats_all[:, :, :H], 1, 2)[..., None]
    delta_all = jnp.swapaxes(stats_all[:, :, H:], 1, 2)[..., None]
    own_keys = key_rows[0].reshape(local_tokens, H, DK)
    own_values = value_rows[0].reshape(local_tokens, H, DV)
    scores_t = (
        jnp.einsum("mihd,jhd->mhij", query_all, own_keys, preferred_element_type=jnp.float32)
        * score_scale
    )
    softmax_t = jnp.exp(scores_t - logsum_all)
    value_grad_t = jnp.einsum(
        "mihd,jhd->mhij", grad_all, own_values, preferred_element_type=jnp.float32
    )
    slopes_t = (softmax_t * (value_grad_t - delta_all)).astype(jnp.bfloat16)
    key_terms = (
        jnp.einsum("mhij,mihd->mjhd", slopes_t, query_all, preferred_element_type=jnp.float32)
        * score_scale
    ).astype(jnp.bfloat16)
    value_terms = jnp.einsum(
        "mhij,mihd->mjhd",
        softmax_t.astype(jnp.bfloat16),
        grad_all,
        preferred_element_type=jnp.float32,
    ).astype(jnp.bfloat16)
    grad_keys = (
        key_terms.astype(jnp.float32).sum(axis=0).astype(jnp.bfloat16).reshape(local_tokens, H * DK)
    )
    grad_values = (
        value_terms.astype(jnp.float32)
        .sum(axis=0)
        .astype(jnp.bfloat16)
        .reshape(local_tokens, H * DV)
    )
    return (
        decoded[None],
        grad_queries.reshape(local_tokens, H * DK)[None],
        grad_keys[None],
        grad_values[None],
        grad_trunk[None],
        grad_skip[None],
        grad_weight,
    )


def solution(mesh):
    return jax.shard_map(
        functools.partial(body, ring_order(mesh)),
        mesh=mesh,
        in_specs=(
            P(("group", "dp"), "seq", None),
            P(("group", "dp"), "seq", None),
            P(("group", "dp"), "seq", None),
            P(("group", "dp"), "seq", None),
            P(("group", "dp"), "seq", None),
            P(),
            P(),
            P(("group", "dp"), "seq", None),
        ),
        out_specs=(
            P(("group", "dp"), "seq", None),
            P(("group", "dp"), "seq", None),
            P(("group", "dp"), "seq", None),
            P(("group", "dp"), "seq", None),
            P(("group", "dp"), "seq", None),
            P(("group", "dp"), "seq", None),
            P(("group", "seq", "dp"), None),
        ),
        check_vma=False,
    )
```

```python
import functools
import math

import jax
import jax.numpy as jnp
from jax import lax
from jax.sharding import PartitionSpec as P

H = 4
DK = 128
DV = 192
C = 768
CO = 384
KW = 5


def extended(array, sides, width):
    for axis, dim in sides:
        count, length = (lax.axis_size(axis), array.shape[dim])
        up = [(i, (i + 1) % count) for i in range(count - 1)]
        down = [(j, i) for i, j in up]
        last = lax.slice_in_dim(array, length - width, length, axis=dim)
        initial = lax.slice_in_dim(array, 0, width, axis=dim)
        before = lax.ppermute(last, axis, up)
        after = lax.ppermute(initial, axis, down)
        array = jnp.concatenate([before, array, after], axis=dim)
    return array


def gelu_parts(preact):
    cdf_value = 0.5 * (1.0 + jax.scipy.special.erf(preact * (1.0 / math.sqrt(2.0))))
    density = jnp.exp(-0.5 * preact * preact) * (1.0 / math.sqrt(2.0 * math.pi))
    return (preact * cdf_value, cdf_value + preact * density)


def window_rows(padded, kernel, row_count):
    return jnp.concatenate(
        [padded[offset : offset + row_count] for offset in range(kernel)], axis=1
    )


def ring_order(mesh):
    count = mesh.shape["seq"]
    try:
        row = mesh.devices.reshape(mesh.shape["group"], count, -1)[0, :, 0]
        coords = [tuple(device.coords) for device in row]
    except (AttributeError, TypeError):
        return list(range(count))
    varying = [d for d in range(3) if len({c[d] for c in coords}) > 1]
    if len(varying) == 2:
        for minor, major in (varying, varying[::-1]):
            if len({c[minor] for c in coords}) == 2:
                low = min(c[minor] for c in coords)
                first = sorted((c[major], s) for s, c in enumerate(coords) if c[minor] == low)
                second = sorted((c[major], s) for s, c in enumerate(coords) if c[minor] != low)
                return [s for _, s in first] + [s for _, s in second[::-1]]
    return list(range(count))


def ring_perms(ring):
    count = len(ring)
    forward = [(ring[q], ring[(q + 1) % count]) for q in range(count)]
    backward = [(ring[q], ring[(q - 1) % count]) for q in range(count)]
    return forward, backward


def ring_gather(block, ring):
    count = len(ring)
    forward, backward = ring_perms(ring)
    full_steps = (count - 1) // 2
    split = count % 2 == 0
    half = block.shape[1] // 2
    lefts, rights = [], []
    current = block
    for _ in range(full_steps):
        current = lax.ppermute(current, "seq", forward)
        lefts.append(current)
    if split:
        left_half = lax.ppermute(current[:, :half], "seq", forward)
    current = block
    for _ in range(full_steps):
        current = lax.ppermute(current, "seq", backward)
        rights.append(current)
    if split:
        right_half = lax.ppermute(current[:, half:], "seq", backward)
    opposite = [jnp.concatenate([left_half, right_half], axis=1)] if split else []
    return [block] + lefts + rights + opposite


def add_part(term, received, side):
    if received.shape == term.shape:
        return term + received
    half = term.shape[1] - received.shape[1] if side else received.shape[1]
    if side:
        return jnp.concatenate([term[:, :half], term[:, half:] + received], axis=1)
    return jnp.concatenate([term[:, :half] + received, term[:, half:]], axis=1)


def ring_scatter_back(blocks, ring):
    count = len(ring)
    forward, backward = ring_perms(ring)
    full_steps = (count - 1) // 2
    split = count % 2 == 0
    own = blocks[0].astype(jnp.float32)
    lefts = blocks[1 : 1 + full_steps]
    rights = blocks[1 + full_steps : 1 + 2 * full_steps]
    total = own
    for side, chain, perm in ((0, lefts, backward), (1, rights, forward)):
        if split:
            half = blocks[-1].shape[1] // 2
            acc = blocks[-1][:, half:] if side else blocks[-1][:, :half]
            top = full_steps + 1
        elif full_steps:
            acc = chain[-1]
            top = full_steps
        else:
            continue
        for t in range(top, 0, -1):
            received = lax.ppermute(acc, "seq", perm).astype(jnp.float32)
            if t == 1:
                total = add_part(total, received, side)
            else:
                acc = add_part(chain[t - 2].astype(jnp.float32), received, side).astype(
                    jnp.bfloat16
                )
    return total


def ring_reduce_scatter(blocks, axis, ring, forward_dir=True):
    count = len(ring)
    if count == 1:
        return blocks[0]
    forward, backward = ring_perms(ring)
    perm = forward if forward_dir else backward
    sign = 1 if forward_dir else -1
    position = jnp.zeros((), jnp.int32)
    index = lax.axis_index(axis)
    for q, s in enumerate(ring):
        position = jnp.where(index == s, q, position)
    offsets = (position + count - sign * jnp.arange(count, dtype=jnp.int32)) % count
    order = jnp.zeros((count,), jnp.int32)
    for q, s in enumerate(ring):
        order = jnp.where(offsets == q, s, order)
    relative = jnp.take(blocks, order, axis=0)
    acc = relative[1]
    for t in range(count - 1):
        received = lax.ppermute(acc, axis, perm)
        acc = received + relative[(t + 2) % count]
    return acc


def ring_position(axis, ring):
    position = jnp.zeros((), jnp.int32)
    index = lax.axis_index(axis)
    for q, s in enumerate(ring):
        position = jnp.where(index == s, q, position)
    return position


def ring_reduce_scatter_sliced(select_block, axis, ring, forward_dir=True, wire_dtype=jnp.bfloat16):
    count = len(ring)
    forward, backward = ring_perms(ring)
    perm = forward if forward_dir else backward
    sign = 1 if forward_dir else -1
    position = ring_position(axis, ring)

    def block_at(offset):
        target = (position + count - sign * (offset % count)) % count
        index = jnp.zeros((), jnp.int32)
        for q, s in enumerate(ring):
            index = jnp.where(target == q, s, index)
        return select_block(index)

    acc = block_at(1).astype(wire_dtype)
    for t in range(count - 1):
        received = lax.ppermute(acc, axis, perm).astype(jnp.float32)
        acc = received + block_at(t + 2)
        if t < count - 2:
            acc = acc.astype(wire_dtype)
    return acc


def body(ring, queries, key_rows, value_rows, trunk_state, skip_input, norm_gain, conv_weight, cotangent):
    score_scale = DK ** (-0.5)
    local_tokens = queries.shape[1]
    positions = 2 * local_tokens
    half_kernel = KW // 2
    query_heads = queries[0].reshape(local_tokens, H, DK)
    key_value_blocks = ring_gather(jnp.concatenate([key_rows[0], value_rows[0]], axis=1), ring)
    gathered = jnp.concatenate(key_value_blocks, axis=0)
    all_keys = gathered[:, : H * DK].reshape(-1, H, DK)
    all_values = gathered[:, H * DK :].reshape(-1, H, DV)
    scores = (
        jnp.einsum("ihd,jhd->hij", query_heads, all_keys, preferred_element_type=jnp.float32)
        * score_scale
    )
    row_peak = jnp.max(scores, axis=2, keepdims=True)
    row_total = jnp.sum(jnp.exp(scores - row_peak), axis=2, keepdims=True)
    logsum = row_peak + jnp.log(row_total)
    softmax = jnp.exp(scores - logsum)
    rounded = softmax.astype(jnp.bfloat16)
    attended = jnp.einsum(
        "hij,jhd->ihd", rounded, all_values, preferred_element_type=jnp.float32
    ).astype(jnp.bfloat16)
    upsample = (
        jnp.arange(positions, dtype=jnp.int32)[:, None] // 2
        == jnp.arange(local_tokens, dtype=jnp.int32)[None, :]
    ).astype(jnp.bfloat16)
    hidden_up = jnp.dot(
        upsample, trunk_state[0], preferred_element_type=jnp.float32
    ) + jnp.dot(
        upsample, attended.reshape(local_tokens, H * DV), preferred_element_type=jnp.float32
    )
    merged = hidden_up + skip_input[0].astype(jnp.float32)
    inverse = lax.rsqrt(jnp.mean(merged * merged, axis=1, keepdims=True) + 1e-06)
    channel_gain = norm_gain.astype(jnp.float32)
    normed = (merged * inverse * channel_gain).astype(jnp.bfloat16)
    padded = extended(normed, (("seq", 0),), half_kernel)
    columns = window_rows(padded, KW, positions)
    preact = jnp.dot(columns, conv_weight, preferred_element_type=jnp.float32)
    activated, derivative = gelu_parts(preact)
    decoded = activated.astype(jnp.bfloat16)
    grad_pre = (cotangent[0].astype(jnp.float32) * derivative).astype(jnp.bfloat16)
    grad_padded = extended(grad_pre, (("seq", 0),), half_kernel)
    norm_scale = (lax.axis_size("dp") * positions * lax.axis_size("seq")) ** (-0.5)
    seq_count, dp_count = lax.axis_size("seq"), lax.axis_size("dp")
    rows_per = KW * C // (seq_count * dp_count)
    stacked = jnp.stack(
        [
            grad_padded[2 * half_kernel - offset : 2 * half_kernel - offset + positions]
            for offset in range(KW)
        ],
        axis=1,
    )
    weight_blocks = conv_weight.reshape(KW, C, CO)
    grad_normed = jnp.einsum(
        "pko,kco->pc", stacked, weight_blocks, preferred_element_type=jnp.float32
    )
    scaled_grad = grad_normed * channel_gain
    grad_merged = inverse * scaled_grad - merged * inverse**3 * jnp.mean(
        scaled_grad * merged, axis=1, keepdims=True
    )
    grad_skip = grad_merged.astype(jnp.bfloat16)
    grad_trunk = jnp.dot(
        upsample.T.astype(jnp.float32),
        grad_merged,
        precision=lax.Precision.HIGHEST,
        preferred_element_type=jnp.float32,
    ).astype(jnp.bfloat16)
    grad_heads = grad_trunk.reshape(local_tokens, H, DV)
    row_delta = jnp.sum(grad_heads.astype(jnp.float32) * attended.astype(jnp.float32), axis=2)
    value_grad = jnp.einsum(
        "ihd,jhd->hij", grad_heads, all_values, preferred_element_type=jnp.float32
    )
    slopes = (softmax * (value_grad - row_delta.T[:, :, None])).astype(jnp.bfloat16)
    grad_queries = (
        jnp.einsum("hij,jhd->ihd", slopes, all_keys, preferred_element_type=jnp.float32)
        * score_scale
    ).astype(jnp.bfloat16)
    key_part = (
        jnp.einsum("hij,ihd->jhd", slopes, query_heads, preferred_element_type=jnp.float32)
        * score_scale
    )
    value_part = jnp.einsum("hij,ihd->jhd", rounded, grad_heads, preferred_element_type=jnp.float32)
    terms = jnp.concatenate(
        [
            key_part.reshape(-1, H * DK),
            value_part.reshape(-1, H * DV),
        ],
        axis=1,
    ).astype(jnp.bfloat16)
    half_co = CO // 2
    if dp_count == 2:
        partner = [(0, 1), (1, 0)]
        both_padded = jnp.stack([padded, lax.ppermute(padded, "dp", partner)])
        both_grad = jnp.stack([grad_pre, lax.ppermute(grad_pre, "dp", partner)])
        both_padded, both_grad, terms = lax.optimization_barrier((both_padded, both_grad, terms))
        full_weight = (
            jnp.concatenate(
                [
                    jnp.einsum(
                        "spc,spo->co",
                        both_padded[:, offset : offset + positions],
                        both_grad,
                        preferred_element_type=jnp.float32,
                    )
                    for offset in range(KW)
                ],
                axis=0,
            )
            * norm_scale
        ).reshape(seq_count, dp_count, rows_per, CO)
        dp_index = lax.axis_index("dp")

        def weight_block(column, width):
            return lambda index: lax.dynamic_slice(
                full_weight, (index, dp_index, 0, column), (1, 1, rows_per, width)
            ).reshape(rows_per, width)

        grad_weight = jnp.concatenate(
            [
                ring_reduce_scatter_sliced(weight_block(0, half_co), "seq", ring, True),
                ring_reduce_scatter_sliced(
                    weight_block(half_co, CO - half_co), "seq", ring, False
                ),
            ],
            axis=1,
        )
    else:
        weight_part = (
            lax.dot_general(
                columns, grad_pre, (((0,), (0,)), ((), ())), preferred_element_type=jnp.float32
            )
            * norm_scale
        )
        weight_blocks_all = weight_part.reshape(seq_count, dp_count, -1, CO)
        dp_summed = ring_reduce_scatter(
            jnp.swapaxes(weight_blocks_all, 0, 1), "dp", list(range(dp_count))
        )
        grad_weight = jnp.concatenate(
            [
                ring_reduce_scatter(dp_summed[:, :, :half_co], "seq", ring, True),
                ring_reduce_scatter(dp_summed[:, :, half_co:], "seq", ring, False),
            ],
            axis=1,
        )
    term_blocks = [
        terms[m * local_tokens : (m + 1) * local_tokens] for m in range(lax.axis_size("seq"))
    ]
    summed = ring_scatter_back(term_blocks, ring)
    grad_keys = summed[:, : H * DK].astype(jnp.bfloat16)
    grad_values = summed[:, H * DK :].astype(jnp.bfloat16)
    return (
        decoded[None],
        grad_queries.reshape(local_tokens, H * DK)[None],
        grad_keys[None],
        grad_values[None],
        grad_trunk[None],
        grad_skip[None],
        grad_weight,
    )


def solution(mesh):
    return jax.shard_map(
        functools.partial(body, ring_order(mesh)),
        mesh=mesh,
        in_specs=(
            P(("group", "dp"), "seq", None),
            P(("group", "dp"), "seq", None),
            P(("group", "dp"), "seq", None),
            P(("group", "dp"), "seq", None),
            P(("group", "dp"), "seq", None),
            P(),
            P(),
            P(("group", "dp"), "seq", None),
        ),
        out_specs=(
            P(("group", "dp"), "seq", None),
            P(("group", "dp"), "seq", None),
            P(("group", "dp"), "seq", None),
            P(("group", "dp"), "seq", None),
            P(("group", "dp"), "seq", None),
            P(("group", "dp"), "seq", None),
            P(("group", "seq", "dp"), None),
        ),
        check_vma=False,
    )
```

```python
import functools
import math

import jax
import jax.numpy as jnp
from jax import lax
from jax.sharding import PartitionSpec as P

H = 4
DK = 128
DV = 192
C = 768
CO = 384
KW = 5


def extended(array, sides, width):
    for axis, dim in sides:
        count, length = (lax.axis_size(axis), array.shape[dim])
        up = [(i, (i + 1) % count) for i in range(count - 1)]
        down = [(j, i) for i, j in up]
        last = lax.slice_in_dim(array, length - width, length, axis=dim)
        initial = lax.slice_in_dim(array, 0, width, axis=dim)
        before = lax.ppermute(last, axis, up)
        after = lax.ppermute(initial, axis, down)
        array = jnp.concatenate([before, array, after], axis=dim)
    return array


def gelu_parts(preact):
    cdf_value = 0.5 * (1.0 + jax.scipy.special.erf(preact * (1.0 / math.sqrt(2.0))))
    density = jnp.exp(-0.5 * preact * preact) * (1.0 / math.sqrt(2.0 * math.pi))
    return (preact * cdf_value, cdf_value + preact * density)


def window_rows(padded, kernel, row_count):
    return jnp.concatenate(
        [padded[offset : offset + row_count] for offset in range(kernel)], axis=1
    )


def ring_order(mesh):
    count = mesh.shape["seq"]
    try:
        row = mesh.devices.reshape(mesh.shape["group"], count, -1)[0, :, 0]
        coords = [tuple(device.coords) for device in row]
    except (AttributeError, TypeError):
        return list(range(count))
    varying = [d for d in range(3) if len({c[d] for c in coords}) > 1]
    if len(varying) == 2:
        for minor, major in (varying, varying[::-1]):
            if len({c[minor] for c in coords}) == 2:
                low = min(c[minor] for c in coords)
                first = sorted((c[major], s) for s, c in enumerate(coords) if c[minor] == low)
                second = sorted((c[major], s) for s, c in enumerate(coords) if c[minor] != low)
                return [s for _, s in first] + [s for _, s in second[::-1]]
    return list(range(count))


def ring_perms(ring):
    count = len(ring)
    forward = [(ring[q], ring[(q + 1) % count]) for q in range(count)]
    backward = [(ring[q], ring[(q - 1) % count]) for q in range(count)]
    return forward, backward


def ring_gather(block, ring):
    count = len(ring)
    forward, backward = ring_perms(ring)
    full_steps = (count - 1) // 2
    split = count % 2 == 0
    half = block.shape[1] // 2
    lefts, rights = [], []
    current = block
    for _ in range(full_steps):
        current = lax.ppermute(current, "seq", forward)
        lefts.append(current)
    if split:
        left_half = lax.ppermute(current[:, :half], "seq", forward)
    current = block
    for _ in range(full_steps):
        current = lax.ppermute(current, "seq", backward)
        rights.append(current)
    if split:
        right_half = lax.ppermute(current[:, half:], "seq", backward)
    opposite = [jnp.concatenate([left_half, right_half], axis=1)] if split else []
    return [block] + lefts + rights + opposite


def add_part(term, received, side):
    if received.shape == term.shape:
        return term + received
    half = term.shape[1] - received.shape[1] if side else received.shape[1]
    if side:
        return jnp.concatenate([term[:, :half], term[:, half:] + received], axis=1)
    return jnp.concatenate([term[:, :half] + received, term[:, half:]], axis=1)


def ring_scatter_back(blocks, ring):
    count = len(ring)
    forward, backward = ring_perms(ring)
    full_steps = (count - 1) // 2
    split = count % 2 == 0
    own = blocks[0].astype(jnp.float32)
    lefts = blocks[1 : 1 + full_steps]
    rights = blocks[1 + full_steps : 1 + 2 * full_steps]
    total = own
    for side, chain, perm in ((0, lefts, backward), (1, rights, forward)):
        if split:
            half = blocks[-1].shape[1] // 2
            acc = blocks[-1][:, half:] if side else blocks[-1][:, :half]
            top = full_steps + 1
        elif full_steps:
            acc = chain[-1]
            top = full_steps
        else:
            continue
        for t in range(top, 0, -1):
            received = lax.ppermute(acc, "seq", perm).astype(jnp.float32)
            if t == 1:
                total = add_part(total, received, side)
            else:
                acc = add_part(chain[t - 2].astype(jnp.float32), received, side).astype(
                    jnp.bfloat16
                )
    return total


def ring_reduce_scatter(blocks, axis, ring, forward_dir=True):
    count = len(ring)
    if count == 1:
        return blocks[0]
    forward, backward = ring_perms(ring)
    perm = forward if forward_dir else backward
    sign = 1 if forward_dir else -1
    position = jnp.zeros((), jnp.int32)
    index = lax.axis_index(axis)
    for q, s in enumerate(ring):
        position = jnp.where(index == s, q, position)
    offsets = (position + count - sign * jnp.arange(count, dtype=jnp.int32)) % count
    order = jnp.zeros((count,), jnp.int32)
    for q, s in enumerate(ring):
        order = jnp.where(offsets == q, s, order)
    relative = jnp.take(blocks, order, axis=0)
    acc = relative[1]
    for t in range(count - 1):
        received = lax.ppermute(acc, axis, perm)
        acc = received + relative[(t + 2) % count]
    return acc


def ring_position(axis, ring):
    position = jnp.zeros((), jnp.int32)
    index = lax.axis_index(axis)
    for q, s in enumerate(ring):
        position = jnp.where(index == s, q, position)
    return position


def ring_reduce_scatter_sliced(select_block, axis, ring, forward_dir=True, wire_dtype=jnp.bfloat16):
    count = len(ring)
    forward, backward = ring_perms(ring)
    perm = forward if forward_dir else backward
    sign = 1 if forward_dir else -1
    position = ring_position(axis, ring)

    def block_at(offset):
        target = (position + count - sign * (offset % count)) % count
        index = jnp.zeros((), jnp.int32)
        for q, s in enumerate(ring):
            index = jnp.where(target == q, s, index)
        return select_block(index)

    acc = block_at(1).astype(wire_dtype)
    for t in range(count - 1):
        received = lax.ppermute(acc, axis, perm).astype(jnp.float32)
        acc = received + block_at(t + 2)
        if t < count - 2:
            acc = acc.astype(wire_dtype)
    return acc


def body(ring, queries, key_rows, value_rows, trunk_state, skip_input, norm_gain, conv_weight, cotangent):
    score_scale = DK ** (-0.5)
    local_tokens = queries.shape[1]
    positions = 2 * local_tokens
    half_kernel = KW // 2
    query_heads = queries[0].reshape(local_tokens, H, DK)
    all_keys = jnp.concatenate(ring_gather(key_rows[0], ring), axis=0).reshape(-1, H, DK)
    all_values = jnp.concatenate(ring_gather(value_rows[0], ring), axis=0).reshape(-1, H, DV)
    scores = (
        jnp.einsum("ihd,jhd->hij", query_heads, all_keys, preferred_element_type=jnp.float32)
        * score_scale
    )
    row_peak = jnp.max(scores, axis=2, keepdims=True)
    row_total = jnp.sum(jnp.exp(scores - row_peak), axis=2, keepdims=True)
    logsum = row_peak + jnp.log(row_total)
    softmax = jnp.exp(scores - logsum)
    rounded = softmax.astype(jnp.bfloat16)
    attended = jnp.einsum(
        "hij,jhd->ihd", rounded, all_values, preferred_element_type=jnp.float32
    ).astype(jnp.bfloat16)
    upsample = (
        jnp.arange(positions, dtype=jnp.int32)[:, None] // 2
        == jnp.arange(local_tokens, dtype=jnp.int32)[None, :]
    ).astype(jnp.bfloat16)
    hidden_up = jnp.dot(
        upsample, trunk_state[0], preferred_element_type=jnp.float32
    ) + jnp.dot(
        upsample, attended.reshape(local_tokens, H * DV), preferred_element_type=jnp.float32
    )
    merged = hidden_up + skip_input[0].astype(jnp.float32)
    inverse = lax.rsqrt(jnp.mean(merged * merged, axis=1, keepdims=True) + 1e-06)
    channel_gain = norm_gain.astype(jnp.float32)
    normed = (merged * inverse * channel_gain).astype(jnp.bfloat16)
    padded = extended(normed, (("seq", 0),), half_kernel)
    columns = window_rows(padded, KW, positions)
    preact = jnp.dot(columns, conv_weight, preferred_element_type=jnp.float32)
    activated, derivative = gelu_parts(preact)
    decoded = activated.astype(jnp.bfloat16)
    grad_pre = (cotangent[0].astype(jnp.float32) * derivative).astype(jnp.bfloat16)
    grad_padded = extended(grad_pre, (("seq", 0),), half_kernel)
    norm_scale = (lax.axis_size("dp") * positions * lax.axis_size("seq")) ** (-0.5)
    seq_count, dp_count = lax.axis_size("seq"), lax.axis_size("dp")
    rows_per = KW * C // (seq_count * dp_count)
    half_co = CO // 2
    if dp_count == 2:
        partner = [(0, 1), (1, 0)]
        both_padded = jnp.stack([padded, lax.ppermute(padded, "dp", partner)])
        both_grad = jnp.stack([grad_pre, lax.ppermute(grad_pre, "dp", partner)])
        full_weight = (
            jnp.concatenate(
                [
                    jnp.einsum(
                        "spc,spo->co",
                        both_padded[:, offset : offset + positions],
                        both_grad,
                        preferred_element_type=jnp.float32,
                    )
                    for offset in range(KW)
                ],
                axis=0,
            )
            * norm_scale
        ).reshape(seq_count, dp_count, rows_per, CO)
        dp_index = lax.axis_index("dp")

        def weight_block(column, width):
            return lambda index: lax.dynamic_slice(
                full_weight, (index, dp_index, 0, column), (1, 1, rows_per, width)
            ).reshape(rows_per, width)

        grad_weight = jnp.concatenate(
            [
                ring_reduce_scatter_sliced(weight_block(0, half_co), "seq", ring, True),
                ring_reduce_scatter_sliced(
                    weight_block(half_co, CO - half_co), "seq", ring, False
                ),
            ],
            axis=1,
        )
    else:
        weight_part = (
            lax.dot_general(
                columns, grad_pre, (((0,), (0,)), ((), ())), preferred_element_type=jnp.float32
            )
            * norm_scale
        )
        weight_blocks_all = weight_part.reshape(seq_count, dp_count, -1, CO)
        dp_summed = ring_reduce_scatter(
            jnp.swapaxes(weight_blocks_all, 0, 1), "dp", list(range(dp_count))
        )
        grad_weight = jnp.concatenate(
            [
                ring_reduce_scatter(dp_summed[:, :, :half_co], "seq", ring, True),
                ring_reduce_scatter(dp_summed[:, :, half_co:], "seq", ring, False),
            ],
            axis=1,
        )
    stacked = jnp.stack(
        [
            grad_padded[2 * half_kernel - offset : 2 * half_kernel - offset + positions]
            for offset in range(KW)
        ],
        axis=1,
    )
    weight_blocks = conv_weight.reshape(KW, C, CO)
    grad_normed = jnp.einsum(
        "pko,kco->pc", stacked, weight_blocks, preferred_element_type=jnp.float32
    )
    scaled_grad = grad_normed * channel_gain
    grad_merged = inverse * scaled_grad - merged * inverse**3 * jnp.mean(
        scaled_grad * merged, axis=1, keepdims=True
    )
    grad_skip = grad_merged.astype(jnp.bfloat16)
    grad_trunk = jnp.dot(
        upsample.T.astype(jnp.float32),
        grad_merged,
        precision=lax.Precision.HIGHEST,
        preferred_element_type=jnp.float32,
    ).astype(jnp.bfloat16)
    grad_heads = grad_trunk.reshape(local_tokens, H, DV)
    row_delta = jnp.sum(grad_heads.astype(jnp.float32) * attended.astype(jnp.float32), axis=2)
    value_grad = jnp.einsum(
        "ihd,jhd->hij", grad_heads, all_values, preferred_element_type=jnp.float32
    )
    slopes = (softmax * (value_grad - row_delta.T[:, :, None])).astype(jnp.bfloat16)
    grad_queries = (
        jnp.einsum("hij,jhd->ihd", slopes, all_keys, preferred_element_type=jnp.float32)
        * score_scale
    ).astype(jnp.bfloat16)
    key_part = (
        jnp.einsum("hij,ihd->jhd", slopes, query_heads, preferred_element_type=jnp.float32)
        * score_scale
    )
    value_part = jnp.einsum("hij,ihd->jhd", rounded, grad_heads, preferred_element_type=jnp.float32)
    terms = jnp.concatenate(
        [
            key_part.reshape(-1, H * DK),
            value_part.reshape(-1, H * DV),
        ],
        axis=1,
    ).astype(jnp.bfloat16)
    term_blocks = [
        terms[m * local_tokens : (m + 1) * local_tokens] for m in range(lax.axis_size("seq"))
    ]
    summed = ring_scatter_back(term_blocks, ring)
    grad_keys = summed[:, : H * DK].astype(jnp.bfloat16)
    grad_values = summed[:, H * DK :].astype(jnp.bfloat16)
    return (
        decoded[None],
        grad_queries.reshape(local_tokens, H * DK)[None],
        grad_keys[None],
        grad_values[None],
        grad_trunk[None],
        grad_skip[None],
        grad_weight,
    )


def solution(mesh):
    return jax.shard_map(
        functools.partial(body, ring_order(mesh)),
        mesh=mesh,
        in_specs=(
            P(("group", "dp"), "seq", None),
            P(("group", "dp"), "seq", None),
            P(("group", "dp"), "seq", None),
            P(("group", "dp"), "seq", None),
            P(("group", "dp"), "seq", None),
            P(),
            P(),
            P(("group", "dp"), "seq", None),
        ),
        out_specs=(
            P(("group", "dp"), "seq", None),
            P(("group", "dp"), "seq", None),
            P(("group", "dp"), "seq", None),
            P(("group", "dp"), "seq", None),
            P(("group", "dp"), "seq", None),
            P(("group", "dp"), "seq", None),
            P(("group", "seq", "dp"), None),
        ),
        check_vma=False,
    )
```

```python
import functools
import math

import jax
import jax.numpy as jnp
from jax import lax
from jax.sharding import PartitionSpec as P

H = 4
DK = 128
DV = 192
C = 768
CO = 384
KW = 5


def extended(array, sides, width):
    for axis, dim in sides:
        count, length = (lax.axis_size(axis), array.shape[dim])
        up = [(i, (i + 1) % count) for i in range(count - 1)]
        down = [(j, i) for i, j in up]
        last = lax.slice_in_dim(array, length - width, length, axis=dim)
        initial = lax.slice_in_dim(array, 0, width, axis=dim)
        before = lax.ppermute(last, axis, up)
        after = lax.ppermute(initial, axis, down)
        array = jnp.concatenate([before, array, after], axis=dim)
    return array


def gelu_parts(preact):
    cdf_value = 0.5 * (1.0 + jax.scipy.special.erf(preact * (1.0 / math.sqrt(2.0))))
    density = jnp.exp(-0.5 * preact * preact) * (1.0 / math.sqrt(2.0 * math.pi))
    return (preact * cdf_value, cdf_value + preact * density)


def window_rows(padded, kernel, row_count):
    return jnp.concatenate(
        [padded[offset : offset + row_count] for offset in range(kernel)], axis=1
    )


def ring_order(mesh):
    count = mesh.shape["seq"]
    try:
        row = mesh.devices.reshape(mesh.shape["group"], count, -1)[0, :, 0]
        coords = [tuple(device.coords) for device in row]
    except (AttributeError, TypeError):
        return list(range(count))
    varying = [d for d in range(3) if len({c[d] for c in coords}) > 1]
    if len(varying) == 2:
        for minor, major in (varying, varying[::-1]):
            if len({c[minor] for c in coords}) == 2:
                low = min(c[minor] for c in coords)
                first = sorted((c[major], s) for s, c in enumerate(coords) if c[minor] == low)
                second = sorted((c[major], s) for s, c in enumerate(coords) if c[minor] != low)
                return [s for _, s in first] + [s for _, s in second[::-1]]
    return list(range(count))


def ring_perms(ring):
    count = len(ring)
    forward = [(ring[q], ring[(q + 1) % count]) for q in range(count)]
    backward = [(ring[q], ring[(q - 1) % count]) for q in range(count)]
    return forward, backward


def ring_gather(block, ring):
    count = len(ring)
    forward, backward = ring_perms(ring)
    full_steps = (count - 1) // 2
    split = count % 2 == 0
    half = block.shape[1] // 2
    lefts, rights = [], []
    current = block
    for _ in range(full_steps):
        current = lax.ppermute(current, "seq", forward)
        lefts.append(current)
    if split:
        left_half = lax.ppermute(current[:, :half], "seq", forward)
    current = block
    for _ in range(full_steps):
        current = lax.ppermute(current, "seq", backward)
        rights.append(current)
    if split:
        right_half = lax.ppermute(current[:, half:], "seq", backward)
    opposite = [jnp.concatenate([left_half, right_half], axis=1)] if split else []
    return [block] + lefts + rights + opposite


def add_part(term, received, side):
    if received.shape == term.shape:
        return term + received
    half = term.shape[1] - received.shape[1] if side else received.shape[1]
    if side:
        return jnp.concatenate([term[:, :half], term[:, half:] + received], axis=1)
    return jnp.concatenate([term[:, :half] + received, term[:, half:]], axis=1)


def ring_scatter_back(blocks, ring):
    count = len(ring)
    forward, backward = ring_perms(ring)
    full_steps = (count - 1) // 2
    split = count % 2 == 0
    own = blocks[0].astype(jnp.float32)
    lefts = blocks[1 : 1 + full_steps]
    rights = blocks[1 + full_steps : 1 + 2 * full_steps]
    total = own
    for side, chain, perm in ((0, lefts, backward), (1, rights, forward)):
        if split:
            half = blocks[-1].shape[1] // 2
            acc = blocks[-1][:, half:] if side else blocks[-1][:, :half]
            top = full_steps + 1
        elif full_steps:
            acc = chain[-1]
            top = full_steps
        else:
            continue
        for t in range(top, 0, -1):
            received = lax.ppermute(acc, "seq", perm).astype(jnp.float32)
            if t == 1:
                total = add_part(total, received, side)
            else:
                acc = add_part(chain[t - 2].astype(jnp.float32), received, side).astype(
                    jnp.bfloat16
                )
    return total


def ring_reduce_scatter(blocks, axis, ring, forward_dir=True):
    count = len(ring)
    if count == 1:
        return blocks[0]
    forward, backward = ring_perms(ring)
    perm = forward if forward_dir else backward
    sign = 1 if forward_dir else -1
    position = jnp.zeros((), jnp.int32)
    index = lax.axis_index(axis)
    for q, s in enumerate(ring):
        position = jnp.where(index == s, q, position)
    offsets = (position + count - sign * jnp.arange(count, dtype=jnp.int32)) % count
    order = jnp.zeros((count,), jnp.int32)
    for q, s in enumerate(ring):
        order = jnp.where(offsets == q, s, order)
    relative = jnp.take(blocks, order, axis=0)
    acc = relative[1]
    for t in range(count - 1):
        received = lax.ppermute(acc, axis, perm)
        acc = received + relative[(t + 2) % count]
    return acc


def ring_position(axis, ring):
    position = jnp.zeros((), jnp.int32)
    index = lax.axis_index(axis)
    for q, s in enumerate(ring):
        position = jnp.where(index == s, q, position)
    return position


def ring_reduce_scatter_sliced(select_block, axis, ring, forward_dir=True, wire_dtype=jnp.bfloat16):
    count = len(ring)
    forward, backward = ring_perms(ring)
    perm = forward if forward_dir else backward
    sign = 1 if forward_dir else -1
    position = ring_position(axis, ring)

    def block_at(offset):
        target = (position + count - sign * (offset % count)) % count
        index = jnp.zeros((), jnp.int32)
        for q, s in enumerate(ring):
            index = jnp.where(target == q, s, index)
        return select_block(index)

    acc = block_at(1).astype(wire_dtype)
    for t in range(count - 1):
        received = lax.ppermute(acc, axis, perm).astype(jnp.float32)
        acc = received + block_at(t + 2)
        if t < count - 2:
            acc = acc.astype(wire_dtype)
    return acc


def body(ring, queries, key_rows, value_rows, trunk_state, skip_input, norm_gain, conv_weight, cotangent):
    score_scale = DK ** (-0.5)
    local_tokens = queries.shape[1]
    positions = 2 * local_tokens
    half_kernel = KW // 2
    query_heads = queries[0].reshape(local_tokens, H, DK)
    key_value_blocks = ring_gather(jnp.concatenate([key_rows[0], value_rows[0]], axis=1), ring)
    gathered = jnp.concatenate(key_value_blocks, axis=0)
    all_keys = gathered[:, : H * DK].reshape(-1, H, DK)
    all_values = gathered[:, H * DK :].reshape(-1, H, DV)
    scores = (
        jnp.einsum("ihd,jhd->hij", query_heads, all_keys, preferred_element_type=jnp.float32)
        * score_scale
    )
    row_peak = jnp.max(scores, axis=2, keepdims=True)
    row_total = jnp.sum(jnp.exp(scores - row_peak), axis=2, keepdims=True)
    logsum = row_peak + jnp.log(row_total)
    softmax = jnp.exp(scores - logsum)
    rounded = softmax.astype(jnp.bfloat16)
    attended = jnp.einsum(
        "hij,jhd->ihd", rounded, all_values, preferred_element_type=jnp.float32
    ).astype(jnp.bfloat16)
    upsample = (
        jnp.arange(positions, dtype=jnp.int32)[:, None] // 2
        == jnp.arange(local_tokens, dtype=jnp.int32)[None, :]
    ).astype(jnp.bfloat16)
    hidden_up = jnp.dot(
        upsample, trunk_state[0], preferred_element_type=jnp.float32
    ) + jnp.dot(
        upsample, attended.reshape(local_tokens, H * DV), preferred_element_type=jnp.float32
    )
    merged = hidden_up + skip_input[0].astype(jnp.float32)
    inverse = lax.rsqrt(jnp.mean(merged * merged, axis=1, keepdims=True) + 1e-06)
    channel_gain = norm_gain.astype(jnp.float32)
    normed = (merged * inverse * channel_gain).astype(jnp.bfloat16)
    padded = extended(normed, (("seq", 0),), half_kernel)
    columns = window_rows(padded, KW, positions)
    preact = jnp.dot(columns, conv_weight, preferred_element_type=jnp.float32)
    activated, derivative = gelu_parts(preact)
    decoded = activated.astype(jnp.bfloat16)
    grad_pre = (cotangent[0].astype(jnp.float32) * derivative).astype(jnp.bfloat16)
    grad_padded = extended(grad_pre, (("seq", 0),), half_kernel)
    norm_scale = (lax.axis_size("dp") * positions * lax.axis_size("seq")) ** (-0.5)
    seq_count, dp_count = lax.axis_size("seq"), lax.axis_size("dp")
    rows_per = KW * C // (seq_count * dp_count)
    half_co = CO // 2
    if dp_count == 2:
        partner = [(0, 1), (1, 0)]
        both_padded = jnp.stack([padded, lax.ppermute(padded, "dp", partner)])
        both_grad = jnp.stack([grad_pre, lax.ppermute(grad_pre, "dp", partner)])
        full_weight = (
            jnp.concatenate(
                [
                    jnp.einsum(
                        "spc,spo->co",
                        both_padded[:, offset : offset + positions],
                        both_grad,
                        preferred_element_type=jnp.float32,
                    )
                    for offset in range(KW)
                ],
                axis=0,
            )
            * norm_scale
        ).reshape(seq_count, dp_count, rows_per, CO)
        dp_index = lax.axis_index("dp")

        def weight_block(column, width):
            return lambda index: lax.dynamic_slice(
                full_weight, (index, dp_index, 0, column), (1, 1, rows_per, width)
            ).reshape(rows_per, width)

        grad_weight = ring_reduce_scatter_sliced(weight_block(0, CO), "seq", ring, True)
    else:
        weight_part = (
            lax.dot_general(
                columns, grad_pre, (((0,), (0,)), ((), ())), preferred_element_type=jnp.float32
            )
            * norm_scale
        )
        weight_blocks_all = weight_part.reshape(seq_count, dp_count, -1, CO)
        dp_summed = ring_reduce_scatter(
            jnp.swapaxes(weight_blocks_all, 0, 1), "dp", list(range(dp_count))
        )
        grad_weight = jnp.concatenate(
            [
                ring_reduce_scatter(dp_summed[:, :, :half_co], "seq", ring, True),
                ring_reduce_scatter(dp_summed[:, :, half_co:], "seq", ring, False),
            ],
            axis=1,
        )
    stacked = jnp.stack(
        [
            grad_padded[2 * half_kernel - offset : 2 * half_kernel - offset + positions]
            for offset in range(KW)
        ],
        axis=1,
    )
    weight_blocks = conv_weight.reshape(KW, C, CO)
    grad_normed = jnp.einsum(
        "pko,kco->pc", stacked, weight_blocks, preferred_element_type=jnp.float32
    )
    scaled_grad = grad_normed * channel_gain
    grad_merged = inverse * scaled_grad - merged * inverse**3 * jnp.mean(
        scaled_grad * merged, axis=1, keepdims=True
    )
    grad_skip = grad_merged.astype(jnp.bfloat16)
    grad_trunk = jnp.dot(
        upsample.T.astype(jnp.float32),
        grad_merged,
        precision=lax.Precision.HIGHEST,
        preferred_element_type=jnp.float32,
    ).astype(jnp.bfloat16)
    grad_heads = grad_trunk.reshape(local_tokens, H, DV)
    row_delta = jnp.sum(grad_heads.astype(jnp.float32) * attended.astype(jnp.float32), axis=2)
    value_grad = jnp.einsum(
        "ihd,jhd->hij", grad_heads, all_values, preferred_element_type=jnp.float32
    )
    slopes = (softmax * (value_grad - row_delta.T[:, :, None])).astype(jnp.bfloat16)
    grad_queries = (
        jnp.einsum("hij,jhd->ihd", slopes, all_keys, preferred_element_type=jnp.float32)
        * score_scale
    ).astype(jnp.bfloat16)
    key_part = (
        jnp.einsum("hij,ihd->jhd", slopes, query_heads, preferred_element_type=jnp.float32)
        * score_scale
    )
    value_part = jnp.einsum("hij,ihd->jhd", rounded, grad_heads, preferred_element_type=jnp.float32)
    terms = jnp.concatenate(
        [
            key_part.reshape(-1, H * DK),
            value_part.reshape(-1, H * DV),
        ],
        axis=1,
    ).astype(jnp.bfloat16)
    term_blocks = [
        terms[m * local_tokens : (m + 1) * local_tokens] for m in range(lax.axis_size("seq"))
    ]
    summed = ring_scatter_back(term_blocks, ring)
    grad_keys = summed[:, : H * DK].astype(jnp.bfloat16)
    grad_values = summed[:, H * DK :].astype(jnp.bfloat16)
    return (
        decoded[None],
        grad_queries.reshape(local_tokens, H * DK)[None],
        grad_keys[None],
        grad_values[None],
        grad_trunk[None],
        grad_skip[None],
        grad_weight,
    )


def solution(mesh):
    return jax.shard_map(
        functools.partial(body, ring_order(mesh)),
        mesh=mesh,
        in_specs=(
            P(("group", "dp"), "seq", None),
            P(("group", "dp"), "seq", None),
            P(("group", "dp"), "seq", None),
            P(("group", "dp"), "seq", None),
            P(("group", "dp"), "seq", None),
            P(),
            P(),
            P(("group", "dp"), "seq", None),
        ),
        out_specs=(
            P(("group", "dp"), "seq", None),
            P(("group", "dp"), "seq", None),
            P(("group", "dp"), "seq", None),
            P(("group", "dp"), "seq", None),
            P(("group", "dp"), "seq", None),
            P(("group", "dp"), "seq", None),
            P(("group", "seq", "dp"), None),
        ),
        check_vma=False,
    )
```

```python
import functools
import math

import jax
import jax.numpy as jnp
from jax import lax
from jax.sharding import PartitionSpec as P

H = 4
DK = 128
DV = 192
C = 768
CO = 384
KW = 5


def extended(array, sides, width):
    for axis, dim in sides:
        count, length = (lax.axis_size(axis), array.shape[dim])
        up = [(i, (i + 1) % count) for i in range(count - 1)]
        down = [(j, i) for i, j in up]
        last = lax.slice_in_dim(array, length - width, length, axis=dim)
        initial = lax.slice_in_dim(array, 0, width, axis=dim)
        before = lax.ppermute(last, axis, up)
        after = lax.ppermute(initial, axis, down)
        array = jnp.concatenate([before, array, after], axis=dim)
    return array


def gelu_parts(preact):
    cdf_value = 0.5 * (1.0 + jax.scipy.special.erf(preact * (1.0 / math.sqrt(2.0))))
    density = jnp.exp(-0.5 * preact * preact) * (1.0 / math.sqrt(2.0 * math.pi))
    return (preact * cdf_value, cdf_value + preact * density)


def window_rows(padded, kernel, row_count):
    return jnp.concatenate(
        [padded[offset : offset + row_count] for offset in range(kernel)], axis=1
    )


def ring_order(mesh):
    count = mesh.shape["seq"]
    try:
        row = mesh.devices.reshape(mesh.shape["group"], count, -1)[0, :, 0]
        coords = [tuple(device.coords) for device in row]
    except (AttributeError, TypeError):
        return list(range(count))
    varying = [d for d in range(3) if len({c[d] for c in coords}) > 1]
    if len(varying) == 2:
        for minor, major in (varying, varying[::-1]):
            if len({c[minor] for c in coords}) == 2:
                low = min(c[minor] for c in coords)
                first = sorted((c[major], s) for s, c in enumerate(coords) if c[minor] == low)
                second = sorted((c[major], s) for s, c in enumerate(coords) if c[minor] != low)
                return [s for _, s in first] + [s for _, s in second[::-1]]
    return list(range(count))


def ring_perms(ring):
    count = len(ring)
    forward = [(ring[q], ring[(q + 1) % count]) for q in range(count)]
    backward = [(ring[q], ring[(q - 1) % count]) for q in range(count)]
    return forward, backward


def ring_gather(block, ring):
    count = len(ring)
    forward, backward = ring_perms(ring)
    full_steps = (count - 1) // 2
    split = count % 2 == 0
    half = block.shape[1] // 2
    lefts, rights = [], []
    current = block
    for _ in range(full_steps):
        current = lax.ppermute(current, "seq", forward)
        lefts.append(current)
    if split:
        left_half = lax.ppermute(current[:, :half], "seq", forward)
    current = block
    for _ in range(full_steps):
        current = lax.ppermute(current, "seq", backward)
        rights.append(current)
    if split:
        right_half = lax.ppermute(current[:, half:], "seq", backward)
    opposite = [jnp.concatenate([left_half, right_half], axis=1)] if split else []
    return [block] + lefts + rights + opposite


def add_part(term, received, side):
    if received.shape == term.shape:
        return term + received
    half = term.shape[1] - received.shape[1] if side else received.shape[1]
    if side:
        return jnp.concatenate([term[:, :half], term[:, half:] + received], axis=1)
    return jnp.concatenate([term[:, :half] + received, term[:, half:]], axis=1)


def ring_scatter_back(blocks, ring):
    count = len(ring)
    forward, backward = ring_perms(ring)
    full_steps = (count - 1) // 2
    split = count % 2 == 0
    own = blocks[0].astype(jnp.float32)
    lefts = blocks[1 : 1 + full_steps]
    rights = blocks[1 + full_steps : 1 + 2 * full_steps]
    total = own
    for side, chain, perm in ((0, lefts, backward), (1, rights, forward)):
        if split:
            half = blocks[-1].shape[1] // 2
            acc = blocks[-1][:, half:] if side else blocks[-1][:, :half]
            top = full_steps + 1
        elif full_steps:
            acc = chain[-1]
            top = full_steps
        else:
            continue
        for t in range(top, 0, -1):
            received = lax.ppermute(acc, "seq", perm).astype(jnp.float32)
            if t == 1:
                total = add_part(total, received, side)
            else:
                acc = add_part(chain[t - 2].astype(jnp.float32), received, side).astype(
                    jnp.bfloat16
                )
    return total


def ring_reduce_scatter(blocks, axis, ring, forward_dir=True):
    count = len(ring)
    if count == 1:
        return blocks[0]
    forward, backward = ring_perms(ring)
    perm = forward if forward_dir else backward
    sign = 1 if forward_dir else -1
    position = jnp.zeros((), jnp.int32)
    index = lax.axis_index(axis)
    for q, s in enumerate(ring):
        position = jnp.where(index == s, q, position)
    offsets = (position + count - sign * jnp.arange(count, dtype=jnp.int32)) % count
    order = jnp.zeros((count,), jnp.int32)
    for q, s in enumerate(ring):
        order = jnp.where(offsets == q, s, order)
    relative = jnp.take(blocks, order, axis=0)
    acc = relative[1]
    for t in range(count - 1):
        received = lax.ppermute(acc, axis, perm)
        acc = received + relative[(t + 2) % count]
    return acc


def ring_position(axis, ring):
    position = jnp.zeros((), jnp.int32)
    index = lax.axis_index(axis)
    for q, s in enumerate(ring):
        position = jnp.where(index == s, q, position)
    return position


def ring_reduce_scatter_sliced(select_block, axis, ring, forward_dir=True, wire_dtype=jnp.bfloat16):
    count = len(ring)
    forward, backward = ring_perms(ring)
    perm = forward if forward_dir else backward
    sign = 1 if forward_dir else -1
    position = ring_position(axis, ring)

    def block_at(offset):
        target = (position + count - sign * (offset % count)) % count
        index = jnp.zeros((), jnp.int32)
        for q, s in enumerate(ring):
            index = jnp.where(target == q, s, index)
        return select_block(index)

    acc = block_at(1).astype(wire_dtype)
    for t in range(count - 1):
        received = lax.ppermute(acc, axis, perm).astype(jnp.float32)
        acc = received + block_at(t + 2)
        if t < count - 2:
            acc = acc.astype(wire_dtype)
    return acc


def body(ring, queries, key_rows, value_rows, trunk_state, skip_input, norm_gain, conv_weight, cotangent):
    score_scale = DK ** (-0.5)
    local_tokens = queries.shape[1]
    positions = 2 * local_tokens
    half_kernel = KW // 2
    query_heads = queries[0].reshape(local_tokens, H, DK)
    key_value_blocks = ring_gather(jnp.concatenate([key_rows[0], value_rows[0]], axis=1), ring)
    gathered = jnp.concatenate(key_value_blocks, axis=0)
    all_keys = gathered[:, : H * DK].reshape(-1, H, DK)
    all_values = gathered[:, H * DK :].reshape(-1, H, DV)
    scores = (
        jnp.einsum("ihd,jhd->hij", query_heads, all_keys, preferred_element_type=jnp.float32)
        * score_scale
    )
    row_peak = jnp.max(scores, axis=2, keepdims=True)
    row_total = jnp.sum(jnp.exp(scores - row_peak), axis=2, keepdims=True)
    logsum = row_peak + jnp.log(row_total)
    softmax = jnp.exp(scores - logsum)
    rounded = softmax.astype(jnp.bfloat16)
    attended = jnp.einsum(
        "hij,jhd->ihd", rounded, all_values, preferred_element_type=jnp.float32
    ).astype(jnp.bfloat16)
    upsample = (
        jnp.arange(positions, dtype=jnp.int32)[:, None] // 2
        == jnp.arange(local_tokens, dtype=jnp.int32)[None, :]
    ).astype(jnp.bfloat16)
    hidden_up = jnp.dot(
        upsample, trunk_state[0], preferred_element_type=jnp.float32
    ) + jnp.dot(
        upsample, attended.reshape(local_tokens, H * DV), preferred_element_type=jnp.float32
    )
    merged = hidden_up + skip_input[0].astype(jnp.float32)
    inverse = lax.rsqrt(jnp.mean(merged * merged, axis=1, keepdims=True) + 1e-06)
    channel_gain = norm_gain.astype(jnp.float32)
    normed = (merged * inverse * channel_gain).astype(jnp.bfloat16)
    padded = extended(normed, (("seq", 0),), half_kernel)
    columns = window_rows(padded, KW, positions)
    preact = jnp.dot(columns, conv_weight, preferred_element_type=jnp.float32)
    activated, derivative = gelu_parts(preact)
    decoded = activated.astype(jnp.bfloat16)
    grad_pre = (cotangent[0].astype(jnp.float32) * derivative).astype(jnp.bfloat16)
    grad_padded = extended(grad_pre, (("seq", 0),), half_kernel)
    norm_scale = (lax.axis_size("dp") * positions * lax.axis_size("seq")) ** (-0.5)
    seq_count, dp_count = lax.axis_size("seq"), lax.axis_size("dp")
    rows_per = KW * C // (seq_count * dp_count)
    half_co = CO // 2
    if dp_count == 2:
        partner = [(0, 1), (1, 0)]
        both_padded = jnp.stack([padded, lax.ppermute(padded, "dp", partner)])
        both_grad = jnp.stack([grad_pre, lax.ppermute(grad_pre, "dp", partner)])
        full_weight = (
            jnp.concatenate(
                [
                    jnp.einsum(
                        "spc,spo->co",
                        both_padded[:, offset : offset + positions],
                        both_grad,
                        preferred_element_type=jnp.float32,
                    )
                    for offset in range(KW)
                ],
                axis=0,
            )
            * norm_scale
        ).astype(jnp.bfloat16).reshape(seq_count, dp_count, rows_per, CO)
        dp_index = lax.axis_index("dp")

        def weight_block(column, width):
            return lambda index: lax.dynamic_slice(
                full_weight, (index, dp_index, 0, column), (1, 1, rows_per, width)
            ).reshape(rows_per, width)

        grad_weight = jnp.concatenate(
            [
                ring_reduce_scatter_sliced(weight_block(0, half_co), "seq", ring, True),
                ring_reduce_scatter_sliced(
                    weight_block(half_co, CO - half_co), "seq", ring, False
                ),
            ],
            axis=1,
        )
    else:
        weight_part = (
            lax.dot_general(
                columns, grad_pre, (((0,), (0,)), ((), ())), preferred_element_type=jnp.float32
            )
            * norm_scale
        )
        weight_blocks_all = weight_part.reshape(seq_count, dp_count, -1, CO)
        dp_summed = ring_reduce_scatter(
            jnp.swapaxes(weight_blocks_all, 0, 1), "dp", list(range(dp_count))
        )
        grad_weight = jnp.concatenate(
            [
                ring_reduce_scatter(dp_summed[:, :, :half_co], "seq", ring, True),
                ring_reduce_scatter(dp_summed[:, :, half_co:], "seq", ring, False),
            ],
            axis=1,
        )
    stacked = jnp.stack(
        [
            grad_padded[2 * half_kernel - offset : 2 * half_kernel - offset + positions]
            for offset in range(KW)
        ],
        axis=1,
    )
    weight_blocks = conv_weight.reshape(KW, C, CO)
    grad_normed = jnp.einsum(
        "pko,kco->pc", stacked, weight_blocks, preferred_element_type=jnp.float32
    )
    scaled_grad = grad_normed * channel_gain
    grad_merged = inverse * scaled_grad - merged * inverse**3 * jnp.mean(
        scaled_grad * merged, axis=1, keepdims=True
    )
    grad_skip = grad_merged.astype(jnp.bfloat16)
    grad_trunk = jnp.dot(
        upsample.T.astype(jnp.float32),
        grad_merged,
        precision=lax.Precision.HIGHEST,
        preferred_element_type=jnp.float32,
    ).astype(jnp.bfloat16)
    grad_heads = grad_trunk.reshape(local_tokens, H, DV)
    row_delta = jnp.sum(grad_heads.astype(jnp.float32) * attended.astype(jnp.float32), axis=2)
    value_grad = jnp.einsum(
        "ihd,jhd->hij", grad_heads, all_values, preferred_element_type=jnp.float32
    )
    slopes = (softmax * (value_grad - row_delta.T[:, :, None])).astype(jnp.bfloat16)
    grad_queries = (
        jnp.einsum("hij,jhd->ihd", slopes, all_keys, preferred_element_type=jnp.float32)
        * score_scale
    ).astype(jnp.bfloat16)
    key_part = (
        jnp.einsum("hij,ihd->jhd", slopes, query_heads, preferred_element_type=jnp.float32)
        * score_scale
    )
    value_part = jnp.einsum("hij,ihd->jhd", rounded, grad_heads, preferred_element_type=jnp.float32)
    terms = jnp.concatenate(
        [
            key_part.reshape(-1, H * DK),
            value_part.reshape(-1, H * DV),
        ],
        axis=1,
    ).astype(jnp.bfloat16)
    term_blocks = [
        terms[m * local_tokens : (m + 1) * local_tokens] for m in range(lax.axis_size("seq"))
    ]
    summed = ring_scatter_back(term_blocks, ring)
    grad_keys = summed[:, : H * DK].astype(jnp.bfloat16)
    grad_values = summed[:, H * DK :].astype(jnp.bfloat16)
    return (
        decoded[None],
        grad_queries.reshape(local_tokens, H * DK)[None],
        grad_keys[None],
        grad_values[None],
        grad_trunk[None],
        grad_skip[None],
        grad_weight,
    )


def solution(mesh):
    return jax.shard_map(
        functools.partial(body, ring_order(mesh)),
        mesh=mesh,
        in_specs=(
            P(("group", "dp"), "seq", None),
            P(("group", "dp"), "seq", None),
            P(("group", "dp"), "seq", None),
            P(("group", "dp"), "seq", None),
            P(("group", "dp"), "seq", None),
            P(),
            P(),
            P(("group", "dp"), "seq", None),
        ),
        out_specs=(
            P(("group", "dp"), "seq", None),
            P(("group", "dp"), "seq", None),
            P(("group", "dp"), "seq", None),
            P(("group", "dp"), "seq", None),
            P(("group", "dp"), "seq", None),
            P(("group", "dp"), "seq", None),
            P(("group", "seq", "dp"), None),
        ),
        check_vma=False,
    )
```

```python
import functools
import math

import jax
import jax.numpy as jnp
from jax import lax
from jax.sharding import PartitionSpec as P

H = 4
DK = 128
DV = 192
C = 768
CO = 384
KW = 5


def extended(array, sides, width):
    for axis, dim in sides:
        count, length = (lax.axis_size(axis), array.shape[dim])
        up = [(i, (i + 1) % count) for i in range(count - 1)]
        down = [(j, i) for i, j in up]
        last = lax.slice_in_dim(array, length - width, length, axis=dim)
        initial = lax.slice_in_dim(array, 0, width, axis=dim)
        before = lax.ppermute(last, axis, up)
        after = lax.ppermute(initial, axis, down)
        array = jnp.concatenate([before, array, after], axis=dim)
    return array


def gelu_parts(preact):
    cdf_value = 0.5 * (1.0 + jax.scipy.special.erf(preact * (1.0 / math.sqrt(2.0))))
    density = jnp.exp(-0.5 * preact * preact) * (1.0 / math.sqrt(2.0 * math.pi))
    return (preact * cdf_value, cdf_value + preact * density)


def window_rows(padded, kernel, row_count):
    return jnp.concatenate(
        [padded[offset : offset + row_count] for offset in range(kernel)], axis=1
    )


def ring_order(mesh):
    count = mesh.shape["seq"]
    try:
        row = mesh.devices.reshape(mesh.shape["group"], count, -1)[0, :, 0]
        coords = [tuple(device.coords) for device in row]
    except (AttributeError, TypeError):
        return list(range(count))
    varying = [d for d in range(3) if len({c[d] for c in coords}) > 1]
    if len(varying) == 2:
        for minor, major in (varying, varying[::-1]):
            if len({c[minor] for c in coords}) == 2:
                low = min(c[minor] for c in coords)
                first = sorted((c[major], s) for s, c in enumerate(coords) if c[minor] == low)
                second = sorted((c[major], s) for s, c in enumerate(coords) if c[minor] != low)
                return [s for _, s in first] + [s for _, s in second[::-1]]
    return list(range(count))


def ring_perms(ring):
    count = len(ring)
    forward = [(ring[q], ring[(q + 1) % count]) for q in range(count)]
    backward = [(ring[q], ring[(q - 1) % count]) for q in range(count)]
    return forward, backward


def ring_gather(block, ring):
    count = len(ring)
    forward, backward = ring_perms(ring)
    full_steps = (count - 1) // 2
    split = count % 2 == 0
    half = block.shape[1] // 2
    lefts, rights = [], []
    current = block
    for _ in range(full_steps):
        current = lax.ppermute(current, "seq", forward)
        lefts.append(current)
    if split:
        left_half = lax.ppermute(current[:, :half], "seq", forward)
    current = block
    for _ in range(full_steps):
        current = lax.ppermute(current, "seq", backward)
        rights.append(current)
    if split:
        right_half = lax.ppermute(current[:, half:], "seq", backward)
    opposite = [jnp.concatenate([left_half, right_half], axis=1)] if split else []
    return [block] + lefts + rights + opposite


def add_part(term, received, side):
    if received.shape == term.shape:
        return term + received
    half = term.shape[1] - received.shape[1] if side else received.shape[1]
    if side:
        return jnp.concatenate([term[:, :half], term[:, half:] + received], axis=1)
    return jnp.concatenate([term[:, :half] + received, term[:, half:]], axis=1)


def ring_scatter_back(blocks, ring):
    count = len(ring)
    forward, backward = ring_perms(ring)
    full_steps = (count - 1) // 2
    split = count % 2 == 0
    own = blocks[0].astype(jnp.float32)
    lefts = blocks[1 : 1 + full_steps]
    rights = blocks[1 + full_steps : 1 + 2 * full_steps]
    total = own
    for side, chain, perm in ((0, lefts, backward), (1, rights, forward)):
        if split:
            half = blocks[-1].shape[1] // 2
            acc = blocks[-1][:, half:] if side else blocks[-1][:, :half]
            top = full_steps + 1
        elif full_steps:
            acc = chain[-1]
            top = full_steps
        else:
            continue
        for t in range(top, 0, -1):
            received = lax.ppermute(acc, "seq", perm).astype(jnp.float32)
            if t == 1:
                total = add_part(total, received, side)
            else:
                acc = add_part(chain[t - 2].astype(jnp.float32), received, side).astype(
                    jnp.bfloat16
                )
    return total


def ring_reduce_scatter(blocks, axis, ring, forward_dir=True):
    count = len(ring)
    if count == 1:
        return blocks[0]
    forward, backward = ring_perms(ring)
    perm = forward if forward_dir else backward
    sign = 1 if forward_dir else -1
    position = jnp.zeros((), jnp.int32)
    index = lax.axis_index(axis)
    for q, s in enumerate(ring):
        position = jnp.where(index == s, q, position)
    offsets = (position + count - sign * jnp.arange(count, dtype=jnp.int32)) % count
    order = jnp.zeros((count,), jnp.int32)
    for q, s in enumerate(ring):
        order = jnp.where(offsets == q, s, order)
    relative = jnp.take(blocks, order, axis=0)
    acc = relative[1]
    for t in range(count - 1):
        received = lax.ppermute(acc, axis, perm)
        acc = received + relative[(t + 2) % count]
    return acc


def ring_position(axis, ring):
    position = jnp.zeros((), jnp.int32)
    index = lax.axis_index(axis)
    for q, s in enumerate(ring):
        position = jnp.where(index == s, q, position)
    return position


def ring_reduce_scatter_sliced(select_block, axis, ring, forward_dir=True, wire_dtype=jnp.bfloat16):
    count = len(ring)
    forward, backward = ring_perms(ring)
    perm = forward if forward_dir else backward
    sign = 1 if forward_dir else -1
    position = ring_position(axis, ring)

    def block_at(offset):
        target = (position + count - sign * (offset % count)) % count
        index = jnp.zeros((), jnp.int32)
        for q, s in enumerate(ring):
            index = jnp.where(target == q, s, index)
        return select_block(index)

    acc = block_at(1).astype(wire_dtype)
    for t in range(count - 1):
        received = lax.ppermute(acc, axis, perm).astype(jnp.float32)
        acc = received + block_at(t + 2)
        if t < count - 2:
            acc = acc.astype(wire_dtype)
    return acc


def body(ring, queries, key_rows, value_rows, trunk_state, skip_input, norm_gain, conv_weight, cotangent):
    score_scale = DK ** (-0.5)
    local_tokens = queries.shape[1]
    positions = 2 * local_tokens
    half_kernel = KW // 2
    query_heads = queries[0].reshape(local_tokens, H, DK)
    key_value_blocks = ring_gather(jnp.concatenate([key_rows[0], value_rows[0]], axis=1), ring)
    gathered = jnp.concatenate(key_value_blocks, axis=0)
    all_keys = gathered[:, : H * DK].reshape(-1, H, DK)
    all_values = gathered[:, H * DK :].reshape(-1, H, DV)
    scores = (
        jnp.einsum("ihd,jhd->hij", query_heads, all_keys, preferred_element_type=jnp.float32)
        * score_scale
    )
    row_peak = jnp.max(scores, axis=2, keepdims=True)
    row_total = jnp.sum(jnp.exp(scores - row_peak), axis=2, keepdims=True)
    logsum = row_peak + jnp.log(row_total)
    softmax = jnp.exp(scores - logsum)
    rounded = softmax.astype(jnp.bfloat16)
    attended = jnp.einsum(
        "hij,jhd->ihd", rounded, all_values, preferred_element_type=jnp.float32
    ).astype(jnp.bfloat16)
    upsample = (
        jnp.arange(positions, dtype=jnp.int32)[:, None] // 2
        == jnp.arange(local_tokens, dtype=jnp.int32)[None, :]
    ).astype(jnp.bfloat16)
    hidden_up = jnp.dot(
        upsample, trunk_state[0], preferred_element_type=jnp.float32
    ) + jnp.dot(
        upsample, attended.reshape(local_tokens, H * DV), preferred_element_type=jnp.float32
    )
    merged = hidden_up + skip_input[0].astype(jnp.float32)
    inverse = lax.rsqrt(jnp.mean(merged * merged, axis=1, keepdims=True) + 1e-06)
    channel_gain = norm_gain.astype(jnp.float32)
    normed = (merged * inverse * channel_gain).astype(jnp.bfloat16)
    padded = extended(normed, (("seq", 0),), half_kernel)
    columns = window_rows(padded, KW, positions)
    preact = jnp.dot(columns, conv_weight, preferred_element_type=jnp.float32)
    activated, derivative = gelu_parts(preact)
    decoded = activated.astype(jnp.bfloat16)
    grad_pre = (cotangent[0].astype(jnp.float32) * derivative).astype(jnp.bfloat16)
    grad_padded = extended(grad_pre, (("seq", 0),), half_kernel)
    norm_scale = (lax.axis_size("dp") * positions * lax.axis_size("seq")) ** (-0.5)
    seq_count, dp_count = lax.axis_size("seq"), lax.axis_size("dp")
    rows_per = KW * C // (seq_count * dp_count)
    half_co = CO // 2
    if dp_count == 2:
        partner = [(0, 1), (1, 0)]
        both_padded = jnp.stack([padded, lax.ppermute(padded, "dp", partner)])
        both_grad = jnp.stack([grad_pre, lax.ppermute(grad_pre, "dp", partner)])
        full_weight = (
            jnp.concatenate(
                [
                    jnp.einsum(
                        "spc,spo->co",
                        both_padded[:, offset : offset + positions],
                        both_grad,
                        preferred_element_type=jnp.float32,
                    )
                    for offset in range(KW)
                ],
                axis=0,
            )
            * norm_scale
        ).reshape(seq_count, dp_count, rows_per, CO)
        dp_index = lax.axis_index("dp")

        def weight_block(column, width):
            return lambda index: lax.dynamic_slice(
                full_weight, (index, dp_index, 0, column), (1, 1, rows_per, width)
            ).reshape(rows_per, width)

        grad_weight = jnp.concatenate(
            [
                ring_reduce_scatter_sliced(weight_block(0, half_co), "seq", ring, True),
                ring_reduce_scatter_sliced(
                    weight_block(half_co, CO - half_co), "seq", ring, False
                ),
            ],
            axis=1,
        )
    else:
        weight_part = (
            lax.dot_general(
                columns, grad_pre, (((0,), (0,)), ((), ())), preferred_element_type=jnp.float32
            )
            * norm_scale
        )
        weight_blocks_all = weight_part.reshape(seq_count, dp_count, -1, CO)
        dp_summed = ring_reduce_scatter(
            jnp.swapaxes(weight_blocks_all, 0, 1), "dp", list(range(dp_count))
        )
        grad_weight = jnp.concatenate(
            [
                ring_reduce_scatter(dp_summed[:, :, :half_co], "seq", ring, True),
                ring_reduce_scatter(dp_summed[:, :, half_co:], "seq", ring, False),
            ],
            axis=1,
        )
    stacked = jnp.stack(
        [
            grad_padded[2 * half_kernel - offset : 2 * half_kernel - offset + positions]
            for offset in range(KW)
        ],
        axis=1,
    )
    weight_blocks = conv_weight.reshape(KW, C, CO)
    grad_normed = jnp.einsum(
        "pko,kco->pc", stacked, weight_blocks, preferred_element_type=jnp.float32
    )
    scaled_grad = grad_normed * channel_gain
    grad_merged = inverse * scaled_grad - merged * inverse**3 * jnp.mean(
        scaled_grad * merged, axis=1, keepdims=True
    )
    grad_skip = grad_merged.astype(jnp.bfloat16)
    paired = grad_merged.reshape(local_tokens, 2 * C)
    grad_trunk = (paired[:, :C] + paired[:, C:]).astype(jnp.bfloat16)
    grad_heads = grad_trunk.reshape(local_tokens, H, DV)
    row_delta = jnp.sum(grad_heads.astype(jnp.float32) * attended.astype(jnp.float32), axis=2)
    value_grad = jnp.einsum(
        "ihd,jhd->hij", grad_heads, all_values, preferred_element_type=jnp.float32
    )
    slopes = (softmax * (value_grad - row_delta.T[:, :, None])).astype(jnp.bfloat16)
    grad_queries = (
        jnp.einsum("hij,jhd->ihd", slopes, all_keys, preferred_element_type=jnp.float32)
        * score_scale
    ).astype(jnp.bfloat16)
    key_part = (
        jnp.einsum("hij,ihd->jhd", slopes, query_heads, preferred_element_type=jnp.float32)
        * score_scale
    )
    value_part = jnp.einsum("hij,ihd->jhd", rounded, grad_heads, preferred_element_type=jnp.float32)
    terms = jnp.concatenate(
        [
            key_part.reshape(-1, H * DK),
            value_part.reshape(-1, H * DV),
        ],
        axis=1,
    ).astype(jnp.bfloat16)
    term_blocks = [
        terms[m * local_tokens : (m + 1) * local_tokens] for m in range(lax.axis_size("seq"))
    ]
    summed = ring_scatter_back(term_blocks, ring)
    grad_keys = summed[:, : H * DK].astype(jnp.bfloat16)
    grad_values = summed[:, H * DK :].astype(jnp.bfloat16)
    return (
        decoded[None],
        grad_queries.reshape(local_tokens, H * DK)[None],
        grad_keys[None],
        grad_values[None],
        grad_trunk[None],
        grad_skip[None],
        grad_weight,
    )


def solution(mesh):
    return jax.shard_map(
        functools.partial(body, ring_order(mesh)),
        mesh=mesh,
        in_specs=(
            P(("group", "dp"), "seq", None),
            P(("group", "dp"), "seq", None),
            P(("group", "dp"), "seq", None),
            P(("group", "dp"), "seq", None),
            P(("group", "dp"), "seq", None),
            P(),
            P(),
            P(("group", "dp"), "seq", None),
        ),
        out_specs=(
            P(("group", "dp"), "seq", None),
            P(("group", "dp"), "seq", None),
            P(("group", "dp"), "seq", None),
            P(("group", "dp"), "seq", None),
            P(("group", "dp"), "seq", None),
            P(("group", "dp"), "seq", None),
            P(("group", "seq", "dp"), None),
        ),
        check_vma=False,
    )
```
